32 devices in a mesh: groups: 2 (over y), frame: 4 (over x, core), row: 4 (over z).
Axes of the slice: x: 2, y: 2, z: 4, core: 2. Of those that a mesh axis runs over, the one named last changes fastest.
Arguments:
- query_in: bfloat16 [8, 4, 64, 2240], P(('groups', 'frame'), 'row'), parts along dimension 0, may hold values from -6 to 6
- key_in: bfloat16 [8, 4, 64, 2240], P(('groups', 'frame'), 'row'), parts along dimension 0, may hold values from -216 to 216
- value_in: bfloat16 [8, 4, 64, 2240], P(('groups', 'frame'), 'row'), parts along dimension 0, may hold values from -6 to 6
- stream_in: bfloat16 [8, 4, 64, 2240], P(('groups', 'frame'), 'row'), parts along dimension 0, may hold values from -6 to 6
- attn_gain: bfloat16 [2240], replicated, may hold values from 0.5 to 1.5
- ffn_gain: bfloat16 [2240], replicated, may hold values from 0.5 to 1.5
- in_weight: bfloat16 [2240, 2, 3360], P('row', None, 'frame'), may hold values from -0.125 to 0.125
- conv_weight: bfloat16 [9, 2, 3360], P(None, None, 'frame'), may hold values from -3.5 to 3.5
- out_weight: bfloat16 [3360, 2240], P('frame'), may hold values from -0.109375 to 0.109375
Outputs:
- stream_out: bfloat16 [8, 4, 64, 2240], P(('groups', 'frame'), 'row'), parts along dimension 0
- block_out: bfloat16 [8, 4, 64, 2240], P(('groups', 'frame'), 'row'), parts along dimension 0
The draws below stay inside these ranges and needn't reach their ends.
There are 2 independent parts, one for each index of `groups`. The reference program is written for one: setup_inputs(seed, part) draws one part's arguments, and reference() takes and returns one part's arrays. A program takes and returns all parts, laid end to end along the dimension named above; an argument that names none is the same for every part. Nothing has to cross between parts.
All inputs are finite; a program needn't handle non-finite values.
Results may differ from the reference program's by a relative error of at most 0.01.
Values may be sent and summed in bfloat16 or wider, within the bound.
No kernel may reach another device: no remote copies, remote signals or barrier semaphores. Data moves between devices by JAX's collectives and lax.ppermute only.
A program may use at most 64 MiB of HBM per device.

```python
import jax
import jax.numpy as jnp
from jax import lax

D = 2240
HEADS = 20
HEAD_DIM = 112
GATED = 3360
COLS = 64
HEIGHT = 4
FRAMES = 4
N_FRAME = 4


def draw_key_in(key, part):
    base_key = jax.random.fold_in(key, 11)
    row_key = jax.random.fold_in(key, 12)
    col_key = jax.random.fold_in(key, 13)
    grid_shape = (FRAMES, HEIGHT, COLS, D)
    base_draw = jnp.clip(jax.random.normal(base_key, grid_shape, jnp.float32), -4.0, 4.0)
    row_scale = jnp.exp(jax.random.uniform(row_key, (FRAMES, HEIGHT, COLS, 1), jnp.float32, -1.2, 1.2))
    col_scale = jnp.exp(jax.random.uniform(col_key, (D,), jnp.float32, -1.2, 1.2))
    position = jnp.arange(FRAMES * HEIGHT, dtype=jnp.float32).reshape(FRAMES, HEIGHT, 1, 1) / max(FRAMES * HEIGHT - 1, 1)
    rising = 1.0 + 2.0 * position
    return (base_draw * row_scale * col_scale * rising).astype(jnp.bfloat16)


def levels(rng, dims, split, low, top_value):
    def one(axis_at, shards_of):
        steps = jax.random.uniform(jax.random.fold_in(jax.random.fold_in(rng, 6), axis_at), (shards_of,), jnp.float32, low / len(split), top_value / len(split))
        return jnp.repeat(jnp.exp(steps), dims[axis_at] // shards_of).reshape((-1,) + (1,) * (len(dims) - axis_at - 1))

    factor_of = one(*split[0])
    for cut in split[1:]:
        factor_of = factor_of * one(*cut)
    return factor_of


def centred(own_key, extent, width, most, split=(), kind=jnp.bfloat16):
    entries = width * jax.random.normal(own_key, extent, jnp.float32)
    if split:
        entries = entries * levels(own_key, extent, split, -0.22, 0.18)
    return jnp.clip(entries, -most, most).astype(kind)


def setup_inputs(seed: int = 0, part: int = 0) -> dict:
    arg_keys = jax.random.split(jax.random.key(seed), 10)
    part_splits = jax.random.split(jax.random.fold_in(arg_keys[9], part), 10)
    query_in = centred(part_splits[0], (FRAMES, HEIGHT, COLS, D), 1.0, 6.0, ((0, 4), (1, 4)))
    key_in = draw_key_in(jax.random.fold_in(jax.random.fold_in(arg_keys[9], part), 71), part)
    value_in = centred(part_splits[2], (FRAMES, HEIGHT, COLS, D), 1.0, 6.0, ((0, 4), (1, 4)))
    stream_in = centred(part_splits[3], (FRAMES, HEIGHT, COLS, D), 1.0, 6.0, ((0, 4), (1, 4)))
    attn_gain = jnp.clip(1.0 + 0.1 * jax.random.normal(arg_keys[4], (D,), jnp.float32), 0.5, 1.5).astype(jnp.bfloat16)
    ffn_gain = jnp.clip(1.0 + 0.1 * jax.random.normal(arg_keys[5], (D,), jnp.float32), 0.5, 1.5).astype(jnp.bfloat16)
    in_weight = centred(arg_keys[6], (D, 2, GATED), D ** -0.5, 0.125, ((0, 4), (2, 4)))
    conv_weight = centred(arg_keys[7], (9, 2, GATED), 3 ** -0.5, 3.5, ((2, 4),))
    out_weight = centred(arg_keys[8], (GATED, D), GATED ** -0.5, 0.109375, ((0, 4),))
    return {"query_in": query_in, "key_in": key_in, "value_in": value_in, "stream_in": stream_in, "attn_gain": attn_gain, "ffn_gain": ffn_gain, "in_weight": in_weight, "conv_weight": conv_weight, "out_weight": out_weight}


NORM_EPS = 1e-06
SHARE_EPS = 1e-06

def rms_norm(features):
    return features * lax.rsqrt(lax.optimization_barrier(jnp.mean(features * features, axis=-1, keepdims=True)) + NORM_EPS)

def reference(query_in, key_in, value_in, stream_in, attn_gain, ffn_gain, in_weight, conv_weight, out_weight):
    token_count = FRAMES * HEIGHT * COLS
    highest = lax.Precision.HIGHEST
    key_pos = jnp.maximum(key_in, 0).reshape(token_count, HEADS, HEAD_DIM).astype(jnp.float32)
    value_heads = value_in.reshape(token_count, HEADS, HEAD_DIM).astype(jnp.float32)
    kv_state = jnp.einsum('thi,thj->ihj', key_pos, value_heads, precision=highest)
    key_total = lax.optimization_barrier(jnp.sum(key_pos, axis=0))
    query_pos = jnp.maximum(query_in, 0).reshape(token_count, HEADS, HEAD_DIM).astype(jnp.float32)
    numerator = jnp.einsum('thi,ihj->thj', query_pos, kv_state, precision=highest)
    denominator = jnp.einsum('thi,hi->th', query_pos, key_total, precision=highest)
    attended = (numerator / (denominator[:, :, None] + SHARE_EPS)).reshape(token_count, D)
    stream_flat = stream_in.reshape(token_count, D).astype(jnp.float32)
    stream_out = (stream_flat + attn_gain.astype(jnp.float32) * rms_norm(attended)).astype(jnp.bfloat16)
    normed = (rms_norm(stream_out.astype(jnp.float32)) * ffn_gain.astype(jnp.float32)).astype(jnp.bfloat16)
    in_flat = in_weight.reshape(D, 2 * GATED)
    conv_taps = conv_weight.reshape(9, 2 * GATED).astype(jnp.float32)

    def frame_hidden(frame_normed):
        projected = jnp.dot(frame_normed.reshape(HEIGHT * COLS, D), in_flat, preferred_element_type=jnp.float32)
        expanded = jax.nn.silu(projected).astype(jnp.bfloat16).reshape(HEIGHT, COLS, 2 * GATED)
        padded = jnp.pad(expanded, ((1, 1), (1, 1), (0, 0)))
        summed = jnp.zeros((HEIGHT, COLS, 2 * GATED), jnp.float32)
        for row_off in range(3):
            for col_off in range(3):
                window = padded[row_off:row_off + HEIGHT, col_off:col_off + COLS, :].astype(jnp.float32)
                summed = summed + window * conv_taps[row_off * 3 + col_off]
        return (summed[..., :GATED] * jax.nn.silu(summed[..., GATED:])).astype(jnp.bfloat16)
    hidden = lax.map(frame_hidden, normed.reshape(FRAMES, HEIGHT, COLS, D))
    group_width = GATED // N_FRAME
    hidden_groups = jnp.transpose(hidden.reshape(token_count, N_FRAME, group_width), (1, 0, 2))
    weight_groups = out_weight.reshape(N_FRAME, group_width, D)

    def add_group(running, group_pair):
        hidden_part, weight_part = group_pair
        partial_sum = jnp.dot(hidden_part, weight_part, preferred_element_type=jnp.float32)
        rounded = lax.optimization_barrier(partial_sum.astype(jnp.bfloat16)).astype(jnp.float32)
        return (running + rounded, None)
    ffn_sum, unused = lax.scan(add_group, jnp.zeros((token_count, D), jnp.float32), (hidden_groups, weight_groups))
    block_out = (stream_out.astype(jnp.float32) + ffn_sum).astype(jnp.bfloat16)
    grid_shape = (FRAMES, HEIGHT, COLS, D)
    return (stream_out.reshape(grid_shape), block_out.reshape(grid_shape))
```

```python
import jax
import jax.numpy as jnp
from jax import lax
from jax.sharding import PartitionSpec as P

HEADS = 20
HEAD_DIM = 112


NORM_EPS = 1e-06
SHARE_EPS = 1e-06


def padded_2(cells, sides, width):
    for axis, dim in sides:
        count = lax.axis_size(axis)
        ends = count - 1
        head = lax.slice_in_dim(cells, 0, width, axis=dim)
        tail = lax.slice_in_dim(cells, cells.shape[dim] - width, cells.shape[dim], axis=dim)
        cells = jnp.concatenate(
            [
                lax.ppermute(tail, axis, [(i, (i + 1) % count) for i in range(ends)]),
                cells,
                lax.ppermute(head, axis, [((i + 1) % count, i) for i in range(ends)]),
            ],
            axis=dim,
        )
    return cells


def rms_norm(features):
    return features * lax.rsqrt(jnp.mean(features * features, axis=-1, keepdims=True) + NORM_EPS)


def depthwise(padded, conv_taps, row_count, col_count, half_width):
    widened = jnp.pad(padded, ((0, 0), (0, 0), (1, 1), (0, 0)))
    summed = jnp.zeros((padded.shape[0], row_count, col_count, padded.shape[3]), jnp.float32)
    for row_off in range(3):
        for col_off in range(3):
            window = widened[
                :, row_off : row_off + row_count, col_off : col_off + col_count, :
            ].astype(jnp.float32)
            summed = summed + window * conv_taps[row_off * 3 + col_off]
    return (summed[..., :half_width] * jax.nn.silu(summed[..., half_width:])).astype(jnp.bfloat16)


def local(
    query_in, key_in, value_in, stream_in, attn_gain, ffn_gain, in_weight, conv_weight, out_weight
):
    frame_count, row_count, col_count, model_width = query_in.shape
    token_count = frame_count * row_count * col_count
    local_gated = in_weight.shape[2]
    highest = lax.Precision.HIGHEST
    key_pos = jnp.maximum(key_in, 0).reshape(token_count, HEADS, HEAD_DIM)
    value_heads = value_in.reshape(token_count, HEADS, HEAD_DIM)
    local_state = jnp.einsum(
        "thi,thj->ihj", key_pos, value_heads, preferred_element_type=jnp.float32
    ).reshape(HEAD_DIM, model_width)
    local_total = jnp.sum(key_pos.reshape(token_count, model_width), axis=0, dtype=jnp.float32)
    stats = jnp.concatenate([local_state, local_total[None, :]], axis=0)
    stats = lax.psum_scatter(stats, "frame", scatter_dimension=1, tiled=True)
    stats = lax.psum(stats, "row")
    stats = lax.all_gather(stats, "frame", axis=1, tiled=True)
    kv_state, key_total = stats[:HEAD_DIM], stats[HEAD_DIM]
    query_pos = jnp.maximum(query_in, 0).reshape(token_count, HEADS, HEAD_DIM).astype(jnp.float32)
    numerator = jnp.einsum(
        "thi,ihj->thj", query_pos, kv_state.reshape(HEAD_DIM, HEADS, HEAD_DIM), precision=highest
    )
    denominator = jnp.einsum(
        "thi,hi->th", query_pos, key_total.reshape(HEADS, HEAD_DIM), precision=highest
    )
    attended = (numerator / (denominator[:, :, None] + SHARE_EPS)).reshape(token_count, model_width)
    stream_flat = stream_in.reshape(token_count, model_width).astype(jnp.float32)
    stream_out = (stream_flat + attn_gain.astype(jnp.float32) * rms_norm(attended)).astype(
        jnp.bfloat16
    )
    normed = (rms_norm(stream_out.astype(jnp.float32)) * ffn_gain.astype(jnp.float32)).astype(
        jnp.bfloat16
    )
    normed_grid = normed.reshape(frame_count, row_count, col_count, model_width)
    conv_taps = conv_weight.reshape(9, 2 * local_gated).astype(jnp.float32)
    row_parts = lax.axis_size("row")
    local_depth = in_weight.shape[0]
    split = jnp.moveaxis(
        normed_grid.reshape(frame_count, row_count, col_count, row_parts, local_depth), 3, 0
    )
    swapped = lax.all_to_all(split, "row", split_axis=0, concat_axis=0, tiled=True)
    tokens = lax.all_gather(swapped, "frame", axis=1, tiled=True)
    piece_frames = tokens.shape[1]
    partial = jnp.dot(
        tokens.reshape(-1, local_depth),
        in_weight.reshape(local_depth, 2 * local_gated),
        preferred_element_type=jnp.float32,
    ).astype(jnp.bfloat16)
    summed = lax.psum_scatter(partial, "row", scatter_dimension=0, tiled=True).reshape(
        piece_frames, row_count, col_count, 2 * local_gated
    )
    expanded = jax.nn.silu(summed.astype(jnp.float32)).astype(jnp.bfloat16)
    padded_expanded = padded_2(expanded, (("row", 1),), 1)
    hidden = depthwise(padded_expanded, conv_taps, row_count, col_count, local_gated)
    hidden_flat = hidden.reshape(-1, local_gated)
    ffn_rows = lax.psum_scatter(
        jnp.dot(hidden_flat, out_weight, preferred_element_type=jnp.float32).astype(jnp.bfloat16),
        "frame",
        scatter_dimension=0,
        tiled=True,
    ).astype(jnp.float32)
    block_out = (stream_out.astype(jnp.float32) + ffn_rows).astype(jnp.bfloat16)
    grid_shape = (frame_count, row_count, col_count, model_width)
    return (stream_out.reshape(grid_shape), block_out.reshape(grid_shape))


def solution(mesh):
    in_specs = (
        P(("groups", "frame"), "row", None, None),
        P(("groups", "frame"), "row", None, None),
        P(("groups", "frame"), "row", None, None),
        P(("groups", "frame"), "row", None, None),
        P(),
        P(),
        P("row", None, "frame"),
        P(None, None, "frame"),
        P("frame", None),
    )
    out_specs = (
        P(("groups", "frame"), "row", None, None),
        P(("groups", "frame"), "row", None, None),
    )
    return jax.shard_map(local, mesh=mesh, in_specs=in_specs, out_specs=out_specs, check_vma=False)
```

```python
import jax
import jax.numpy as jnp
from jax import lax
from jax.sharding import PartitionSpec as P

HEADS = 20
HEAD_DIM = 112


NORM_EPS = 1e-06
SHARE_EPS = 1e-06


def padded_2(cells, sides, width):
    for axis, dim in sides:
        count = lax.axis_size(axis)
        ends = count - 1
        head = lax.slice_in_dim(cells, 0, width, axis=dim)
        tail = lax.slice_in_dim(cells, cells.shape[dim] - width, cells.shape[dim], axis=dim)
        cells = jnp.concatenate(
            [
                lax.ppermute(tail, axis, [(i, (i + 1) % count) for i in range(ends)]),
                cells,
                lax.ppermute(head, axis, [((i + 1) % count, i) for i in range(ends)]),
            ],
            axis=dim,
        )
    return cells


def exchange_steps(axes):
    steps = []
    for axis in axes:
        count = lax.axis_size(axis)
        bit = 1
        while bit < count:
            steps.append((axis, count, bit))
            bit *= 2
    return steps


def halving_sum(block, axes):
    steps = exchange_steps(axes)
    for axis, count, bit in steps:
        upper = (lax.axis_index(axis) & bit) != 0
        half = block.shape[1] // 2
        low, high = block[:, :half], block[:, half:]
        sent = jnp.where(upper, low, high)
        kept = jnp.where(upper, high, low)
        block = kept + lax.ppermute(sent, axis, [(i, i ^ bit) for i in range(count)])
    for axis, count, bit in reversed(steps):
        upper = (lax.axis_index(axis) & bit) != 0
        other = lax.ppermute(block, axis, [(i, i ^ bit) for i in range(count)])
        block = jnp.where(
            upper, jnp.concatenate([other, block], 1), jnp.concatenate([block, other], 1)
        )
    return block


def rms_norm(features):
    return features * lax.rsqrt(jnp.mean(features * features, axis=-1, keepdims=True) + NORM_EPS)


def depthwise(padded, conv_taps, row_count, col_count, half_width):
    widened = jnp.pad(padded, ((0, 0), (0, 0), (1, 1), (0, 0)))
    summed = jnp.zeros((padded.shape[0], row_count, col_count, padded.shape[3]), jnp.float32)
    for row_off in range(3):
        for col_off in range(3):
            window = widened[
                :, row_off : row_off + row_count, col_off : col_off + col_count, :
            ].astype(jnp.float32)
            summed = summed + window * conv_taps[row_off * 3 + col_off]
    return (summed[..., :half_width] * jax.nn.silu(summed[..., half_width:])).astype(jnp.bfloat16)


def local(
    query_in, key_in, value_in, stream_in, attn_gain, ffn_gain, in_weight, conv_weight, out_weight
):
    frame_count, row_count, col_count, model_width = query_in.shape
    token_count = frame_count * row_count * col_count
    local_gated = in_weight.shape[2]
    highest = lax.Precision.HIGHEST
    key_pos = jnp.maximum(key_in, 0).reshape(token_count, HEADS, HEAD_DIM)
    value_heads = value_in.reshape(token_count, HEADS, HEAD_DIM)
    local_state = jnp.einsum(
        "thi,thj->ihj", key_pos, value_heads, preferred_element_type=jnp.float32
    ).reshape(HEAD_DIM, model_width)
    local_total = jnp.sum(key_pos.reshape(token_count, model_width), axis=0, dtype=jnp.float32)
    stats = jnp.concatenate([local_state, local_total[None, :]], axis=0)
    parts = 1
    for axis, count, bit in exchange_steps(("frame", "row")):
        parts *= 2
    padded_width = -(-model_width // parts) * parts
    stats = jnp.pad(stats, ((0, 0), (0, padded_width - model_width)))
    stats = halving_sum(stats, ("frame", "row"))[:, :model_width]
    kv_state, key_total = stats[:HEAD_DIM], stats[HEAD_DIM]
    query_pos = jnp.maximum(query_in, 0).reshape(token_count, HEADS, HEAD_DIM).astype(jnp.float32)
    numerator = jnp.einsum(
        "thi,ihj->thj", query_pos, kv_state.reshape(HEAD_DIM, HEADS, HEAD_DIM), precision=highest
    )
    denominator = jnp.einsum(
        "thi,hi->th", query_pos, key_total.reshape(HEADS, HEAD_DIM), precision=highest
    )
    attended = (numerator / (denominator[:, :, None] + SHARE_EPS)).reshape(token_count, model_width)
    stream_flat = stream_in.reshape(token_count, model_width).astype(jnp.float32)
    stream_out = (stream_flat + attn_gain.astype(jnp.float32) * rms_norm(attended)).astype(
        jnp.bfloat16
    )
    normed = (rms_norm(stream_out.astype(jnp.float32)) * ffn_gain.astype(jnp.float32)).astype(
        jnp.bfloat16
    )
    normed_grid = normed.reshape(frame_count, row_count, col_count, model_width)
    conv_taps = conv_weight.reshape(9, 2 * local_gated).astype(jnp.float32)
    row_parts = lax.axis_size("row")
    local_depth = in_weight.shape[0]
    split = jnp.moveaxis(
        normed_grid.reshape(frame_count, row_count, col_count, row_parts, local_depth), 3, 0
    )
    swapped = lax.all_to_all(split, "row", split_axis=0, concat_axis=0, tiled=True)
    tokens = lax.all_gather(swapped, "frame", axis=1, tiled=True)
    piece_frames = tokens.shape[1]
    partial = jnp.dot(
        tokens.reshape(-1, local_depth),
        in_weight.reshape(local_depth, 2 * local_gated),
        preferred_element_type=jnp.float32,
    ).astype(jnp.bfloat16)
    summed = lax.psum_scatter(partial, "row", scatter_dimension=0, tiled=True).reshape(
        piece_frames, row_count, col_count, 2 * local_gated
    )
    expanded = jax.nn.silu(summed.astype(jnp.float32)).astype(jnp.bfloat16)
    padded_expanded = padded_2(expanded, (("row", 1),), 1)
    hidden = depthwise(padded_expanded, conv_taps, row_count, col_count, local_gated)
    hidden_flat = hidden.reshape(-1, local_gated)
    ffn_rows = lax.psum_scatter(
        jnp.dot(hidden_flat, out_weight, preferred_element_type=jnp.float32).astype(jnp.bfloat16),
        "frame",
        scatter_dimension=0,
        tiled=True,
    ).astype(jnp.float32)
    block_out = (stream_out.astype(jnp.float32) + ffn_rows).astype(jnp.bfloat16)
    grid_shape = (frame_count, row_count, col_count, model_width)
    return (stream_out.reshape(grid_shape), block_out.reshape(grid_shape))


def solution(mesh):
    in_specs = (
        P(("groups", "frame"), "row", None, None),
        P(("groups", "frame"), "row", None, None),
        P(("groups", "frame"), "row", None, None),
        P(("groups", "frame"), "row", None, None),
        P(),
        P(),
        P("row", None, "frame"),
        P(None, None, "frame"),
        P("frame", None),
    )
    out_specs = (
        P(("groups", "frame"), "row", None, None),
        P(("groups", "frame"), "row", None, None),
    )
    return jax.shard_map(local, mesh=mesh, in_specs=in_specs, out_specs=out_specs, check_vma=False)
```

```python
import jax
import jax.numpy as jnp
from jax import lax
from jax.sharding import PartitionSpec as P

HEADS = 20
HEAD_DIM = 112


NORM_EPS = 1e-06
SHARE_EPS = 1e-06


def padded_2(cells, sides, width):
    for axis, dim in sides:
        count = lax.axis_size(axis)
        ends = count - 1
        head = lax.slice_in_dim(cells, 0, width, axis=dim)
        tail = lax.slice_in_dim(cells, cells.shape[dim] - width, cells.shape[dim], axis=dim)
        cells = jnp.concatenate(
            [
                lax.ppermute(tail, axis, [(i, (i + 1) % count) for i in range(ends)]),
                cells,
                lax.ppermute(head, axis, [((i + 1) % count, i) for i in range(ends)]),
            ],
            axis=dim,
        )
    return cells


def exchange_steps(axes):
    steps = []
    for axis in axes:
        count = lax.axis_size(axis)
        bit = 1
        while bit < count:
            steps.append((axis, count, bit))
            bit *= 2
    return steps


def halving_sum(block, axes):
    steps = exchange_steps(axes)
    for axis, count, bit in steps:
        upper = (lax.axis_index(axis) & bit) != 0
        half = block.shape[1] // 2
        low, high = block[:, :half], block[:, half:]
        sent = jnp.where(upper, low, high)
        kept = jnp.where(upper, high, low)
        block = kept + lax.ppermute(sent, axis, [(i, i ^ bit) for i in range(count)])
    for axis, count, bit in reversed(steps):
        upper = (lax.axis_index(axis) & bit) != 0
        other = lax.ppermute(block, axis, [(i, i ^ bit) for i in range(count)])
        block = jnp.where(
            upper, jnp.concatenate([other, block], 1), jnp.concatenate([block, other], 1)
        )
    return block


def pick(blocks, index):
    stacked = jnp.stack(blocks)
    return lax.dynamic_index_in_dim(stacked, index, axis=0, keepdims=False)


def swap_chunks(chunks, axis):
    count = lax.axis_size(axis)
    own = lax.axis_index(axis)
    by_mask = [pick(chunks, own)]
    for mask in range(1, count):
        sent = pick(chunks, own ^ mask)
        by_mask.append(lax.ppermute(sent, axis, [(i, i ^ mask) for i in range(count)]))
    return [pick(by_mask, own ^ source) for source in range(count)]


def rms_norm(features):
    return features * lax.rsqrt(jnp.mean(features * features, axis=-1, keepdims=True) + NORM_EPS)


def depthwise(padded, conv_taps, row_count, col_count, half_width):
    widened = jnp.pad(padded, ((0, 0), (0, 0), (1, 1), (0, 0)))
    summed = jnp.zeros((padded.shape[0], row_count, col_count, padded.shape[3]), jnp.float32)
    for row_off in range(3):
        for col_off in range(3):
            window = widened[
                :, row_off : row_off + row_count, col_off : col_off + col_count, :
            ].astype(jnp.float32)
            summed = summed + window * conv_taps[row_off * 3 + col_off]
    return (summed[..., :half_width] * jax.nn.silu(summed[..., half_width:])).astype(jnp.bfloat16)


def local(
    query_in, key_in, value_in, stream_in, attn_gain, ffn_gain, in_weight, conv_weight, out_weight
):
    frame_count, row_count, col_count, model_width = query_in.shape
    token_count = frame_count * row_count * col_count
    local_gated = in_weight.shape[2]
    highest = lax.Precision.HIGHEST
    key_pos = jnp.maximum(key_in, 0).reshape(token_count, HEADS, HEAD_DIM)
    value_heads = value_in.reshape(token_count, HEADS, HEAD_DIM)
    local_state = jnp.einsum(
        "thi,thj->ihj", key_pos, value_heads, preferred_element_type=jnp.float32
    ).reshape(HEAD_DIM, model_width)
    local_total = jnp.sum(key_pos.reshape(token_count, model_width), axis=0, dtype=jnp.float32)
    stats = jnp.concatenate([local_state, local_total[None, :]], axis=0)
    parts = 1
    for axis, count, bit in exchange_steps(("frame", "row")):
        parts *= 2
    padded_width = -(-model_width // parts) * parts
    stats = jnp.pad(stats, ((0, 0), (0, padded_width - model_width)))
    stats = halving_sum(stats, ("frame", "row"))[:, :model_width]
    kv_state, key_total = stats[:HEAD_DIM], stats[HEAD_DIM]
    query_pos = jnp.maximum(query_in, 0).reshape(token_count, HEADS, HEAD_DIM).astype(jnp.float32)
    numerator = jnp.einsum(
        "thi,ihj->thj", query_pos, kv_state.reshape(HEAD_DIM, HEADS, HEAD_DIM), precision=highest
    )
    denominator = jnp.einsum(
        "thi,hi->th", query_pos, key_total.reshape(HEADS, HEAD_DIM), precision=highest
    )
    attended = (numerator / (denominator[:, :, None] + SHARE_EPS)).reshape(token_count, model_width)
    stream_flat = stream_in.reshape(token_count, model_width).astype(jnp.float32)
    stream_out = (stream_flat + attn_gain.astype(jnp.float32) * rms_norm(attended)).astype(
        jnp.bfloat16
    )
    normed = (rms_norm(stream_out.astype(jnp.float32)) * ffn_gain.astype(jnp.float32)).astype(
        jnp.bfloat16
    )
    normed_grid = normed.reshape(frame_count, row_count, col_count, model_width)
    conv_taps = conv_weight.reshape(9, 2 * local_gated).astype(jnp.float32)
    row_parts = lax.axis_size("row")
    local_depth = in_weight.shape[0]
    depth_chunks = [
        normed_grid[..., part * local_depth : (part + 1) * local_depth] for part in range(row_parts)
    ]
    by_row = jnp.concatenate(swap_chunks(depth_chunks, "row"), axis=1)
    frame_parts = lax.axis_size("frame")
    by_frame = swap_chunks([by_row] * frame_parts, "frame")
    tokens = jnp.stack([piece.transpose(1, 0, 2, 3) for piece in by_frame], axis=1)
    piece_frames = tokens.shape[1] * tokens.shape[2]
    partial = jnp.dot(
        tokens.reshape(-1, local_depth),
        in_weight.reshape(local_depth, 2 * local_gated),
        preferred_element_type=jnp.float32,
    ).astype(jnp.bfloat16)
    summed = lax.psum_scatter(partial, "row", scatter_dimension=0, tiled=True).reshape(
        piece_frames, row_count, col_count, 2 * local_gated
    )
    expanded = jax.nn.silu(summed.astype(jnp.float32)).astype(jnp.bfloat16)
    padded_expanded = padded_2(expanded, (("row", 1),), 1)
    hidden = depthwise(padded_expanded, conv_taps, row_count, col_count, local_gated)
    hidden_flat = hidden.reshape(-1, local_gated)
    projected = jnp.dot(hidden_flat, out_weight, preferred_element_type=jnp.float32).astype(
        jnp.bfloat16
    )
    frame_blocks = jnp.split(projected, frame_parts, axis=0)
    ffn_rows = sum(
        piece.astype(jnp.float32) for piece in swap_chunks(frame_blocks, "frame")
    ).reshape(token_count, model_width)
    block_out = (stream_out.astype(jnp.float32) + ffn_rows).astype(jnp.bfloat16)
    grid_shape = (frame_count, row_count, col_count, model_width)
    return (stream_out.reshape(grid_shape), block_out.reshape(grid_shape))


def solution(mesh):
    in_specs = (
        P(("groups", "frame"), "row", None, None),
        P(("groups", "frame"), "row", None, None),
        P(("groups", "frame"), "row", None, None),
        P(("groups", "frame"), "row", None, None),
        P(),
        P(),
        P("row", None, "frame"),
        P(None, None, "frame"),
        P("frame", None),
    )
    out_specs = (
        P(("groups", "frame"), "row", None, None),
        P(("groups", "frame"), "row", None, None),
    )
    return jax.shard_map(local, mesh=mesh, in_specs=in_specs, out_specs=out_specs, check_vma=False)
```

```python
import jax
import jax.numpy as jnp
from jax import lax
from jax.sharding import PartitionSpec as P

HEADS = 20
HEAD_DIM = 112


NORM_EPS = 1e-06
SHARE_EPS = 1e-06


def padded_2(cells, sides, width):
    for axis, dim in sides:
        count = lax.axis_size(axis)
        ends = count - 1
        head = lax.slice_in_dim(cells, 0, width, axis=dim)
        tail = lax.slice_in_dim(cells, cells.shape[dim] - width, cells.shape[dim], axis=dim)
        cells = jnp.concatenate(
            [
                lax.ppermute(tail, axis, [(i, (i + 1) % count) for i in range(ends)]),
                cells,
                lax.ppermute(head, axis, [((i + 1) % count, i) for i in range(ends)]),
            ],
            axis=dim,
        )
    return cells


def exchange_steps(axes):
    steps = []
    for axis in axes:
        count = lax.axis_size(axis)
        bit = 1
        while bit < count:
            steps.append((axis, count, bit))
            bit *= 2
    return steps


def halving_sum(block, axes):
    steps = exchange_steps(axes)
    for axis, count, bit in steps:
        upper = (lax.axis_index(axis) & bit) != 0
        half = block.shape[1] // 2
        low, high = block[:, :half], block[:, half:]
        sent = jnp.where(upper, low, high)
        kept = jnp.where(upper, high, low)
        block = kept + lax.ppermute(sent, axis, [(i, i ^ bit) for i in range(count)])
    for axis, count, bit in reversed(steps):
        upper = (lax.axis_index(axis) & bit) != 0
        other = lax.ppermute(block, axis, [(i, i ^ bit) for i in range(count)])
        block = jnp.where(
            upper, jnp.concatenate([other, block], 1), jnp.concatenate([block, other], 1)
        )
    return block


def pick(blocks, index):
    stacked = jnp.stack(blocks)
    return lax.dynamic_index_in_dim(stacked, index, axis=0, keepdims=False)


def swap_chunks(chunks, axis):
    count = lax.axis_size(axis)
    own = lax.axis_index(axis)
    by_mask = [pick(chunks, own)]
    for mask in range(1, count):
        sent = pick(chunks, own ^ mask)
        by_mask.append(lax.ppermute(sent, axis, [(i, i ^ mask) for i in range(count)]))
    return [pick(by_mask, own ^ source) for source in range(count)]


def rms_norm(features):
    return features * lax.rsqrt(jnp.mean(features * features, axis=-1, keepdims=True) + NORM_EPS)


def depthwise(padded, conv_taps, row_count, col_count, half_width):
    widened = jnp.pad(padded, ((0, 0), (0, 0), (1, 1), (0, 0)))
    summed = jnp.zeros((padded.shape[0], row_count, col_count, padded.shape[3]), jnp.float32)
    for row_off in range(3):
        for col_off in range(3):
            window = widened[
                :, row_off : row_off + row_count, col_off : col_off + col_count, :
            ].astype(jnp.float32)
            summed = summed + window * conv_taps[row_off * 3 + col_off]
    return (summed[..., :half_width] * jax.nn.silu(summed[..., half_width:])).astype(jnp.bfloat16)


def local(
    query_in, key_in, value_in, stream_in, attn_gain, ffn_gain, in_weight, conv_weight, out_weight
):
    frame_count, row_count, col_count, model_width = query_in.shape
    token_count = frame_count * row_count * col_count
    local_gated = in_weight.shape[2]
    highest = lax.Precision.HIGHEST
    key_pos = jnp.maximum(key_in, 0).reshape(token_count, HEADS, HEAD_DIM)
    value_heads = value_in.reshape(token_count, HEADS, HEAD_DIM)
    local_state = jnp.einsum(
        "thi,thj->ihj", key_pos, value_heads, preferred_element_type=jnp.float32
    ).reshape(HEAD_DIM, model_width)
    local_total = jnp.sum(key_pos.reshape(token_count, model_width), axis=0, dtype=jnp.float32)
    stats = jnp.concatenate([local_state, local_total[None, :]], axis=0)
    parts = 1
    for axis, count, bit in exchange_steps(("frame", "row")):
        parts *= 2
    padded_width = -(-model_width // parts) * parts
    stats = jnp.pad(stats, ((0, 0), (0, padded_width - model_width)))
    stats = halving_sum(stats, ("frame", "row"))[:, :model_width]
    kv_state, key_total = stats[:HEAD_DIM], stats[HEAD_DIM]
    query_pos = jnp.maximum(query_in, 0).reshape(token_count, HEADS, HEAD_DIM).astype(jnp.float32)
    numerator = jnp.einsum(
        "thi,ihj->thj", query_pos, kv_state.reshape(HEAD_DIM, HEADS, HEAD_DIM), precision=highest
    )
    denominator = jnp.einsum(
        "thi,hi->th", query_pos, key_total.reshape(HEADS, HEAD_DIM), precision=highest
    )
    attended = (numerator / (denominator[:, :, None] + SHARE_EPS)).reshape(token_count, model_width)
    stream_flat = stream_in.reshape(token_count, model_width).astype(jnp.float32)
    stream_out = (stream_flat + attn_gain.astype(jnp.float32) * rms_norm(attended)).astype(
        jnp.bfloat16
    )
    normed = (rms_norm(stream_out.astype(jnp.float32)) * ffn_gain.astype(jnp.float32)).astype(
        jnp.bfloat16
    )
    normed_grid = normed.reshape(frame_count, row_count, col_count, model_width)
    conv_taps = conv_weight.reshape(9, 2 * local_gated).astype(jnp.float32)
    row_parts = lax.axis_size("row")
    local_depth = in_weight.shape[0]
    depth_chunks = [
        normed_grid[..., part * local_depth : (part + 1) * local_depth] for part in range(row_parts)
    ]
    by_row = jnp.concatenate(swap_chunks(depth_chunks, "row"), axis=1)
    frame_parts = lax.axis_size("frame")
    by_frame = swap_chunks([by_row] * frame_parts, "frame")
    tokens = jnp.stack([piece.transpose(1, 0, 2, 3) for piece in by_frame], axis=1)
    piece_frames = tokens.shape[1] * tokens.shape[2]
    weight_flat = in_weight.reshape(local_depth, 2 * local_gated)
    halves = 2 if piece_frames % 2 == 0 else 1
    half_frames = piece_frames // halves
    chunks = [tokens[:, half * half_frames : (half + 1) * half_frames] for half in range(halves)]
    sums = []
    for half in range(halves):
        chunk = chunks[half]
        if sums:
            sums[-1], chunk = lax.optimization_barrier((sums[-1], chunk))
        partial = jnp.dot(
            chunk.reshape(-1, local_depth), weight_flat, preferred_element_type=jnp.float32
        ).astype(jnp.bfloat16)
        sums.append(lax.psum_scatter(partial, "row", scatter_dimension=0, tiled=True))
    projected_parts = []
    for summed in sums:
        expanded = (
            jax.nn.silu(summed.astype(jnp.float32))
            .astype(jnp.bfloat16)
            .reshape(half_frames, row_count, col_count, 2 * local_gated)
        )
        padded_expanded = padded_2(expanded, (("row", 1),), 1)
        hidden = depthwise(padded_expanded, conv_taps, row_count, col_count, local_gated)
        projected_parts.append(
            jnp.dot(
                hidden.reshape(-1, local_gated), out_weight, preferred_element_type=jnp.float32
            ).astype(jnp.bfloat16)
        )
    projected = jnp.concatenate(projected_parts, axis=0)
    frame_blocks = jnp.split(projected, frame_parts, axis=0)
    ffn_rows = sum(
        piece.astype(jnp.float32) for piece in swap_chunks(frame_blocks, "frame")
    ).reshape(token_count, model_width)
    block_out = (stream_out.astype(jnp.float32) + ffn_rows).astype(jnp.bfloat16)
    grid_shape = (frame_count, row_count, col_count, model_width)
    return (stream_out.reshape(grid_shape), block_out.reshape(grid_shape))


def solution(mesh):
    in_specs = (
        P(("groups", "frame"), "row", None, None),
        P(("groups", "frame"), "row", None, None),
        P(("groups", "frame"), "row", None, None),
        P(("groups", "frame"), "row", None, None),
        P(),
        P(),
        P("row", None, "frame"),
        P(None, None, "frame"),
        P("frame", None),
    )
    out_specs = (
        P(("groups", "frame"), "row", None, None),
        P(("groups", "frame"), "row", None, None),
    )
    return jax.shard_map(local, mesh=mesh, in_specs=in_specs, out_specs=out_specs, check_vma=False)
```

```python
import jax
import jax.numpy as jnp
from jax import lax
from jax.sharding import PartitionSpec as P

HEADS = 20
HEAD_DIM = 112


NORM_EPS = 1e-06
SHARE_EPS = 1e-06


def padded_2(cells, sides, width):
    for axis, dim in sides:
        count = lax.axis_size(axis)
        ends = count - 1
        head = lax.slice_in_dim(cells, 0, width, axis=dim)
        tail = lax.slice_in_dim(cells, cells.shape[dim] - width, cells.shape[dim], axis=dim)
        cells = jnp.concatenate(
            [
                lax.ppermute(tail, axis, [(i, (i + 1) % count) for i in range(ends)]),
                cells,
                lax.ppermute(head, axis, [((i + 1) % count, i) for i in range(ends)]),
            ],
            axis=dim,
        )
    return cells


def exchange_steps(axes):
    steps = []
    for axis in axes:
        count = lax.axis_size(axis)
        bit = 1
        while bit < count:
            steps.append((axis, count, bit))
            bit *= 2
    return steps


def halving_sum(block, axes):
    steps = exchange_steps(axes)
    for axis, count, bit in steps:
        upper = (lax.axis_index(axis) & bit) != 0
        half = block.shape[1] // 2
        low, high = block[:, :half], block[:, half:]
        sent = jnp.where(upper, low, high)
        kept = jnp.where(upper, high, low)
        block = kept + lax.ppermute(sent, axis, [(i, i ^ bit) for i in range(count)])
    for axis, count, bit in reversed(steps):
        upper = (lax.axis_index(axis) & bit) != 0
        other = lax.ppermute(block, axis, [(i, i ^ bit) for i in range(count)])
        block = jnp.where(
            upper, jnp.concatenate([other, block], 1), jnp.concatenate([block, other], 1)
        )
    return block


def pick(blocks, index):
    stacked = jnp.stack(blocks)
    return lax.dynamic_index_in_dim(stacked, index, axis=0, keepdims=False)


def swap_chunks(chunks, axis):
    count = lax.axis_size(axis)
    own = lax.axis_index(axis)
    by_mask = [pick(chunks, own)]
    for mask in range(1, count):
        sent = pick(chunks, own ^ mask)
        by_mask.append(lax.ppermute(sent, axis, [(i, i ^ mask) for i in range(count)]))
    return [pick(by_mask, own ^ source) for source in range(count)]


def gather_depth_chunks(chunks, frame_parts):
    row_parts = len(chunks)
    frame_at = lax.axis_index("frame")
    row_at = lax.axis_index("row")
    pairs_of = lambda fm, rm: [
        (f * row_parts + r, (f ^ fm) * row_parts + (r ^ rm))
        for f in range(frame_parts)
        for r in range(row_parts)
    ]
    by_mask = []
    for frame_mask in range(frame_parts):
        for row_mask in range(row_parts):
            sent = pick(chunks, row_at ^ row_mask)
            if frame_mask == 0 and row_mask == 0:
                by_mask.append(sent)
            else:
                by_mask.append(
                    lax.ppermute(sent, ("frame", "row"), pairs_of(frame_mask, row_mask))
                )
    return [
        [
            pick(by_mask, (frame_at ^ source_frame) * row_parts + (row_at ^ source_row))
            for source_frame in range(frame_parts)
        ]
        for source_row in range(row_parts)
    ]


def rms_norm(features):
    return features * lax.rsqrt(jnp.mean(features * features, axis=-1, keepdims=True) + NORM_EPS)


def depthwise(padded, conv_taps, row_count, col_count, half_width):
    widened = jnp.pad(padded, ((0, 0), (0, 0), (1, 1), (0, 0)))
    summed = jnp.zeros((padded.shape[0], row_count, col_count, padded.shape[3]), jnp.float32)
    for row_off in range(3):
        for col_off in range(3):
            window = widened[
                :, row_off : row_off + row_count, col_off : col_off + col_count, :
            ].astype(jnp.float32)
            summed = summed + window * conv_taps[row_off * 3 + col_off]
    return (summed[..., :half_width] * jax.nn.silu(summed[..., half_width:])).astype(jnp.bfloat16)


def local(
    query_in, key_in, value_in, stream_in, attn_gain, ffn_gain, in_weight, conv_weight, out_weight
):
    frame_count, row_count, col_count, model_width = query_in.shape
    token_count = frame_count * row_count * col_count
    local_gated = in_weight.shape[2]
    highest = lax.Precision.HIGHEST
    key_pos = jnp.maximum(key_in, 0).reshape(token_count, HEADS, HEAD_DIM)
    value_heads = value_in.reshape(token_count, HEADS, HEAD_DIM)
    local_state = jnp.einsum(
        "thi,thj->ihj", key_pos, value_heads, preferred_element_type=jnp.float32
    ).reshape(HEAD_DIM, model_width)
    local_total = jnp.sum(key_pos.reshape(token_count, model_width), axis=0, dtype=jnp.float32)
    stats = jnp.concatenate([local_state, local_total[None, :]], axis=0)
    parts = 1
    for axis, count, bit in exchange_steps(("frame", "row")):
        parts *= 2
    padded_width = -(-model_width // parts) * parts
    stats = jnp.pad(stats, ((0, 0), (0, padded_width - model_width)))
    stats = halving_sum(stats, ("frame", "row"))[:, :model_width]
    kv_state, key_total = stats[:HEAD_DIM], stats[HEAD_DIM]
    query_pos = jnp.maximum(query_in, 0).reshape(token_count, HEADS, HEAD_DIM).astype(jnp.float32)
    numerator = jnp.einsum(
        "thi,ihj->thj", query_pos, kv_state.reshape(HEAD_DIM, HEADS, HEAD_DIM), precision=highest
    )
    denominator = jnp.einsum(
        "thi,hi->th", query_pos, key_total.reshape(HEADS, HEAD_DIM), precision=highest
    )
    attended = (numerator / (denominator[:, :, None] + SHARE_EPS)).reshape(token_count, model_width)
    stream_flat = stream_in.reshape(token_count, model_width).astype(jnp.float32)
    stream_out = (stream_flat + attn_gain.astype(jnp.float32) * rms_norm(attended)).astype(
        jnp.bfloat16
    )
    normed = (rms_norm(stream_out.astype(jnp.float32)) * ffn_gain.astype(jnp.float32)).astype(
        jnp.bfloat16
    )
    normed_grid = normed.reshape(frame_count, row_count, col_count, model_width)
    conv_taps = conv_weight.reshape(9, 2 * local_gated).astype(jnp.float32)
    row_parts = lax.axis_size("row")
    local_depth = in_weight.shape[0]
    depth_chunks = [
        normed_grid[..., part * local_depth : (part + 1) * local_depth] for part in range(row_parts)
    ]
    frame_parts = lax.axis_size("frame")
    if frame_parts * row_parts <= 16 and frame_count == 1 and row_count == 1:
        grid = gather_depth_chunks(depth_chunks, frame_parts)
        tokens = jnp.stack([jnp.concatenate(per_row, axis=0) for per_row in grid])
    else:
        by_row = jnp.concatenate(swap_chunks(depth_chunks, "row"), axis=1)
        by_frame = swap_chunks([by_row] * frame_parts, "frame")
        tokens = jnp.stack([piece.transpose(1, 0, 2, 3) for piece in by_frame], axis=1)
    piece_frames = tokens.shape[1] * tokens.shape[2]
    partial = jnp.dot(
        tokens.reshape(-1, local_depth),
        in_weight.reshape(local_depth, 2 * local_gated),
        preferred_element_type=jnp.float32,
    ).astype(jnp.bfloat16)
    summed = lax.psum_scatter(partial, "row", scatter_dimension=0, tiled=True).reshape(
        piece_frames, row_count, col_count, 2 * local_gated
    )
    expanded = jax.nn.silu(summed.astype(jnp.float32)).astype(jnp.bfloat16)
    padded_expanded = padded_2(expanded, (("row", 1),), 1)
    hidden = depthwise(padded_expanded, conv_taps, row_count, col_count, local_gated)
    hidden_flat = hidden.reshape(-1, local_gated)
    projected = jnp.dot(hidden_flat, out_weight, preferred_element_type=jnp.float32).astype(
        jnp.bfloat16
    )
    frame_blocks = jnp.split(projected, frame_parts, axis=0)
    ffn_rows = sum(
        piece.astype(jnp.float32) for piece in swap_chunks(frame_blocks, "frame")
    ).reshape(token_count, model_width)
    block_out = (stream_out.astype(jnp.float32) + ffn_rows).astype(jnp.bfloat16)
    grid_shape = (frame_count, row_count, col_count, model_width)
    return (stream_out.reshape(grid_shape), block_out.reshape(grid_shape))


def solution(mesh):
    in_specs = (
        P(("groups", "frame"), "row", None, None),
        P(("groups", "frame"), "row", None, None),
        P(("groups", "frame"), "row", None, None),
        P(("groups", "frame"), "row", None, None),
        P(),
        P(),
        P("row", None, "frame"),
        P(None, None, "frame"),
        P("frame", None),
    )
    out_specs = (
        P(("groups", "frame"), "row", None, None),
        P(("groups", "frame"), "row", None, None),
    )
    return jax.shard_map(local, mesh=mesh, in_specs=in_specs, out_specs=out_specs, check_vma=False)
```

```python
import jax
import jax.numpy as jnp
from jax import lax
from jax.sharding import PartitionSpec as P

HEADS = 20
HEAD_DIM = 112


NORM_EPS = 1e-06
SHARE_EPS = 1e-06


def padded_2(cells, sides, width):
    for axis, dim in sides:
        count = lax.axis_size(axis)
        ends = count - 1
        head = lax.slice_in_dim(cells, 0, width, axis=dim)
        tail = lax.slice_in_dim(cells, cells.shape[dim] - width, cells.shape[dim], axis=dim)
        cells = jnp.concatenate(
            [
                lax.ppermute(tail, axis, [(i, (i + 1) % count) for i in range(ends)]),
                cells,
                lax.ppermute(head, axis, [((i + 1) % count, i) for i in range(ends)]),
            ],
            axis=dim,
        )
    return cells


def exchange_steps(axes):
    steps = []
    for axis in axes:
        count = lax.axis_size(axis)
        bit = 1
        while bit < count:
            steps.append((axis, count, bit))
            bit *= 2
    return steps


def halving_sum(block, axes):
    steps = exchange_steps(axes)
    for axis, count, bit in steps:
        upper = (lax.axis_index(axis) & bit) != 0
        half = block.shape[1] // 2
        low, high = block[:, :half], block[:, half:]
        sent = jnp.where(upper, low, high)
        kept = jnp.where(upper, high, low)
        block = kept + lax.ppermute(sent, axis, [(i, i ^ bit) for i in range(count)])
    for axis, count, bit in reversed(steps):
        upper = (lax.axis_index(axis) & bit) != 0
        other = lax.ppermute(block, axis, [(i, i ^ bit) for i in range(count)])
        block = jnp.where(
            upper, jnp.concatenate([other, block], 1), jnp.concatenate([block, other], 1)
        )
    return block


def pick(blocks, index):
    stacked = jnp.stack(blocks)
    return lax.dynamic_index_in_dim(stacked, index, axis=0, keepdims=False)


def swap_chunks(chunks, axis):
    count = lax.axis_size(axis)
    own = lax.axis_index(axis)
    by_mask = [pick(chunks, own)]
    for mask in range(1, count):
        sent = pick(chunks, own ^ mask)
        by_mask.append(lax.ppermute(sent, axis, [(i, i ^ mask) for i in range(count)]))
    return [pick(by_mask, own ^ source) for source in range(count)]


def rms_norm(features):
    return features * lax.rsqrt(jnp.mean(features * features, axis=-1, keepdims=True) + NORM_EPS)


def depthwise(padded, conv_taps, row_count, col_count, half_width):
    widened = jnp.pad(padded, ((0, 0), (0, 0), (1, 1), (0, 0)))
    summed = jnp.zeros((padded.shape[0], row_count, col_count, padded.shape[3]), jnp.float32)
    for row_off in range(3):
        for col_off in range(3):
            window = widened[
                :, row_off : row_off + row_count, col_off : col_off + col_count, :
            ].astype(jnp.float32)
            summed = summed + window * conv_taps[row_off * 3 + col_off]
    return (summed[..., :half_width] * jax.nn.silu(summed[..., half_width:])).astype(jnp.bfloat16)


def local(
    query_in, key_in, value_in, stream_in, attn_gain, ffn_gain, in_weight, conv_weight, out_weight
):
    frame_count, row_count, col_count, model_width = query_in.shape
    token_count = frame_count * row_count * col_count
    local_gated = in_weight.shape[2]
    highest = lax.Precision.HIGHEST
    key_pos = jnp.maximum(key_in, 0).reshape(token_count, HEADS, HEAD_DIM)
    value_heads = value_in.reshape(token_count, HEADS, HEAD_DIM)
    local_state = jnp.einsum(
        "thi,thj->ihj", key_pos, value_heads, preferred_element_type=jnp.float32
    ).reshape(HEAD_DIM, model_width)
    local_total = jnp.sum(key_pos.reshape(token_count, model_width), axis=0, dtype=jnp.float32)
    stats = jnp.concatenate([local_state, local_total[None, :]], axis=0)
    parts = 1
    for axis, count, bit in exchange_steps(("frame", "row")):
        parts *= 2
    padded_width = -(-model_width // parts) * parts
    stats = jnp.pad(stats, ((0, 0), (0, padded_width - model_width)))
    stats = halving_sum(stats, ("frame", "row"))[:, :model_width]
    kv_state, key_total = stats[:HEAD_DIM], stats[HEAD_DIM]
    query_pos = jnp.maximum(query_in, 0).reshape(token_count, HEADS, HEAD_DIM).astype(jnp.float32)
    numerator = jnp.einsum(
        "thi,ihj->thj", query_pos, kv_state.reshape(HEAD_DIM, HEADS, HEAD_DIM), precision=highest
    )
    denominator = jnp.einsum(
        "thi,hi->th", query_pos, key_total.reshape(HEADS, HEAD_DIM), precision=highest
    )
    attended = (numerator / (denominator[:, :, None] + SHARE_EPS)).reshape(token_count, model_width)
    stream_flat = stream_in.reshape(token_count, model_width).astype(jnp.float32)
    stream_out = (stream_flat + attn_gain.astype(jnp.float32) * rms_norm(attended)).astype(
        jnp.bfloat16
    )
    normed = (rms_norm(stream_out.astype(jnp.float32)) * ffn_gain.astype(jnp.float32)).astype(
        jnp.bfloat16
    )
    normed_grid = normed.reshape(frame_count, row_count, col_count, model_width)
    conv_taps = conv_weight.reshape(9, 2 * local_gated).astype(jnp.float32)
    row_parts = lax.axis_size("row")
    local_depth = in_weight.shape[0]
    depth_chunks = [
        normed_grid[..., part * local_depth : (part + 1) * local_depth] for part in range(row_parts)
    ]
    by_row = jnp.concatenate(swap_chunks(depth_chunks, "row"), axis=1)
    frame_parts = lax.axis_size("frame")
    by_frame = swap_chunks([by_row] * frame_parts, "frame")
    whole_frames = frame_parts == row_parts and frame_count == 1 and row_count == 1
    weight_flat = in_weight.reshape(local_depth, 2 * local_gated)
    if whole_frames:
        tokens = jnp.stack([piece[0] for piece in by_frame])
        partial = jnp.dot(
            tokens.reshape(-1, local_depth), weight_flat, preferred_element_type=jnp.float32
        ).astype(jnp.bfloat16)
        summed = lax.psum_scatter(partial, "row", scatter_dimension=0, tiled=True)
        frame_rows = tokens.shape[1]
        expanded = (
            jax.nn.silu(summed.astype(jnp.float32))
            .astype(jnp.bfloat16)
            .reshape(1, frame_rows, col_count, 2 * local_gated)
        )
        padded_expanded = jnp.pad(expanded, ((0, 0), (1, 1), (0, 0), (0, 0)))
        hidden = depthwise(padded_expanded, conv_taps, frame_rows, col_count, local_gated)
        projected = jnp.dot(
            hidden.reshape(-1, local_gated), out_weight, preferred_element_type=jnp.float32
        ).astype(jnp.bfloat16)
        row_blocks = jnp.split(projected, frame_parts, axis=0)
        crossed = sum(piece.astype(jnp.float32) for piece in swap_chunks(row_blocks, "frame"))
        ffn_rows = lax.ppermute(
            crossed,
            ("frame", "row"),
            [(f * row_parts + r, r * row_parts + f) for f in range(frame_parts) for r in range(row_parts)],
        ).reshape(token_count, model_width)
        block_out = (stream_out.astype(jnp.float32) + ffn_rows).astype(jnp.bfloat16)
        grid_shape = (frame_count, row_count, col_count, model_width)
        return (stream_out.reshape(grid_shape), block_out.reshape(grid_shape))
    tokens = jnp.stack([piece.transpose(1, 0, 2, 3) for piece in by_frame], axis=1)
    piece_frames = tokens.shape[1] * tokens.shape[2]
    partial = jnp.dot(
        tokens.reshape(-1, local_depth), weight_flat, preferred_element_type=jnp.float32
    ).astype(jnp.bfloat16)
    summed = lax.psum_scatter(partial, "row", scatter_dimension=0, tiled=True).reshape(
        piece_frames, row_count, col_count, 2 * local_gated
    )
    expanded = jax.nn.silu(summed.astype(jnp.float32)).astype(jnp.bfloat16)
    padded_expanded = padded_2(expanded, (("row", 1),), 1)
    hidden = depthwise(padded_expanded, conv_taps, row_count, col_count, local_gated)
    hidden_flat = hidden.reshape(-1, local_gated)
    projected = jnp.dot(hidden_flat, out_weight, preferred_element_type=jnp.float32).astype(
        jnp.bfloat16
    )
    frame_blocks = jnp.split(projected, frame_parts, axis=0)
    ffn_rows = sum(
        piece.astype(jnp.float32) for piece in swap_chunks(frame_blocks, "frame")
    ).reshape(token_count, model_width)
    block_out = (stream_out.astype(jnp.float32) + ffn_rows).astype(jnp.bfloat16)
    grid_shape = (frame_count, row_count, col_count, model_width)
    return (stream_out.reshape(grid_shape), block_out.reshape(grid_shape))


def solution(mesh):
    in_specs = (
        P(("groups", "frame"), "row", None, None),
        P(("groups", "frame"), "row", None, None),
        P(("groups", "frame"), "row", None, None),
        P(("groups", "frame"), "row", None, None),
        P(),
        P(),
        P("row", None, "frame"),
        P(None, None, "frame"),
        P("frame", None),
    )
    out_specs = (
        P(("groups", "frame"), "row", None, None),
        P(("groups", "frame"), "row", None, None),
    )
    return jax.shard_map(local, mesh=mesh, in_specs=in_specs, out_specs=out_specs, check_vma=False)
```

```python
import jax
import jax.numpy as jnp
from jax import lax
from jax.sharding import PartitionSpec as P

HEADS = 20
HEAD_DIM = 112


NORM_EPS = 1e-06
SHARE_EPS = 1e-06


def padded_2(cells, sides, width):
    for axis, dim in sides:
        count = lax.axis_size(axis)
        ends = count - 1
        head = lax.slice_in_dim(cells, 0, width, axis=dim)
        tail = lax.slice_in_dim(cells, cells.shape[dim] - width, cells.shape[dim], axis=dim)
        cells = jnp.concatenate(
            [
                lax.ppermute(tail, axis, [(i, (i + 1) % count) for i in range(ends)]),
                cells,
                lax.ppermute(head, axis, [((i + 1) % count, i) for i in range(ends)]),
            ],
            axis=dim,
        )
    return cells


def exchange_steps(axes):
    steps = []
    for axis in axes:
        count = lax.axis_size(axis)
        bit = 1
        while bit < count:
            steps.append((axis, count, bit))
            bit *= 2
    return steps


def halving_sum(block, axes):
    steps = exchange_steps(axes)
    for axis, count, bit in steps:
        upper = (lax.axis_index(axis) & bit) != 0
        half = block.shape[1] // 2
        low, high = block[:, :half], block[:, half:]
        sent = jnp.where(upper, low, high)
        kept = jnp.where(upper, high, low)
        block = kept + lax.ppermute(sent, axis, [(i, i ^ bit) for i in range(count)])
    for axis, count, bit in reversed(steps):
        upper = (lax.axis_index(axis) & bit) != 0
        other = lax.ppermute(block, axis, [(i, i ^ bit) for i in range(count)])
        block = jnp.where(
            upper, jnp.concatenate([other, block], 1), jnp.concatenate([block, other], 1)
        )
    return block


def pick(blocks, index):
    stacked = jnp.stack(blocks)
    return lax.dynamic_index_in_dim(stacked, index, axis=0, keepdims=False)


def swap_chunks(chunks, axis):
    count = lax.axis_size(axis)
    own = lax.axis_index(axis)
    by_mask = [pick(chunks, own)]
    for mask in range(1, count):
        sent = pick(chunks, own ^ mask)
        by_mask.append(lax.ppermute(sent, axis, [(i, i ^ mask) for i in range(count)]))
    return [pick(by_mask, own ^ source) for source in range(count)]


def rms_norm(features):
    return features * lax.rsqrt(jnp.mean(features * features, axis=-1, keepdims=True) + NORM_EPS)


def depthwise(padded, conv_taps, row_count, col_count, half_width):
    widened = jnp.pad(padded, ((0, 0), (0, 0), (1, 1), (0, 0)))
    summed = jnp.zeros((padded.shape[0], row_count, col_count, padded.shape[3]), jnp.float32)
    for row_off in range(3):
        for col_off in range(3):
            window = widened[
                :, row_off : row_off + row_count, col_off : col_off + col_count, :
            ].astype(jnp.float32)
            summed = summed + window * conv_taps[row_off * 3 + col_off]
    return (summed[..., :half_width] * jax.nn.silu(summed[..., half_width:])).astype(jnp.bfloat16)


def local(
    query_in, key_in, value_in, stream_in, attn_gain, ffn_gain, in_weight, conv_weight, out_weight
):
    frame_count, row_count, col_count, model_width = query_in.shape
    token_count = frame_count * row_count * col_count
    local_gated = in_weight.shape[2]
    highest = lax.Precision.HIGHEST
    key_pos = jnp.maximum(key_in, 0).reshape(token_count, HEADS, HEAD_DIM)
    value_heads = value_in.reshape(token_count, HEADS, HEAD_DIM)
    local_state = jnp.einsum(
        "thi,thj->ihj", key_pos, value_heads, preferred_element_type=jnp.float32
    ).reshape(HEAD_DIM, model_width)
    local_total = jnp.sum(key_pos.reshape(token_count, model_width), axis=0, dtype=jnp.float32)
    stats = jnp.concatenate([local_state, local_total[None, :]], axis=0)
    parts = 1
    for axis, count, bit in exchange_steps(("frame", "row")):
        parts *= 2
    padded_width = -(-model_width // parts) * parts
    stats = jnp.pad(stats, ((0, 0), (0, padded_width - model_width)))
    stats = halving_sum(stats, ("frame", "row"))[:, :model_width]
    kv_state, key_total = stats[:HEAD_DIM], stats[HEAD_DIM]
    query_pos = jnp.maximum(query_in, 0).reshape(token_count, HEADS, HEAD_DIM).astype(jnp.float32)
    numerator = jnp.einsum(
        "thi,ihj->thj", query_pos, kv_state.reshape(HEAD_DIM, HEADS, HEAD_DIM), precision=highest
    )
    denominator = jnp.einsum(
        "thi,hi->th", query_pos, key_total.reshape(HEADS, HEAD_DIM), precision=highest
    )
    attended = (numerator / (denominator[:, :, None] + SHARE_EPS)).reshape(token_count, model_width)
    stream_flat = stream_in.reshape(token_count, model_width).astype(jnp.float32)
    stream_out = (stream_flat + attn_gain.astype(jnp.float32) * rms_norm(attended)).astype(
        jnp.bfloat16
    )
    normed = (rms_norm(stream_out.astype(jnp.float32)) * ffn_gain.astype(jnp.float32)).astype(
        jnp.bfloat16
    )
    normed_grid = normed.reshape(frame_count, row_count, col_count, model_width)
    conv_taps = conv_weight.reshape(9, 2 * local_gated).astype(jnp.float32)
    row_parts = lax.axis_size("row")
    local_depth = in_weight.shape[0]
    depth_chunks = [
        normed_grid[..., part * local_depth : (part + 1) * local_depth] for part in range(row_parts)
    ]
    by_row = jnp.concatenate(swap_chunks(depth_chunks, "row"), axis=1)
    frame_parts = lax.axis_size("frame")
    by_frame = swap_chunks([by_row] * frame_parts, "frame")
    whole_frames = frame_parts == row_parts and frame_count == 1 and row_count == 1
    weight_flat = in_weight.reshape(local_depth, 2 * local_gated)
    if whole_frames:
        tokens = jnp.stack([piece[0] for piece in by_frame])
        partial = jnp.dot(
            tokens.reshape(-1, local_depth), weight_flat, preferred_element_type=jnp.float32
        ).astype(jnp.bfloat16)
        summed = lax.psum_scatter(partial, "row", scatter_dimension=0, tiled=True)
        frame_rows = tokens.shape[1]
        expanded = (
            jax.nn.silu(summed.astype(jnp.float32))
            .astype(jnp.bfloat16)
            .reshape(1, frame_rows, col_count, 2 * local_gated)
        )
        padded_expanded = jnp.pad(expanded, ((0, 0), (1, 1), (0, 0), (0, 0)))
        hidden = depthwise(padded_expanded, conv_taps, frame_rows, col_count, local_gated)
        projected = jnp.dot(
            hidden.reshape(-1, local_gated), out_weight, preferred_element_type=jnp.float32
        ).astype(jnp.bfloat16)
        row_blocks = jnp.split(projected, frame_parts, axis=0)
        frame_at = lax.axis_index("frame")
        arrived = []
        for mask in range(row_parts):
            arrived.append(
                lax.ppermute(
                    pick(row_blocks, frame_at ^ mask),
                    ("frame", "row"),
                    [
                        (f * row_parts + r, r * row_parts + (f ^ mask))
                        for f in range(frame_parts)
                        for r in range(row_parts)
                    ],
                ).astype(jnp.float32)
            )
        ffn_rows = sum(arrived).reshape(token_count, model_width)
        block_out = (stream_out.astype(jnp.float32) + ffn_rows).astype(jnp.bfloat16)
        grid_shape = (frame_count, row_count, col_count, model_width)
        return (stream_out.reshape(grid_shape), block_out.reshape(grid_shape))
    tokens = jnp.stack([piece.transpose(1, 0, 2, 3) for piece in by_frame], axis=1)
    piece_frames = tokens.shape[1] * tokens.shape[2]
    partial = jnp.dot(
        tokens.reshape(-1, local_depth), weight_flat, preferred_element_type=jnp.float32
    ).astype(jnp.bfloat16)
    summed = lax.psum_scatter(partial, "row", scatter_dimension=0, tiled=True).reshape(
        piece_frames, row_count, col_count, 2 * local_gated
    )
    expanded = jax.nn.silu(summed.astype(jnp.float32)).astype(jnp.bfloat16)
    padded_expanded = padded_2(expanded, (("row", 1),), 1)
    hidden = depthwise(padded_expanded, conv_taps, row_count, col_count, local_gated)
    hidden_flat = hidden.reshape(-1, local_gated)
    projected = jnp.dot(hidden_flat, out_weight, preferred_element_type=jnp.float32).astype(
        jnp.bfloat16
    )
    frame_blocks = jnp.split(projected, frame_parts, axis=0)
    ffn_rows = sum(
        piece.astype(jnp.float32) for piece in swap_chunks(frame_blocks, "frame")
    ).reshape(token_count, model_width)
    block_out = (stream_out.astype(jnp.float32) + ffn_rows).astype(jnp.bfloat16)
    grid_shape = (frame_count, row_count, col_count, model_width)
    return (stream_out.reshape(grid_shape), block_out.reshape(grid_shape))


def solution(mesh):
    in_specs = (
        P(("groups", "frame"), "row", None, None),
        P(("groups", "frame"), "row", None, None),
        P(("groups", "frame"), "row", None, None),
        P(("groups", "frame"), "row", None, None),
        P(),
        P(),
        P("row", None, "frame"),
        P(None, None, "frame"),
        P("frame", None),
    )
    out_specs = (
        P(("groups", "frame"), "row", None, None),
        P(("groups", "frame"), "row", None, None),
    )
    return jax.shard_map(local, mesh=mesh, in_specs=in_specs, out_specs=out_specs, check_vma=False)
```

```python
import jax
import jax.numpy as jnp
from jax import lax
from jax.sharding import PartitionSpec as P

HEADS = 20
HEAD_DIM = 112


NORM_EPS = 1e-06
SHARE_EPS = 1e-06


def padded_2(cells, sides, width):
    for axis, dim in sides:
        count = lax.axis_size(axis)
        ends = count - 1
        head = lax.slice_in_dim(cells, 0, width, axis=dim)
        tail = lax.slice_in_dim(cells, cells.shape[dim] - width, cells.shape[dim], axis=dim)
        cells = jnp.concatenate(
            [
                lax.ppermute(tail, axis, [(i, (i + 1) % count) for i in range(ends)]),
                cells,
                lax.ppermute(head, axis, [((i + 1) % count, i) for i in range(ends)]),
            ],
            axis=dim,
        )
    return cells


def exchange_steps(axes):
    steps = []
    for axis in axes:
        count = lax.axis_size(axis)
        bit = 1
        while bit < count:
            steps.append((axis, count, bit))
            bit *= 2
    return steps


def halving_sum(block, axes, inner_axis):
    steps = exchange_steps(axes)
    for axis, count, bit in steps:
        upper = (lax.axis_index(axis) & bit) != 0
        half = block.shape[1] // 2
        low, high = block[:, :half], block[:, half:]
        sent = jnp.where(upper, low, high)
        kept = jnp.where(upper, high, low)
        block = kept + lax.ppermute(sent, axis, [(i, i ^ bit) for i in range(count)])
    inner_count = lax.axis_size(inner_axis)
    pieces = jnp.split(block, inner_count, axis=1)
    mine = sum(swap_chunks(pieces, inner_axis))
    block = jnp.concatenate(swap_chunks([mine] * inner_count, inner_axis), axis=1)
    for axis, count, bit in reversed(steps):
        upper = (lax.axis_index(axis) & bit) != 0
        other = lax.ppermute(block, axis, [(i, i ^ bit) for i in range(count)])
        block = jnp.where(
            upper, jnp.concatenate([other, block], 1), jnp.concatenate([block, other], 1)
        )
    return block


def pick(blocks, index):
    stacked = jnp.stack(blocks)
    return lax.dynamic_index_in_dim(stacked, index, axis=0, keepdims=False)


def swap_chunks(chunks, axis):
    count = lax.axis_size(axis)
    own = lax.axis_index(axis)
    by_mask = [pick(chunks, own)]
    for mask in range(1, count):
        sent = pick(chunks, own ^ mask)
        by_mask.append(lax.ppermute(sent, axis, [(i, i ^ mask) for i in range(count)]))
    return [pick(by_mask, own ^ source) for source in range(count)]


def doubling_gather(block, axis):
    count = lax.axis_size(axis)
    own = lax.axis_index(axis)
    by_mask = {0: block}
    bit = count // 2
    while bit >= 1:
        keys = sorted(by_mask)
        received = lax.ppermute(
            jnp.stack([by_mask[key] for key in keys]), axis, [(i, i ^ bit) for i in range(count)]
        )
        for at, key in enumerate(keys):
            by_mask[key ^ bit] = received[at]
        bit //= 2
    ordered = [by_mask[mask] for mask in range(count)]
    return [pick(ordered, own ^ source) for source in range(count)]


def rms_norm(features):
    return features * lax.rsqrt(jnp.mean(features * features, axis=-1, keepdims=True) + NORM_EPS)


def depthwise(padded, conv_taps, row_count, col_count, half_width):
    widened = jnp.pad(padded, ((0, 0), (0, 0), (1, 1), (0, 0)))
    summed = jnp.zeros((padded.shape[0], row_count, col_count, padded.shape[3]), jnp.float32)
    for row_off in range(3):
        for col_off in range(3):
            window = widened[
                :, row_off : row_off + row_count, col_off : col_off + col_count, :
            ].astype(jnp.float32)
            summed = summed + window * conv_taps[row_off * 3 + col_off]
    return (summed[..., :half_width] * jax.nn.silu(summed[..., half_width:])).astype(jnp.bfloat16)


def local(
    query_in, key_in, value_in, stream_in, attn_gain, ffn_gain, in_weight, conv_weight, out_weight
):
    frame_count, row_count, col_count, model_width = query_in.shape
    token_count = frame_count * row_count * col_count
    local_gated = in_weight.shape[2]
    highest = lax.Precision.HIGHEST
    key_pos = jnp.maximum(key_in, 0).reshape(token_count, HEADS, HEAD_DIM)
    value_heads = value_in.reshape(token_count, HEADS, HEAD_DIM)
    local_state = jnp.einsum(
        "thi,thj->ihj", key_pos, value_heads, preferred_element_type=jnp.float32
    ).reshape(HEAD_DIM, model_width)
    local_total = jnp.sum(key_pos.reshape(token_count, model_width), axis=0, dtype=jnp.float32)
    stats = jnp.concatenate([local_state, local_total[None, :]], axis=0)
    parts = 1
    for axis, count, bit in exchange_steps(("frame", "row")):
        parts *= 2
    padded_width = -(-model_width // parts) * parts
    stats = jnp.pad(stats, ((0, 0), (0, padded_width - model_width)))
    stats = halving_sum(stats, ("frame",), inner_axis="row")[:, :model_width]
    kv_state, key_total = stats[:HEAD_DIM], stats[HEAD_DIM]
    query_pos = jnp.maximum(query_in, 0).reshape(token_count, HEADS, HEAD_DIM).astype(jnp.float32)
    numerator = jnp.einsum(
        "thi,ihj->thj", query_pos, kv_state.reshape(HEAD_DIM, HEADS, HEAD_DIM), precision=highest
    )
    denominator = jnp.einsum(
        "thi,hi->th", query_pos, key_total.reshape(HEADS, HEAD_DIM), precision=highest
    )
    attended = (numerator / (denominator[:, :, None] + SHARE_EPS)).reshape(token_count, model_width)
    stream_flat = stream_in.reshape(token_count, model_width).astype(jnp.float32)
    stream_out = (stream_flat + attn_gain.astype(jnp.float32) * rms_norm(attended)).astype(
        jnp.bfloat16
    )
    normed = (rms_norm(stream_out.astype(jnp.float32)) * ffn_gain.astype(jnp.float32)).astype(
        jnp.bfloat16
    )
    normed_grid = normed.reshape(frame_count, row_count, col_count, model_width)
    conv_taps = conv_weight.reshape(9, 2 * local_gated).astype(jnp.float32)
    row_parts = lax.axis_size("row")
    local_depth = in_weight.shape[0]
    depth_chunks = [
        normed_grid[..., part * local_depth : (part + 1) * local_depth] for part in range(row_parts)
    ]
    by_row = jnp.concatenate(swap_chunks(depth_chunks, "row"), axis=1)
    frame_parts = lax.axis_size("frame")
    by_frame = doubling_gather(by_row, "frame")
    whole_frames = frame_parts == row_parts and frame_count == 1 and row_count == 1
    weight_flat = in_weight.reshape(local_depth, 2 * local_gated)
    if whole_frames:
        tokens = jnp.stack([piece[0] for piece in by_frame])
        partial = jnp.dot(
            tokens.reshape(-1, local_depth), weight_flat, preferred_element_type=jnp.float32
        ).astype(jnp.bfloat16)
        summed = lax.psum_scatter(partial, "row", scatter_dimension=0, tiled=True)
        frame_rows = tokens.shape[1]
        expanded = (
            jax.nn.silu(summed.astype(jnp.float32))
            .astype(jnp.bfloat16)
            .reshape(1, frame_rows, col_count, 2 * local_gated)
        )
        padded_expanded = jnp.pad(expanded, ((0, 0), (1, 1), (0, 0), (0, 0)))
        hidden = depthwise(padded_expanded, conv_taps, frame_rows, col_count, local_gated)
        projected = jnp.dot(
            hidden.reshape(-1, local_gated), out_weight, preferred_element_type=jnp.float32
        ).astype(jnp.bfloat16)
        row_blocks = jnp.split(projected, frame_parts, axis=0)
        frame_at = lax.axis_index("frame")
        arrived = []
        for mask in range(row_parts):
            arrived.append(
                lax.ppermute(
                    pick(row_blocks, frame_at ^ mask),
                    ("frame", "row"),
                    [
                        (f * row_parts + r, r * row_parts + (f ^ mask))
                        for f in range(frame_parts)
                        for r in range(row_parts)
                    ],
                ).astype(jnp.float32)
            )
        ffn_rows = sum(arrived).reshape(token_count, model_width)
        block_out = (stream_out.astype(jnp.float32) + ffn_rows).astype(jnp.bfloat16)
        grid_shape = (frame_count, row_count, col_count, model_width)
        return (stream_out.reshape(grid_shape), block_out.reshape(grid_shape))
    tokens = jnp.stack([piece.transpose(1, 0, 2, 3) for piece in by_frame], axis=1)
    piece_frames = tokens.shape[1] * tokens.shape[2]
    partial = jnp.dot(
        tokens.reshape(-1, local_depth), weight_flat, preferred_element_type=jnp.float32
    ).astype(jnp.bfloat16)
    summed = lax.psum_scatter(partial, "row", scatter_dimension=0, tiled=True).reshape(
        piece_frames, row_count, col_count, 2 * local_gated
    )
    expanded = jax.nn.silu(summed.astype(jnp.float32)).astype(jnp.bfloat16)
    padded_expanded = padded_2(expanded, (("row", 1),), 1)
    hidden = depthwise(padded_expanded, conv_taps, row_count, col_count, local_gated)
    hidden_flat = hidden.reshape(-1, local_gated)
    projected = jnp.dot(hidden_flat, out_weight, preferred_element_type=jnp.float32).astype(
        jnp.bfloat16
    )
    frame_blocks = jnp.split(projected, frame_parts, axis=0)
    ffn_rows = sum(
        piece.astype(jnp.float32) for piece in swap_chunks(frame_blocks, "frame")
    ).reshape(token_count, model_width)
    block_out = (stream_out.astype(jnp.float32) + ffn_rows).astype(jnp.bfloat16)
    grid_shape = (frame_count, row_count, col_count, model_width)
    return (stream_out.reshape(grid_shape), block_out.reshape(grid_shape))


def solution(mesh):
    in_specs = (
        P(("groups", "frame"), "row", None, None),
        P(("groups", "frame"), "row", None, None),
        P(("groups", "frame"), "row", None, None),
        P(("groups", "frame"), "row", None, None),
        P(),
        P(),
        P("row", None, "frame"),
        P(None, None, "frame"),
        P("frame", None),
    )
    out_specs = (
        P(("groups", "frame"), "row", None, None),
        P(("groups", "frame"), "row", None, None),
    )
    return jax.shard_map(local, mesh=mesh, in_specs=in_specs, out_specs=out_specs, check_vma=False)
```

```python
import jax
import jax.numpy as jnp
from jax import lax
from jax.sharding import PartitionSpec as P

HEADS = 20
HEAD_DIM = 112


NORM_EPS = 1e-06
SHARE_EPS = 1e-06


def padded_2(cells, sides, width):
    for axis, dim in sides:
        count = lax.axis_size(axis)
        ends = count - 1
        head = lax.slice_in_dim(cells, 0, width, axis=dim)
        tail = lax.slice_in_dim(cells, cells.shape[dim] - width, cells.shape[dim], axis=dim)
        cells = jnp.concatenate(
            [
                lax.ppermute(tail, axis, [(i, (i + 1) % count) for i in range(ends)]),
                cells,
                lax.ppermute(head, axis, [((i + 1) % count, i) for i in range(ends)]),
            ],
            axis=dim,
        )
    return cells


def exchange_steps(axes):
    steps = []
    for axis in axes:
        count = lax.axis_size(axis)
        bit = 1
        while bit < count:
            steps.append((axis, count, bit))
            bit *= 2
    return steps


def halving_sum(block, axes, inner_axis):
    steps = exchange_steps(axes)
    for axis, count, bit in steps:
        upper = (lax.axis_index(axis) & bit) != 0
        half = block.shape[1] // 2
        low, high = block[:, :half], block[:, half:]
        sent = jnp.where(upper, low, high)
        kept = jnp.where(upper, high, low)
        sent = sent.astype(jnp.bfloat16)
        block = kept + lax.ppermute(sent, axis, [(i, i ^ bit) for i in range(count)]).astype(
            jnp.float32
        )
    inner_count = lax.axis_size(inner_axis)
    pieces = [piece.astype(jnp.bfloat16) for piece in jnp.split(block, inner_count, axis=1)]
    mine = sum(piece.astype(jnp.float32) for piece in swap_chunks(pieces, inner_axis))
    block = jnp.concatenate(swap_chunks([mine] * inner_count, inner_axis), axis=1)
    for axis, count, bit in reversed(steps):
        upper = (lax.axis_index(axis) & bit) != 0
        other = lax.ppermute(block, axis, [(i, i ^ bit) for i in range(count)])
        block = jnp.where(
            upper, jnp.concatenate([other, block], 1), jnp.concatenate([block, other], 1)
        )
    return block


def pick(blocks, index):
    stacked = jnp.stack(blocks)
    return lax.dynamic_index_in_dim(stacked, index, axis=0, keepdims=False)


def swap_chunks(chunks, axis):
    count = lax.axis_size(axis)
    own = lax.axis_index(axis)
    by_mask = [pick(chunks, own)]
    for mask in range(1, count):
        sent = pick(chunks, own ^ mask)
        by_mask.append(lax.ppermute(sent, axis, [(i, i ^ mask) for i in range(count)]))
    return [pick(by_mask, own ^ source) for source in range(count)]


def doubling_gather(block, axis):
    count = lax.axis_size(axis)
    own = lax.axis_index(axis)
    by_mask = {0: block}
    bit = count // 2
    while bit >= 1:
        keys = sorted(by_mask)
        received = lax.ppermute(
            jnp.stack([by_mask[key] for key in keys]), axis, [(i, i ^ bit) for i in range(count)]
        )
        for at, key in enumerate(keys):
            by_mask[key ^ bit] = received[at]
        bit //= 2
    ordered = [by_mask[mask] for mask in range(count)]
    return [pick(ordered, own ^ source) for source in range(count)]


def rms_norm(features):
    return features * lax.rsqrt(jnp.mean(features * features, axis=-1, keepdims=True) + NORM_EPS)


def depthwise(padded, conv_taps, row_count, col_count, half_width):
    widened = jnp.pad(padded, ((0, 0), (0, 0), (1, 1), (0, 0)))
    summed = jnp.zeros((padded.shape[0], row_count, col_count, padded.shape[3]), jnp.float32)
    for row_off in range(3):
        for col_off in range(3):
            window = widened[
                :, row_off : row_off + row_count, col_off : col_off + col_count, :
            ].astype(jnp.float32)
            summed = summed + window * conv_taps[row_off * 3 + col_off]
    return (summed[..., :half_width] * jax.nn.silu(summed[..., half_width:])).astype(jnp.bfloat16)


def local(
    query_in, key_in, value_in, stream_in, attn_gain, ffn_gain, in_weight, conv_weight, out_weight
):
    frame_count, row_count, col_count, model_width = query_in.shape
    token_count = frame_count * row_count * col_count
    local_gated = in_weight.shape[2]
    highest = lax.Precision.HIGHEST
    key_pos = jnp.maximum(key_in, 0).reshape(token_count, HEADS, HEAD_DIM)
    value_heads = value_in.reshape(token_count, HEADS, HEAD_DIM)
    local_state = jnp.einsum(
        "thi,thj->ihj", key_pos, value_heads, preferred_element_type=jnp.float32
    ).reshape(HEAD_DIM, model_width)
    local_total = jnp.sum(key_pos.reshape(token_count, model_width), axis=0, dtype=jnp.float32)
    stats = jnp.concatenate([local_state, local_total[None, :]], axis=0)
    parts = 1
    for axis, count, bit in exchange_steps(("frame", "row")):
        parts *= 2
    padded_width = -(-model_width // parts) * parts
    stats = jnp.pad(stats, ((0, 0), (0, padded_width - model_width)))
    stats = halving_sum(stats, ("frame",), inner_axis="row")[:, :model_width]
    kv_state, key_total = stats[:HEAD_DIM], stats[HEAD_DIM]
    query_pos = jnp.maximum(query_in, 0).reshape(token_count, HEADS, HEAD_DIM).astype(jnp.float32)
    numerator = jnp.einsum(
        "thi,ihj->thj", query_pos, kv_state.reshape(HEAD_DIM, HEADS, HEAD_DIM), precision=highest
    )
    denominator = jnp.einsum(
        "thi,hi->th", query_pos, key_total.reshape(HEADS, HEAD_DIM), precision=highest
    )
    attended = (numerator / (denominator[:, :, None] + SHARE_EPS)).reshape(token_count, model_width)
    stream_flat = stream_in.reshape(token_count, model_width).astype(jnp.float32)
    stream_out = (stream_flat + attn_gain.astype(jnp.float32) * rms_norm(attended)).astype(
        jnp.bfloat16
    )
    normed = (rms_norm(stream_out.astype(jnp.float32)) * ffn_gain.astype(jnp.float32)).astype(
        jnp.bfloat16
    )
    normed_grid = normed.reshape(frame_count, row_count, col_count, model_width)
    conv_taps = conv_weight.reshape(9, 2 * local_gated).astype(jnp.float32)
    row_parts = lax.axis_size("row")
    local_depth = in_weight.shape[0]
    depth_chunks = [
        normed_grid[..., part * local_depth : (part + 1) * local_depth] for part in range(row_parts)
    ]
    by_row = jnp.concatenate(swap_chunks(depth_chunks, "row"), axis=1)
    frame_parts = lax.axis_size("frame")
    by_frame = doubling_gather(by_row, "frame")
    whole_frames = frame_parts == row_parts and frame_count == 1 and row_count == 1
    weight_flat = in_weight.reshape(local_depth, 2 * local_gated)
    if whole_frames:
        tokens = jnp.stack([piece[0] for piece in by_frame])
        partial = jnp.dot(
            tokens.reshape(-1, local_depth), weight_flat, preferred_element_type=jnp.float32
        ).astype(jnp.bfloat16)
        summed = lax.psum_scatter(partial, "row", scatter_dimension=0, tiled=True)
        frame_rows = tokens.shape[1]
        expanded = (
            jax.nn.silu(summed.astype(jnp.float32))
            .astype(jnp.bfloat16)
            .reshape(1, frame_rows, col_count, 2 * local_gated)
        )
        padded_expanded = jnp.pad(expanded, ((0, 0), (1, 1), (0, 0), (0, 0)))
        hidden = depthwise(padded_expanded, conv_taps, frame_rows, col_count, local_gated)
        projected = jnp.dot(
            hidden.reshape(-1, local_gated), out_weight, preferred_element_type=jnp.float32
        ).astype(jnp.bfloat16)
        row_blocks = jnp.split(projected, frame_parts, axis=0)
        frame_at = lax.axis_index("frame")
        arrived = []
        for mask in range(row_parts):
            arrived.append(
                lax.ppermute(
                    pick(row_blocks, frame_at ^ mask),
                    ("frame", "row"),
                    [
                        (f * row_parts + r, r * row_parts + (f ^ mask))
                        for f in range(frame_parts)
                        for r in range(row_parts)
                    ],
                ).astype(jnp.float32)
            )
        ffn_rows = sum(arrived).reshape(token_count, model_width)
        block_out = (stream_out.astype(jnp.float32) + ffn_rows).astype(jnp.bfloat16)
        grid_shape = (frame_count, row_count, col_count, model_width)
        return (stream_out.reshape(grid_shape), block_out.reshape(grid_shape))
    tokens = jnp.stack([piece.transpose(1, 0, 2, 3) for piece in by_frame], axis=1)
    piece_frames = tokens.shape[1] * tokens.shape[2]
    partial = jnp.dot(
        tokens.reshape(-1, local_depth), weight_flat, preferred_element_type=jnp.float32
    ).astype(jnp.bfloat16)
    summed = lax.psum_scatter(partial, "row", scatter_dimension=0, tiled=True).reshape(
        piece_frames, row_count, col_count, 2 * local_gated
    )
    expanded = jax.nn.silu(summed.astype(jnp.float32)).astype(jnp.bfloat16)
    padded_expanded = padded_2(expanded, (("row", 1),), 1)
    hidden = depthwise(padded_expanded, conv_taps, row_count, col_count, local_gated)
    hidden_flat = hidden.reshape(-1, local_gated)
    projected = jnp.dot(hidden_flat, out_weight, preferred_element_type=jnp.float32).astype(
        jnp.bfloat16
    )
    frame_blocks = jnp.split(projected, frame_parts, axis=0)
    ffn_rows = sum(
        piece.astype(jnp.float32) for piece in swap_chunks(frame_blocks, "frame")
    ).reshape(token_count, model_width)
    block_out = (stream_out.astype(jnp.float32) + ffn_rows).astype(jnp.bfloat16)
    grid_shape = (frame_count, row_count, col_count, model_width)
    return (stream_out.reshape(grid_shape), block_out.reshape(grid_shape))


def solution(mesh):
    in_specs = (
        P(("groups", "frame"), "row", None, None),
        P(("groups", "frame"), "row", None, None),
        P(("groups", "frame"), "row", None, None),
        P(("groups", "frame"), "row", None, None),
        P(),
        P(),
        P("row", None, "frame"),
        P(None, None, "frame"),
        P("frame", None),
    )
    out_specs = (
        P(("groups", "frame"), "row", None, None),
        P(("groups", "frame"), "row", None, None),
    )
    return jax.shard_map(local, mesh=mesh, in_specs=in_specs, out_specs=out_specs, check_vma=False)
```

```python
import jax
import jax.numpy as jnp
from jax import lax
from jax.sharding import PartitionSpec as P

HEADS = 20
HEAD_DIM = 112


NORM_EPS = 1e-06
SHARE_EPS = 1e-06


def padded_2(cells, sides, width):
    for axis, dim in sides:
        count = lax.axis_size(axis)
        ends = count - 1
        head = lax.slice_in_dim(cells, 0, width, axis=dim)
        tail = lax.slice_in_dim(cells, cells.shape[dim] - width, cells.shape[dim], axis=dim)
        cells = jnp.concatenate(
            [
                lax.ppermute(tail, axis, [(i, (i + 1) % count) for i in range(ends)]),
                cells,
                lax.ppermute(head, axis, [((i + 1) % count, i) for i in range(ends)]),
            ],
            axis=dim,
        )
    return cells


def exchange_steps(axes):
    steps = []
    for axis in axes:
        count = lax.axis_size(axis)
        bit = 1
        while bit < count:
            steps.append((axis, count, bit))
            bit *= 2
    return steps


def halving_sum(block, axes, inner_axis, rider):
    steps = exchange_steps(axes)
    for at, (axis, count, bit) in enumerate(steps):
        upper = (lax.axis_index(axis) & bit) != 0
        half = block.shape[1] // 2
        low, high = block[:, :half], block[:, half:]
        sent = jnp.where(upper, low, high)
        kept = jnp.where(upper, high, low)
        sent = sent.astype(jnp.bfloat16)
        block = kept + lax.ppermute(sent, axis, [(i, i ^ bit) for i in range(count)]).astype(
            jnp.float32
        )
        if at == 0:
            block, rider = lax.optimization_barrier((block, rider))
    inner_count = lax.axis_size(inner_axis)
    pieces = [piece.astype(jnp.bfloat16) for piece in jnp.split(block, inner_count, axis=1)]
    mine = sum(piece.astype(jnp.float32) for piece in swap_chunks(pieces, inner_axis))
    block = jnp.concatenate(swap_chunks([mine] * inner_count, inner_axis), axis=1)
    for axis, count, bit in reversed(steps):
        upper = (lax.axis_index(axis) & bit) != 0
        other = lax.ppermute(block, axis, [(i, i ^ bit) for i in range(count)])
        block = jnp.where(
            upper, jnp.concatenate([other, block], 1), jnp.concatenate([block, other], 1)
        )
    return block, rider


def pick(blocks, index):
    stacked = jnp.stack(blocks)
    return lax.dynamic_index_in_dim(stacked, index, axis=0, keepdims=False)


def swap_chunks(chunks, axis):
    count = lax.axis_size(axis)
    own = lax.axis_index(axis)
    by_mask = [pick(chunks, own)]
    for mask in range(1, count):
        sent = pick(chunks, own ^ mask)
        by_mask.append(lax.ppermute(sent, axis, [(i, i ^ mask) for i in range(count)]))
    return [pick(by_mask, own ^ source) for source in range(count)]


def doubling_gather(block, axis, by_source=True):
    count = lax.axis_size(axis)
    own = lax.axis_index(axis)
    by_mask = {0: block}
    bit = count // 2
    while bit >= 1:
        keys = sorted(by_mask)
        received = lax.ppermute(
            jnp.stack([by_mask[key] for key in keys]), axis, [(i, i ^ bit) for i in range(count)]
        )
        for at, key in enumerate(keys):
            by_mask[key ^ bit] = received[at]
        bit //= 2
    ordered = [by_mask[mask] for mask in range(count)]
    if not by_source:
        return ordered
    return [pick(ordered, own ^ source) for source in range(count)]


def rms_norm(features):
    return features * lax.rsqrt(jnp.mean(features * features, axis=-1, keepdims=True) + NORM_EPS)


def depthwise(padded, conv_taps, row_count, col_count, half_width):
    widened = jnp.pad(padded, ((0, 0), (0, 0), (1, 1), (0, 0)))
    summed = jnp.zeros((padded.shape[0], row_count, col_count, padded.shape[3]), jnp.float32)
    for row_off in range(3):
        for col_off in range(3):
            window = widened[
                :, row_off : row_off + row_count, col_off : col_off + col_count, :
            ].astype(jnp.float32)
            summed = summed + window * conv_taps[row_off * 3 + col_off]
    return (summed[..., :half_width] * jax.nn.silu(summed[..., half_width:])).astype(jnp.bfloat16)


def local(
    query_in, key_in, value_in, stream_in, attn_gain, ffn_gain, in_weight, conv_weight, out_weight
):
    frame_count, row_count, col_count, model_width = query_in.shape
    token_count = frame_count * row_count * col_count
    local_gated = in_weight.shape[2]
    highest = lax.Precision.HIGHEST
    key_pos = jnp.maximum(key_in, 0).reshape(token_count, HEADS, HEAD_DIM)
    value_heads = value_in.reshape(token_count, HEADS, HEAD_DIM)
    local_state = jnp.einsum(
        "thi,thj->ihj", key_pos, value_heads, preferred_element_type=jnp.float32
    ).reshape(HEAD_DIM, model_width)
    local_total = jnp.sum(key_pos.reshape(token_count, model_width), axis=0, dtype=jnp.float32)
    stats = jnp.concatenate([local_state, local_total[None, :]], axis=0)
    parts = 1
    for axis, count, bit in exchange_steps(("frame", "row")):
        parts *= 2
    padded_width = -(-model_width // parts) * parts
    stats = jnp.pad(stats, ((0, 0), (0, padded_width - model_width)))
    weight_flat = in_weight.reshape(in_weight.shape[0], 2 * local_gated)
    stats, weight_flat = halving_sum(stats, ("frame",), "row", weight_flat)
    stats = stats[:, :model_width]
    kv_state, key_total = stats[:HEAD_DIM], stats[HEAD_DIM]
    query_pos = jnp.maximum(query_in, 0).reshape(token_count, HEADS, HEAD_DIM).astype(jnp.float32)
    numerator = jnp.einsum(
        "thi,ihj->thj", query_pos, kv_state.reshape(HEAD_DIM, HEADS, HEAD_DIM), precision=highest
    )
    denominator = jnp.einsum(
        "thi,hi->th", query_pos, key_total.reshape(HEADS, HEAD_DIM), precision=highest
    )
    attended = (numerator / (denominator[:, :, None] + SHARE_EPS)).reshape(token_count, model_width)
    stream_flat = stream_in.reshape(token_count, model_width).astype(jnp.float32)
    stream_out = (stream_flat + attn_gain.astype(jnp.float32) * rms_norm(attended)).astype(
        jnp.bfloat16
    )
    normed = (rms_norm(stream_out.astype(jnp.float32)) * ffn_gain.astype(jnp.float32)).astype(
        jnp.bfloat16
    )
    normed_grid = normed.reshape(frame_count, row_count, col_count, model_width)
    conv_taps = conv_weight.reshape(9, 2 * local_gated).astype(jnp.float32)
    row_parts = lax.axis_size("row")
    local_depth = in_weight.shape[0]
    depth_chunks = [
        normed_grid[..., part * local_depth : (part + 1) * local_depth] for part in range(row_parts)
    ]
    by_row = jnp.concatenate(swap_chunks(depth_chunks, "row"), axis=1)
    frame_parts = lax.axis_size("frame")
    whole_frames = frame_parts == row_parts and frame_count == 1 and row_count == 1
    by_frame = doubling_gather(by_row, "frame", by_source=not whole_frames)
    if whole_frames:
        tokens = jnp.stack([piece[0] for piece in by_frame])
        partial = jnp.dot(
            tokens.reshape(-1, local_depth), weight_flat, preferred_element_type=jnp.float32
        ).astype(jnp.bfloat16)
        summed = lax.psum_scatter(partial, "row", scatter_dimension=0, tiled=True)
        frame_rows = tokens.shape[1]
        expanded = (
            jax.nn.silu(summed.astype(jnp.float32))
            .astype(jnp.bfloat16)
            .reshape(1, frame_rows, col_count, 2 * local_gated)
        )
        padded_expanded = jnp.pad(expanded, ((0, 0), (1, 1), (0, 0), (0, 0)))
        hidden = depthwise(padded_expanded, conv_taps, frame_rows, col_count, local_gated)
        projected = jnp.dot(
            hidden.reshape(-1, local_gated), out_weight, preferred_element_type=jnp.float32
        ).astype(jnp.bfloat16)
        row_blocks = jnp.split(projected, frame_parts, axis=0)
        frame_at = lax.axis_index("frame")
        arrived = []
        for mask in range(row_parts):
            arrived.append(
                lax.ppermute(
                    pick(row_blocks, frame_at ^ mask),
                    ("frame", "row"),
                    [
                        (f * row_parts + r, (f ^ r) * row_parts + (f ^ mask))
                        for f in range(frame_parts)
                        for r in range(row_parts)
                    ],
                ).astype(jnp.float32)
            )
        ffn_rows = sum(arrived).reshape(token_count, model_width)
        block_out = (stream_out.astype(jnp.float32) + ffn_rows).astype(jnp.bfloat16)
        grid_shape = (frame_count, row_count, col_count, model_width)
        return (stream_out.reshape(grid_shape), block_out.reshape(grid_shape))
    tokens = jnp.stack([piece.transpose(1, 0, 2, 3) for piece in by_frame], axis=1)
    piece_frames = tokens.shape[1] * tokens.shape[2]
    partial = jnp.dot(
        tokens.reshape(-1, local_depth), weight_flat, preferred_element_type=jnp.float32
    ).astype(jnp.bfloat16)
    summed = lax.psum_scatter(partial, "row", scatter_dimension=0, tiled=True).reshape(
        piece_frames, row_count, col_count, 2 * local_gated
    )
    expanded = jax.nn.silu(summed.astype(jnp.float32)).astype(jnp.bfloat16)
    padded_expanded = padded_2(expanded, (("row", 1),), 1)
    hidden = depthwise(padded_expanded, conv_taps, row_count, col_count, local_gated)
    hidden_flat = hidden.reshape(-1, local_gated)
    projected = jnp.dot(hidden_flat, out_weight, preferred_element_type=jnp.float32).astype(
        jnp.bfloat16
    )
    frame_blocks = jnp.split(projected, frame_parts, axis=0)
    ffn_rows = sum(
        piece.astype(jnp.float32) for piece in swap_chunks(frame_blocks, "frame")
    ).reshape(token_count, model_width)
    block_out = (stream_out.astype(jnp.float32) + ffn_rows).astype(jnp.bfloat16)
    grid_shape = (frame_count, row_count, col_count, model_width)
    return (stream_out.reshape(grid_shape), block_out.reshape(grid_shape))


def solution(mesh):
    in_specs = (
        P(("groups", "frame"), "row", None, None),
        P(("groups", "frame"), "row", None, None),
        P(("groups", "frame"), "row", None, None),
        P(("groups", "frame"), "row", None, None),
        P(),
        P(),
        P("row", None, "frame"),
        P(None, None, "frame"),
        P("frame", None),
    )
    out_specs = (
        P(("groups", "frame"), "row", None, None),
        P(("groups", "frame"), "row", None, None),
    )
    return jax.shard_map(local, mesh=mesh, in_specs=in_specs, out_specs=out_specs, check_vma=False)
```

```python
import jax
import jax.numpy as jnp
from jax import lax
from jax.sharding import PartitionSpec as P

HEADS = 20
HEAD_DIM = 112


NORM_EPS = 1e-06
SHARE_EPS = 1e-06


def padded_2(cells, sides, width):
    for axis, dim in sides:
        count = lax.axis_size(axis)
        ends = count - 1
        head = lax.slice_in_dim(cells, 0, width, axis=dim)
        tail = lax.slice_in_dim(cells, cells.shape[dim] - width, cells.shape[dim], axis=dim)
        cells = jnp.concatenate(
            [
                lax.ppermute(tail, axis, [(i, (i + 1) % count) for i in range(ends)]),
                cells,
                lax.ppermute(head, axis, [((i + 1) % count, i) for i in range(ends)]),
            ],
            axis=dim,
        )
    return cells


def exchange_steps(axes):
    steps = []
    for axis in axes:
        count = lax.axis_size(axis)
        bit = 1
        while bit < count:
            steps.append((axis, count, bit))
            bit *= 2
    return steps


def halving_sum(block, axes, inner_axis):
    steps = exchange_steps(axes)
    for axis, count, bit in steps:
        upper = (lax.axis_index(axis) & bit) != 0
        half = block.shape[1] // 2
        low, high = block[:, :half], block[:, half:]
        sent = jnp.where(upper, low, high)
        kept = jnp.where(upper, high, low)
        sent = sent.astype(jnp.bfloat16)
        block = kept + lax.ppermute(sent, axis, [(i, i ^ bit) for i in range(count)]).astype(
            jnp.float32
        )
    inner_count = lax.axis_size(inner_axis)
    pieces = [piece.astype(jnp.bfloat16) for piece in jnp.split(block, inner_count, axis=1)]
    mine = sum(piece.astype(jnp.float32) for piece in swap_chunks(pieces, inner_axis))
    shared = swap_chunks([mine.astype(jnp.bfloat16)] * inner_count, inner_axis)
    block = jnp.concatenate([piece.astype(jnp.float32) for piece in shared], axis=1)
    for axis, count, bit in reversed(steps):
        upper = (lax.axis_index(axis) & bit) != 0
        other = lax.ppermute(
            block.astype(jnp.bfloat16), axis, [(i, i ^ bit) for i in range(count)]
        ).astype(jnp.float32)
        block = jnp.where(
            upper, jnp.concatenate([other, block], 1), jnp.concatenate([block, other], 1)
        )
    return block


def pick(blocks, index):
    stacked = jnp.stack(blocks)
    return lax.dynamic_index_in_dim(stacked, index, axis=0, keepdims=False)


def swap_chunks(chunks, axis):
    count = lax.axis_size(axis)
    own = lax.axis_index(axis)
    by_mask = [pick(chunks, own)]
    for mask in range(1, count):
        sent = pick(chunks, own ^ mask)
        by_mask.append(lax.ppermute(sent, axis, [(i, i ^ mask) for i in range(count)]))
    return [pick(by_mask, own ^ source) for source in range(count)]


def doubling_gather(block, axis):
    count = lax.axis_size(axis)
    own = lax.axis_index(axis)
    by_mask = {0: block}
    bit = count // 2
    while bit >= 1:
        keys = sorted(by_mask)
        received = lax.ppermute(
            jnp.stack([by_mask[key] for key in keys]), axis, [(i, i ^ bit) for i in range(count)]
        )
        for at, key in enumerate(keys):
            by_mask[key ^ bit] = received[at]
        bit //= 2
    ordered = [by_mask[mask] for mask in range(count)]
    return [pick(ordered, own ^ source) for source in range(count)]


def rms_norm(features):
    return features * lax.rsqrt(jnp.mean(features * features, axis=-1, keepdims=True) + NORM_EPS)


def depthwise(padded, conv_taps, row_count, col_count, half_width):
    widened = jnp.pad(padded, ((0, 0), (0, 0), (1, 1), (0, 0)))
    summed = jnp.zeros((padded.shape[0], row_count, col_count, padded.shape[3]), jnp.float32)
    for row_off in range(3):
        for col_off in range(3):
            window = widened[
                :, row_off : row_off + row_count, col_off : col_off + col_count, :
            ].astype(jnp.float32)
            summed = summed + window * conv_taps[row_off * 3 + col_off]
    return (summed[..., :half_width] * jax.nn.silu(summed[..., half_width:])).astype(jnp.bfloat16)


def local(
    query_in, key_in, value_in, stream_in, attn_gain, ffn_gain, in_weight, conv_weight, out_weight
):
    frame_count, row_count, col_count, model_width = query_in.shape
    token_count = frame_count * row_count * col_count
    local_gated = in_weight.shape[2]
    highest = lax.Precision.HIGHEST
    key_pos = jnp.maximum(key_in, 0).reshape(token_count, HEADS, HEAD_DIM)
    value_heads = value_in.reshape(token_count, HEADS, HEAD_DIM)
    local_state = jnp.einsum(
        "thi,thj->ihj", key_pos, value_heads, preferred_element_type=jnp.float32
    ).reshape(HEAD_DIM, model_width)
    local_total = jnp.sum(key_pos.reshape(token_count, model_width), axis=0, dtype=jnp.float32)
    stats = jnp.concatenate([local_state, local_total[None, :]], axis=0)
    parts = 1
    for axis, count, bit in exchange_steps(("frame", "row")):
        parts *= 2
    padded_width = -(-model_width // parts) * parts
    stats = jnp.pad(stats, ((0, 0), (0, padded_width - model_width)))
    stats = halving_sum(stats, ("frame",), inner_axis="row")[:, :model_width]
    kv_state, key_total = stats[:HEAD_DIM], stats[HEAD_DIM]
    query_pos = jnp.maximum(query_in, 0).reshape(token_count, HEADS, HEAD_DIM).astype(jnp.float32)
    numerator = jnp.einsum(
        "thi,ihj->thj", query_pos, kv_state.reshape(HEAD_DIM, HEADS, HEAD_DIM), precision=highest
    )
    denominator = jnp.einsum(
        "thi,hi->th", query_pos, key_total.reshape(HEADS, HEAD_DIM), precision=highest
    )
    attended = (numerator / (denominator[:, :, None] + SHARE_EPS)).reshape(token_count, model_width)
    stream_flat = stream_in.reshape(token_count, model_width).astype(jnp.float32)
    stream_out = (stream_flat + attn_gain.astype(jnp.float32) * rms_norm(attended)).astype(
        jnp.bfloat16
    )
    normed = (rms_norm(stream_out.astype(jnp.float32)) * ffn_gain.astype(jnp.float32)).astype(
        jnp.bfloat16
    )
    normed_grid = normed.reshape(frame_count, row_count, col_count, model_width)
    conv_taps = conv_weight.reshape(9, 2 * local_gated).astype(jnp.float32)
    row_parts = lax.axis_size("row")
    local_depth = in_weight.shape[0]
    depth_chunks = [
        normed_grid[..., part * local_depth : (part + 1) * local_depth] for part in range(row_parts)
    ]
    by_row = jnp.concatenate(swap_chunks(depth_chunks, "row"), axis=1)
    frame_parts = lax.axis_size("frame")
    by_frame = doubling_gather(by_row, "frame")
    whole_frames = frame_parts == row_parts and frame_count == 1 and row_count == 1
    weight_flat = in_weight.reshape(local_depth, 2 * local_gated)
    if whole_frames:
        tokens = jnp.stack([piece[0] for piece in by_frame])
        partial = jnp.dot(
            tokens.reshape(-1, local_depth), weight_flat, preferred_element_type=jnp.float32
        ).astype(jnp.bfloat16)
        summed = lax.psum_scatter(partial, "row", scatter_dimension=0, tiled=True)
        frame_rows = tokens.shape[1]
        expanded = (
            jax.nn.silu(summed.astype(jnp.float32))
            .astype(jnp.bfloat16)
            .reshape(1, frame_rows, col_count, 2 * local_gated)
        )
        padded_expanded = jnp.pad(expanded, ((0, 0), (1, 1), (0, 0), (0, 0)))
        hidden = depthwise(padded_expanded, conv_taps, frame_rows, col_count, local_gated)
        projected = jnp.dot(
            hidden.reshape(-1, local_gated), out_weight, preferred_element_type=jnp.float32
        ).astype(jnp.bfloat16)
        row_blocks = jnp.split(projected, frame_parts, axis=0)
        frame_at = lax.axis_index("frame")
        arrived = []
        for mask in range(row_parts):
            arrived.append(
                lax.ppermute(
                    pick(row_blocks, frame_at ^ mask),
                    ("frame", "row"),
                    [
                        (f * row_parts + r, r * row_parts + (f ^ mask))
                        for f in range(frame_parts)
                        for r in range(row_parts)
                    ],
                ).astype(jnp.float32)
            )
        ffn_rows = sum(arrived).reshape(token_count, model_width)
        block_out = (stream_out.astype(jnp.float32) + ffn_rows).astype(jnp.bfloat16)
        grid_shape = (frame_count, row_count, col_count, model_width)
        return (stream_out.reshape(grid_shape), block_out.reshape(grid_shape))
    tokens = jnp.stack([piece.transpose(1, 0, 2, 3) for piece in by_frame], axis=1)
    piece_frames = tokens.shape[1] * tokens.shape[2]
    partial = jnp.dot(
        tokens.reshape(-1, local_depth), weight_flat, preferred_element_type=jnp.float32
    ).astype(jnp.bfloat16)
    summed = lax.psum_scatter(partial, "row", scatter_dimension=0, tiled=True).reshape(
        piece_frames, row_count, col_count, 2 * local_gated
    )
    expanded = jax.nn.silu(summed.astype(jnp.float32)).astype(jnp.bfloat16)
    padded_expanded = padded_2(expanded, (("row", 1),), 1)
    hidden = depthwise(padded_expanded, conv_taps, row_count, col_count, local_gated)
    hidden_flat = hidden.reshape(-1, local_gated)
    projected = jnp.dot(hidden_flat, out_weight, preferred_element_type=jnp.float32).astype(
        jnp.bfloat16
    )
    frame_blocks = jnp.split(projected, frame_parts, axis=0)
    ffn_rows = sum(
        piece.astype(jnp.float32) for piece in swap_chunks(frame_blocks, "frame")
    ).reshape(token_count, model_width)
    block_out = (stream_out.astype(jnp.float32) + ffn_rows).astype(jnp.bfloat16)
    grid_shape = (frame_count, row_count, col_count, model_width)
    return (stream_out.reshape(grid_shape), block_out.reshape(grid_shape))


def solution(mesh):
    in_specs = (
        P(("groups", "frame"), "row", None, None),
        P(("groups", "frame"), "row", None, None),
        P(("groups", "frame"), "row", None, None),
        P(("groups", "frame"), "row", None, None),
        P(),
        P(),
        P("row", None, "frame"),
        P(None, None, "frame"),
        P("frame", None),
    )
    out_specs = (
        P(("groups", "frame"), "row", None, None),
        P(("groups", "frame"), "row", None, None),
    )
    return jax.shard_map(local, mesh=mesh, in_specs=in_specs, out_specs=out_specs, check_vma=False)
```

```python
import jax
import jax.numpy as jnp
from jax import lax
from jax.sharding import PartitionSpec as P

HEADS = 20
HEAD_DIM = 112


NORM_EPS = 1e-06
SHARE_EPS = 1e-06


def padded_2(cells, sides, width):
    for axis, dim in sides:
        count = lax.axis_size(axis)
        ends = count - 1
        head = lax.slice_in_dim(cells, 0, width, axis=dim)
        tail = lax.slice_in_dim(cells, cells.shape[dim] - width, cells.shape[dim], axis=dim)
        cells = jnp.concatenate(
            [
                lax.ppermute(tail, axis, [(i, (i + 1) % count) for i in range(ends)]),
                cells,
                lax.ppermute(head, axis, [((i + 1) % count, i) for i in range(ends)]),
            ],
            axis=dim,
        )
    return cells


def exchange_steps(axes):
    steps = []
    for axis in axes:
        count = lax.axis_size(axis)
        bit = 1
        while bit < count:
            steps.append((axis, count, bit))
            bit *= 2
    return steps


def halving_sum(block, axes, inner_axis):
    steps = exchange_steps(axes)
    for axis, count, bit in steps:
        upper = (lax.axis_index(axis) & bit) != 0
        half = block.shape[1] // 2
        low, high = block[:, :half], block[:, half:]
        sent = jnp.where(upper, low, high)
        kept = jnp.where(upper, high, low)
        sent = sent.astype(jnp.bfloat16)
        block = kept + lax.ppermute(sent, axis, [(i, i ^ bit) for i in range(count)]).astype(
            jnp.float32
        )
    inner_count = lax.axis_size(inner_axis)
    pieces = [piece.astype(jnp.bfloat16) for piece in jnp.split(block, inner_count, axis=1)]
    mine = sum(piece.astype(jnp.float32) for piece in swap_chunks(pieces, inner_axis))
    shared = swap_chunks([mine.astype(jnp.bfloat16)] * inner_count, inner_axis)
    block = jnp.concatenate([piece.astype(jnp.float32) for piece in shared], axis=1)
    for axis, count, bit in reversed(steps):
        upper = (lax.axis_index(axis) & bit) != 0
        other = lax.ppermute(
            block.astype(jnp.bfloat16), axis, [(i, i ^ bit) for i in range(count)]
        ).astype(jnp.float32)
        block = jnp.where(
            upper, jnp.concatenate([other, block], 1), jnp.concatenate([block, other], 1)
        )
    return block


def pick(blocks, index):
    stacked = jnp.stack(blocks)
    return lax.dynamic_index_in_dim(stacked, index, axis=0, keepdims=False)


def swap_chunks(chunks, axis):
    count = lax.axis_size(axis)
    own = lax.axis_index(axis)
    by_mask = [pick(chunks, own)]
    for mask in range(1, count):
        sent = pick(chunks, own ^ mask)
        by_mask.append(lax.ppermute(sent, axis, [(i, i ^ mask) for i in range(count)]))
    return [pick(by_mask, own ^ source) for source in range(count)]


def doubling_gather(block, axis):
    count = lax.axis_size(axis)
    own = lax.axis_index(axis)
    by_mask = {0: block}
    bit = count // 2
    while bit >= 1:
        keys = sorted(by_mask)
        received = lax.ppermute(
            jnp.stack([by_mask[key] for key in keys]), axis, [(i, i ^ bit) for i in range(count)]
        )
        for at, key in enumerate(keys):
            by_mask[key ^ bit] = received[at]
        bit //= 2
    ordered = [by_mask[mask] for mask in range(count)]
    return [pick(ordered, own ^ source) for source in range(count)]


def line_reduce_scatter(blocks, axis):
    count = lax.axis_size(axis)
    own = lax.axis_index(axis)
    from_left = None
    from_right = None
    for step in range(1, count):
        rightward = pick(blocks, jnp.minimum(count - step + own, count - 1)).astype(jnp.float32)
        leftward = pick(blocks, jnp.maximum(own + step - count, 0)).astype(jnp.float32)
        if from_left is not None:
            rightward = rightward + from_left.astype(jnp.float32)
            leftward = leftward + from_right.astype(jnp.float32)
        from_left = lax.ppermute(
            rightward.astype(jnp.bfloat16), axis, [(p, p + 1) for p in range(step)]
        )
        from_right = lax.ppermute(
            leftward.astype(jnp.bfloat16), axis, [(p, p - 1) for p in range(count - step, count)]
        )
    mine = pick(blocks, own).astype(jnp.float32)
    if from_left is None:
        return mine
    return mine + from_left.astype(jnp.float32) + from_right.astype(jnp.float32)


def rms_norm(features):
    return features * lax.rsqrt(jnp.mean(features * features, axis=-1, keepdims=True) + NORM_EPS)


def depthwise(padded, conv_taps, row_count, col_count, half_width):
    widened = jnp.pad(padded, ((0, 0), (0, 0), (1, 1), (0, 0)))
    summed = jnp.zeros((padded.shape[0], row_count, col_count, padded.shape[3]), jnp.float32)
    for row_off in range(3):
        for col_off in range(3):
            window = widened[
                :, row_off : row_off + row_count, col_off : col_off + col_count, :
            ].astype(jnp.float32)
            summed = summed + window * conv_taps[row_off * 3 + col_off]
    return (summed[..., :half_width] * jax.nn.silu(summed[..., half_width:])).astype(jnp.bfloat16)


def local(
    query_in, key_in, value_in, stream_in, attn_gain, ffn_gain, in_weight, conv_weight, out_weight
):
    frame_count, row_count, col_count, model_width = query_in.shape
    token_count = frame_count * row_count * col_count
    local_gated = in_weight.shape[2]
    highest = lax.Precision.HIGHEST
    key_pos = jnp.maximum(key_in, 0).reshape(token_count, HEADS, HEAD_DIM)
    value_heads = value_in.reshape(token_count, HEADS, HEAD_DIM)
    local_state = jnp.einsum(
        "thi,thj->ihj", key_pos, value_heads, preferred_element_type=jnp.float32
    ).reshape(HEAD_DIM, model_width)
    local_total = jnp.sum(key_pos.reshape(token_count, model_width), axis=0, dtype=jnp.float32)
    stats = jnp.concatenate([local_state, local_total[None, :]], axis=0)
    parts = 1
    for axis, count, bit in exchange_steps(("frame", "row")):
        parts *= 2
    padded_width = -(-model_width // parts) * parts
    stats = jnp.pad(stats, ((0, 0), (0, padded_width - model_width)))
    stats = halving_sum(stats, ("frame",), inner_axis="row")[:, :model_width]
    kv_state, key_total = stats[:HEAD_DIM], stats[HEAD_DIM]
    query_pos = jnp.maximum(query_in, 0).reshape(token_count, HEADS, HEAD_DIM).astype(jnp.float32)
    numerator = jnp.einsum(
        "thi,ihj->thj", query_pos, kv_state.reshape(HEAD_DIM, HEADS, HEAD_DIM), precision=highest
    )
    denominator = jnp.einsum(
        "thi,hi->th", query_pos, key_total.reshape(HEADS, HEAD_DIM), precision=highest
    )
    attended = (numerator / (denominator[:, :, None] + SHARE_EPS)).reshape(token_count, model_width)
    stream_flat = stream_in.reshape(token_count, model_width).astype(jnp.float32)
    stream_out = (stream_flat + attn_gain.astype(jnp.float32) * rms_norm(attended)).astype(
        jnp.bfloat16
    )
    normed = (rms_norm(stream_out.astype(jnp.float32)) * ffn_gain.astype(jnp.float32)).astype(
        jnp.bfloat16
    )
    normed_grid = normed.reshape(frame_count, row_count, col_count, model_width)
    conv_taps = conv_weight.reshape(9, 2 * local_gated).astype(jnp.float32)
    row_parts = lax.axis_size("row")
    local_depth = in_weight.shape[0]
    depth_chunks = [
        normed_grid[..., part * local_depth : (part + 1) * local_depth] for part in range(row_parts)
    ]
    by_row = jnp.concatenate(swap_chunks(depth_chunks, "row"), axis=1)
    frame_parts = lax.axis_size("frame")
    by_frame = doubling_gather(by_row, "frame")
    whole_frames = frame_parts == row_parts and frame_count == 1 and row_count == 1
    weight_flat = in_weight.reshape(local_depth, 2 * local_gated)
    if whole_frames:
        tokens = jnp.stack([piece[0] for piece in by_frame])
        partial = jnp.dot(
            tokens.reshape(-1, local_depth), weight_flat, preferred_element_type=jnp.float32
        ).astype(jnp.bfloat16)
        summed = line_reduce_scatter(jnp.split(partial, row_parts, axis=0), "row")
        frame_rows = tokens.shape[1]
        expanded = (
            jax.nn.silu(summed.astype(jnp.float32))
            .astype(jnp.bfloat16)
            .reshape(1, frame_rows, col_count, 2 * local_gated)
        )
        padded_expanded = jnp.pad(expanded, ((0, 0), (1, 1), (0, 0), (0, 0)))
        hidden = depthwise(padded_expanded, conv_taps, frame_rows, col_count, local_gated)
        projected = jnp.dot(
            hidden.reshape(-1, local_gated), out_weight, preferred_element_type=jnp.float32
        ).astype(jnp.bfloat16)
        row_blocks = jnp.split(projected, frame_parts, axis=0)
        frame_at = lax.axis_index("frame")
        arrived = []
        for mask in range(row_parts):
            arrived.append(
                lax.ppermute(
                    pick(row_blocks, frame_at ^ mask),
                    ("frame", "row"),
                    [
                        (f * row_parts + r, r * row_parts + (f ^ mask))
                        for f in range(frame_parts)
                        for r in range(row_parts)
                    ],
                ).astype(jnp.float32)
            )
        ffn_rows = sum(arrived).reshape(token_count, model_width)
        block_out = (stream_out.astype(jnp.float32) + ffn_rows).astype(jnp.bfloat16)
        grid_shape = (frame_count, row_count, col_count, model_width)
        return (stream_out.reshape(grid_shape), block_out.reshape(grid_shape))
    tokens = jnp.stack([piece.transpose(1, 0, 2, 3) for piece in by_frame], axis=1)
    piece_frames = tokens.shape[1] * tokens.shape[2]
    partial = jnp.dot(
        tokens.reshape(-1, local_depth), weight_flat, preferred_element_type=jnp.float32
    ).astype(jnp.bfloat16)
    summed = lax.psum_scatter(partial, "row", scatter_dimension=0, tiled=True).reshape(
        piece_frames, row_count, col_count, 2 * local_gated
    )
    expanded = jax.nn.silu(summed.astype(jnp.float32)).astype(jnp.bfloat16)
    padded_expanded = padded_2(expanded, (("row", 1),), 1)
    hidden = depthwise(padded_expanded, conv_taps, row_count, col_count, local_gated)
    hidden_flat = hidden.reshape(-1, local_gated)
    projected = jnp.dot(hidden_flat, out_weight, preferred_element_type=jnp.float32).astype(
        jnp.bfloat16
    )
    frame_blocks = jnp.split(projected, frame_parts, axis=0)
    ffn_rows = sum(
        piece.astype(jnp.float32) for piece in swap_chunks(frame_blocks, "frame")
    ).reshape(token_count, model_width)
    block_out = (stream_out.astype(jnp.float32) + ffn_rows).astype(jnp.bfloat16)
    grid_shape = (frame_count, row_count, col_count, model_width)
    return (stream_out.reshape(grid_shape), block_out.reshape(grid_shape))


def solution(mesh):
    in_specs = (
        P(("groups", "frame"), "row", None, None),
        P(("groups", "frame"), "row", None, None),
        P(("groups", "frame"), "row", None, None),
        P(("groups", "frame"), "row", None, None),
        P(),
        P(),
        P("row", None, "frame"),
        P(None, None, "frame"),
        P("frame", None),
    )
    out_specs = (
        P(("groups", "frame"), "row", None, None),
        P(("groups", "frame"), "row", None, None),
    )
    return jax.shard_map(local, mesh=mesh, in_specs=in_specs, out_specs=out_specs, check_vma=False)
```

```python
import jax
import jax.numpy as jnp
from jax import lax
from jax.sharding import PartitionSpec as P

HEADS = 20
HEAD_DIM = 112


NORM_EPS = 1e-06
SHARE_EPS = 1e-06


def padded_2(cells, sides, width):
    for axis, dim in sides:
        count = lax.axis_size(axis)
        ends = count - 1
        head = lax.slice_in_dim(cells, 0, width, axis=dim)
        tail = lax.slice_in_dim(cells, cells.shape[dim] - width, cells.shape[dim], axis=dim)
        cells = jnp.concatenate(
            [
                lax.ppermute(tail, axis, [(i, (i + 1) % count) for i in range(ends)]),
                cells,
                lax.ppermute(head, axis, [((i + 1) % count, i) for i in range(ends)]),
            ],
            axis=dim,
        )
    return cells


def exchange_steps(axes):
    steps = []
    for axis in axes:
        count = lax.axis_size(axis)
        bit = 1
        while bit < count:
            steps.append((axis, count, bit))
            bit *= 2
    return steps


def halving_sum(block, axes, inner_axis):
    steps = exchange_steps(axes)
    for axis, count, bit in steps:
        upper = (lax.axis_index(axis) & bit) != 0
        half = block.shape[1] // 2
        low, high = block[:, :half], block[:, half:]
        sent = jnp.where(upper, low, high)
        kept = jnp.where(upper, high, low)
        sent = sent.astype(jnp.bfloat16)
        block = kept + lax.ppermute(sent, axis, [(i, i ^ bit) for i in range(count)]).astype(
            jnp.float32
        )
    inner_count = lax.axis_size(inner_axis)
    pieces = [piece.astype(jnp.bfloat16) for piece in jnp.split(block, inner_count, axis=1)]
    mine = sum(piece.astype(jnp.float32) for piece in swap_chunks(pieces, inner_axis))
    shared = swap_chunks([mine.astype(jnp.bfloat16)] * inner_count, inner_axis)
    block = jnp.concatenate([piece.astype(jnp.float32) for piece in shared], axis=1)
    for axis, count, bit in reversed(steps):
        upper = (lax.axis_index(axis) & bit) != 0
        other = lax.ppermute(
            block.astype(jnp.bfloat16), axis, [(i, i ^ bit) for i in range(count)]
        ).astype(jnp.float32)
        block = jnp.where(
            upper, jnp.concatenate([other, block], 1), jnp.concatenate([block, other], 1)
        )
    return block


def pick(blocks, index):
    stacked = jnp.stack(blocks)
    return lax.dynamic_index_in_dim(stacked, index, axis=0, keepdims=False)


def swap_chunks(chunks, axis):
    count = lax.axis_size(axis)
    own = lax.axis_index(axis)
    by_mask = [pick(chunks, own)]
    for mask in range(1, count):
        sent = pick(chunks, own ^ mask)
        by_mask.append(lax.ppermute(sent, axis, [(i, i ^ mask) for i in range(count)]))
    return [pick(by_mask, own ^ source) for source in range(count)]


def doubling_gather(block, axis):
    count = lax.axis_size(axis)
    own = lax.axis_index(axis)
    by_mask = {0: block}
    bit = count // 2
    while bit >= 1:
        keys = sorted(by_mask)
        received = lax.ppermute(
            jnp.stack([by_mask[key] for key in keys]), axis, [(i, i ^ bit) for i in range(count)]
        )
        for at, key in enumerate(keys):
            by_mask[key ^ bit] = received[at]
        bit //= 2
    ordered = [by_mask[mask] for mask in range(count)]
    return [pick(ordered, own ^ source) for source in range(count)]


def exchange_sum(block, axes):
    for axis in axes:
        count = lax.axis_size(axis)
        pieces = [piece.astype(jnp.bfloat16) for piece in jnp.split(block, count, axis=1)]
        block = sum(piece.astype(jnp.float32) for piece in swap_chunks(pieces, axis))
    block = block.astype(jnp.bfloat16)
    for axis in reversed(axes):
        count = lax.axis_size(axis)
        block = jnp.concatenate(swap_chunks([block] * count, axis), axis=1)
    return block.astype(jnp.float32)


def rms_norm(features):
    return features * lax.rsqrt(jnp.mean(features * features, axis=-1, keepdims=True) + NORM_EPS)


def depthwise(padded, conv_taps, row_count, col_count, half_width):
    widened = jnp.pad(padded, ((0, 0), (0, 0), (1, 1), (0, 0)))
    summed = jnp.zeros((padded.shape[0], row_count, col_count, padded.shape[3]), jnp.float32)
    for row_off in range(3):
        for col_off in range(3):
            window = widened[
                :, row_off : row_off + row_count, col_off : col_off + col_count, :
            ].astype(jnp.float32)
            summed = summed + window * conv_taps[row_off * 3 + col_off]
    return (summed[..., :half_width] * jax.nn.silu(summed[..., half_width:])).astype(jnp.bfloat16)


def local(
    query_in, key_in, value_in, stream_in, attn_gain, ffn_gain, in_weight, conv_weight, out_weight
):
    frame_count, row_count, col_count, model_width = query_in.shape
    token_count = frame_count * row_count * col_count
    local_gated = in_weight.shape[2]
    highest = lax.Precision.HIGHEST
    key_pos = jnp.maximum(key_in, 0).reshape(token_count, HEADS, HEAD_DIM)
    value_heads = value_in.reshape(token_count, HEADS, HEAD_DIM)
    local_state = jnp.einsum(
        "thi,thj->ihj", key_pos, value_heads, preferred_element_type=jnp.float32
    ).reshape(HEAD_DIM, model_width)
    local_total = jnp.sum(key_pos.reshape(token_count, model_width), axis=0, dtype=jnp.float32)
    stats = jnp.concatenate([local_state, local_total[None, :]], axis=0)
    parts = lax.axis_size("frame") * lax.axis_size("row")
    padded_width = -(-model_width // parts) * parts
    stats = jnp.pad(stats, ((0, 0), (0, padded_width - model_width)))
    stats = exchange_sum(stats, ("frame", "row"))[:, :model_width]
    kv_state, key_total = stats[:HEAD_DIM], stats[HEAD_DIM]
    query_pos = jnp.maximum(query_in, 0).reshape(token_count, HEADS, HEAD_DIM).astype(jnp.float32)
    numerator = jnp.einsum(
        "thi,ihj->thj", query_pos, kv_state.reshape(HEAD_DIM, HEADS, HEAD_DIM), precision=highest
    )
    denominator = jnp.einsum(
        "thi,hi->th", query_pos, key_total.reshape(HEADS, HEAD_DIM), precision=highest
    )
    attended = (numerator / (denominator[:, :, None] + SHARE_EPS)).reshape(token_count, model_width)
    stream_flat = stream_in.reshape(token_count, model_width).astype(jnp.float32)
    stream_out = (stream_flat + attn_gain.astype(jnp.float32) * rms_norm(attended)).astype(
        jnp.bfloat16
    )
    normed = (rms_norm(stream_out.astype(jnp.float32)) * ffn_gain.astype(jnp.float32)).astype(
        jnp.bfloat16
    )
    normed_grid = normed.reshape(frame_count, row_count, col_count, model_width)
    conv_taps = conv_weight.reshape(9, 2 * local_gated).astype(jnp.float32)
    row_parts = lax.axis_size("row")
    local_depth = in_weight.shape[0]
    depth_chunks = [
        normed_grid[..., part * local_depth : (part + 1) * local_depth] for part in range(row_parts)
    ]
    by_row = jnp.concatenate(swap_chunks(depth_chunks, "row"), axis=1)
    frame_parts = lax.axis_size("frame")
    by_frame = doubling_gather(by_row, "frame")
    whole_frames = frame_parts == row_parts and frame_count == 1 and row_count == 1
    weight_flat = in_weight.reshape(local_depth, 2 * local_gated)
    if whole_frames:
        tokens = jnp.stack([piece[0] for piece in by_frame])
        partial = jnp.dot(
            tokens.reshape(-1, local_depth), weight_flat, preferred_element_type=jnp.float32
        ).astype(jnp.bfloat16)
        summed = lax.psum_scatter(partial, "row", scatter_dimension=0, tiled=True)
        frame_rows = tokens.shape[1]
        expanded = (
            jax.nn.silu(summed.astype(jnp.float32))
            .astype(jnp.bfloat16)
            .reshape(1, frame_rows, col_count, 2 * local_gated)
        )
        padded_expanded = jnp.pad(expanded, ((0, 0), (1, 1), (0, 0), (0, 0)))
        hidden = depthwise(padded_expanded, conv_taps, frame_rows, col_count, local_gated)
        projected = jnp.dot(
            hidden.reshape(-1, local_gated), out_weight, preferred_element_type=jnp.float32
        ).astype(jnp.bfloat16)
        row_blocks = jnp.split(projected, frame_parts, axis=0)
        frame_at = lax.axis_index("frame")
        arrived = []
        for mask in range(row_parts):
            arrived.append(
                lax.ppermute(
                    pick(row_blocks, frame_at ^ mask),
                    ("frame", "row"),
                    [
                        (f * row_parts + r, r * row_parts + (f ^ mask))
                        for f in range(frame_parts)
                        for r in range(row_parts)
                    ],
                ).astype(jnp.float32)
            )
        ffn_rows = sum(arrived).reshape(token_count, model_width)
        block_out = (stream_out.astype(jnp.float32) + ffn_rows).astype(jnp.bfloat16)
        grid_shape = (frame_count, row_count, col_count, model_width)
        return (stream_out.reshape(grid_shape), block_out.reshape(grid_shape))
    tokens = jnp.stack([piece.transpose(1, 0, 2, 3) for piece in by_frame], axis=1)
    piece_frames = tokens.shape[1] * tokens.shape[2]
    partial = jnp.dot(
        tokens.reshape(-1, local_depth), weight_flat, preferred_element_type=jnp.float32
    ).astype(jnp.bfloat16)
    summed = lax.psum_scatter(partial, "row", scatter_dimension=0, tiled=True).reshape(
        piece_frames, row_count, col_count, 2 * local_gated
    )
    expanded = jax.nn.silu(summed.astype(jnp.float32)).astype(jnp.bfloat16)
    padded_expanded = padded_2(expanded, (("row", 1),), 1)
    hidden = depthwise(padded_expanded, conv_taps, row_count, col_count, local_gated)
    hidden_flat = hidden.reshape(-1, local_gated)
    projected = jnp.dot(hidden_flat, out_weight, preferred_element_type=jnp.float32).astype(
        jnp.bfloat16
    )
    frame_blocks = jnp.split(projected, frame_parts, axis=0)
    ffn_rows = sum(
        piece.astype(jnp.float32) for piece in swap_chunks(frame_blocks, "frame")
    ).reshape(token_count, model_width)
    block_out = (stream_out.astype(jnp.float32) + ffn_rows).astype(jnp.bfloat16)
    grid_shape = (frame_count, row_count, col_count, model_width)
    return (stream_out.reshape(grid_shape), block_out.reshape(grid_shape))


def solution(mesh):
    in_specs = (
        P(("groups", "frame"), "row", None, None),
        P(("groups", "frame"), "row", None, None),
        P(("groups", "frame"), "row", None, None),
        P(("groups", "frame"), "row", None, None),
        P(),
        P(),
        P("row", None, "frame"),
        P(None, None, "frame"),
        P("frame", None),
    )
    out_specs = (
        P(("groups", "frame"), "row", None, None),
        P(("groups", "frame"), "row", None, None),
    )
    return jax.shard_map(local, mesh=mesh, in_specs=in_specs, out_specs=out_specs, check_vma=False)
```

```python
import jax
import jax.numpy as jnp
from jax import lax
from jax.sharding import PartitionSpec as P

HEADS = 20
HEAD_DIM = 112


NORM_EPS = 1e-06
SHARE_EPS = 1e-06


def padded_2(cells, sides, width):
    for axis, dim in sides:
        count = lax.axis_size(axis)
        ends = count - 1
        head = lax.slice_in_dim(cells, 0, width, axis=dim)
        tail = lax.slice_in_dim(cells, cells.shape[dim] - width, cells.shape[dim], axis=dim)
        cells = jnp.concatenate(
            [
                lax.ppermute(tail, axis, [(i, (i + 1) % count) for i in range(ends)]),
                cells,
                lax.ppermute(head, axis, [((i + 1) % count, i) for i in range(ends)]),
            ],
            axis=dim,
        )
    return cells


def exchange_steps(axes):
    steps = []
    for axis in axes:
        count = lax.axis_size(axis)
        bit = 1
        while bit < count:
            steps.append((axis, count, bit))
            bit *= 2
    return steps


def halving_sum(block, axes, inner_axis):
    steps = exchange_steps(axes)
    for axis, count, bit in steps:
        upper = (lax.axis_index(axis) & bit) != 0
        half = block.shape[1] // 2
        low, high = block[:, :half], block[:, half:]
        sent = jnp.where(upper, low, high)
        kept = jnp.where(upper, high, low)
        sent = sent.astype(jnp.bfloat16)
        block = kept + lax.ppermute(sent, axis, [(i, i ^ bit) for i in range(count)]).astype(
            jnp.float32
        )
    inner_count = lax.axis_size(inner_axis)
    pieces = [piece.astype(jnp.bfloat16) for piece in jnp.split(block, inner_count, axis=1)]
    mine = sum(piece.astype(jnp.float32) for piece in swap_chunks(pieces, inner_axis))
    shared = swap_chunks([mine.astype(jnp.bfloat16)] * inner_count, inner_axis)
    block = jnp.concatenate([piece.astype(jnp.float32) for piece in shared], axis=1)
    for axis, count, bit in reversed(steps):
        upper = (lax.axis_index(axis) & bit) != 0
        other = lax.ppermute(
            block.astype(jnp.bfloat16), axis, [(i, i ^ bit) for i in range(count)]
        ).astype(jnp.float32)
        block = jnp.where(
            upper, jnp.concatenate([other, block], 1), jnp.concatenate([block, other], 1)
        )
    return block


def pick(blocks, index):
    stacked = jnp.stack(blocks)
    return lax.dynamic_index_in_dim(stacked, index, axis=0, keepdims=False)


def swap_chunks(chunks, axis):
    count = lax.axis_size(axis)
    own = lax.axis_index(axis)
    by_mask = [pick(chunks, own)]
    for mask in range(1, count):
        sent = pick(chunks, own ^ mask)
        by_mask.append(lax.ppermute(sent, axis, [(i, i ^ mask) for i in range(count)]))
    return [pick(by_mask, own ^ source) for source in range(count)]


def doubling_gather(block, axis):
    count = lax.axis_size(axis)
    own = lax.axis_index(axis)
    by_mask = {0: block}
    bit = count // 2
    while bit >= 1:
        keys = sorted(by_mask)
        received = lax.ppermute(
            jnp.stack([by_mask[key] for key in keys]), axis, [(i, i ^ bit) for i in range(count)]
        )
        for at, key in enumerate(keys):
            by_mask[key ^ bit] = received[at]
        bit //= 2
    ordered = [by_mask[mask] for mask in range(count)]
    return [pick(ordered, own ^ source) for source in range(count)]


def rms_norm(features):
    return features * lax.rsqrt(jnp.mean(features * features, axis=-1, keepdims=True) + NORM_EPS)


def depthwise(padded, conv_taps, row_count, col_count, half_width):
    widened = jnp.pad(padded, ((0, 0), (0, 0), (1, 1), (0, 0)))
    summed = jnp.zeros((padded.shape[0], row_count, col_count, padded.shape[3]), jnp.float32)
    for row_off in range(3):
        for col_off in range(3):
            window = widened[
                :, row_off : row_off + row_count, col_off : col_off + col_count, :
            ].astype(jnp.float32)
            summed = summed + window * conv_taps[row_off * 3 + col_off]
    return (summed[..., :half_width] * jax.nn.silu(summed[..., half_width:])).astype(jnp.bfloat16)


def local(
    query_in, key_in, value_in, stream_in, attn_gain, ffn_gain, in_weight, conv_weight, out_weight
):
    frame_count, row_count, col_count, model_width = query_in.shape
    token_count = frame_count * row_count * col_count
    local_gated = in_weight.shape[2]
    highest = lax.Precision.HIGHEST
    key_pos = jnp.maximum(key_in, 0).reshape(token_count, HEADS, HEAD_DIM)
    value_heads = value_in.reshape(token_count, HEADS, HEAD_DIM)
    local_state = jnp.einsum(
        "thi,thj->ihj", key_pos, value_heads, preferred_element_type=jnp.float32
    ).reshape(HEAD_DIM, model_width)
    local_total = jnp.sum(key_pos.reshape(token_count, model_width), axis=0, dtype=jnp.float32)
    stats = jnp.concatenate([local_state, local_total[None, :]], axis=0)
    parts = 1
    for axis, count, bit in exchange_steps(("frame", "row")):
        parts *= 2
    padded_width = -(-model_width // parts) * parts
    stats = jnp.pad(stats, ((0, 0), (0, padded_width - model_width)))
    stats = halving_sum(stats, ("frame",), inner_axis="row")[:, :model_width]
    kv_state, key_total = stats[:HEAD_DIM], stats[HEAD_DIM]
    query_pos = jnp.maximum(query_in, 0).reshape(token_count, HEADS, HEAD_DIM).astype(jnp.float32)
    numerator = jnp.einsum(
        "thi,ihj->thj", query_pos, kv_state.reshape(HEAD_DIM, HEADS, HEAD_DIM), precision=highest
    )
    denominator = jnp.einsum(
        "thi,hi->th", query_pos, key_total.reshape(HEADS, HEAD_DIM), precision=highest
    )
    attended = (numerator / (denominator[:, :, None] + SHARE_EPS)).reshape(token_count, model_width)
    stream_flat = stream_in.reshape(token_count, model_width).astype(jnp.float32)
    stream_out = (stream_flat + attn_gain.astype(jnp.float32) * rms_norm(attended)).astype(
        jnp.bfloat16
    )
    normed = (rms_norm(stream_out.astype(jnp.float32)) * ffn_gain.astype(jnp.float32)).astype(
        jnp.bfloat16
    )
    normed_grid = normed.reshape(frame_count, row_count, col_count, model_width)
    conv_taps = conv_weight.reshape(9, 2 * local_gated).astype(jnp.float32)
    row_parts = lax.axis_size("row")
    local_depth = in_weight.shape[0]
    depth_chunks = [
        normed_grid[..., part * local_depth : (part + 1) * local_depth] for part in range(row_parts)
    ]
    by_row = jnp.concatenate(swap_chunks(depth_chunks, "row"), axis=1)
    frame_parts = lax.axis_size("frame")
    by_frame = doubling_gather(by_row, "frame")
    whole_frames = (
        frame_parts == row_parts and frame_parts % 2 == 0 and frame_count == 1 and row_count == 1
    )
    weight_flat = in_weight.reshape(local_depth, 2 * local_gated)
    if whole_frames:
        tokens = jnp.stack([piece[0] for piece in by_frame])
        partial = jnp.dot(
            tokens.reshape(-1, local_depth), weight_flat, preferred_element_type=jnp.float32
        ).astype(jnp.bfloat16)
        summed = lax.psum_scatter(partial, "row", scatter_dimension=0, tiled=True)
        frame_rows = tokens.shape[1]
        expanded = (
            jax.nn.silu(summed.astype(jnp.float32))
            .astype(jnp.bfloat16)
            .reshape(1, frame_rows, col_count, 2 * local_gated)
        )
        padded_expanded = jnp.pad(expanded, ((0, 0), (1, 1), (0, 0), (0, 0)))
        hidden = depthwise(padded_expanded, conv_taps, frame_rows, col_count, local_gated)
        projected = jnp.dot(
            hidden.reshape(-1, local_gated), out_weight, preferred_element_type=jnp.float32
        ).astype(jnp.bfloat16)
        row_blocks = jnp.split(projected, row_parts, axis=0)
        frame_at = lax.axis_index("frame")
        core_at = frame_at % 2
        chip_at = frame_at // 2
        chips = frame_parts // 2
        core_pairs = [(i, i ^ 1) for i in range(frame_parts)]
        partner_rows = [pick(row_blocks, (1 - core_at) + 2 * chip) for chip in range(chips)]
        from_partner = lax.ppermute(jnp.stack(partner_rows), "frame", core_pairs)
        pair_sums = [
            (
                pick(row_blocks, core_at + 2 * chip).astype(jnp.float32)
                + from_partner[chip].astype(jnp.float32)
            ).astype(jnp.bfloat16)
            for chip in range(chips)
        ]
        arrived = []
        for mask in range(chips):
            arrived.append(
                lax.ppermute(
                    pick(pair_sums, chip_at ^ mask),
                    ("frame", "row"),
                    [
                        (f * row_parts + r, r * row_parts + (f % 2) + 2 * ((f // 2) ^ mask))
                        for f in range(frame_parts)
                        for r in range(row_parts)
                    ],
                ).astype(jnp.float32)
            )
        ffn_rows = sum(arrived).reshape(token_count, model_width)
        block_out = (stream_out.astype(jnp.float32) + ffn_rows).astype(jnp.bfloat16)
        grid_shape = (frame_count, row_count, col_count, model_width)
        return (stream_out.reshape(grid_shape), block_out.reshape(grid_shape))
    tokens = jnp.stack([piece.transpose(1, 0, 2, 3) for piece in by_frame], axis=1)
    piece_frames = tokens.shape[1] * tokens.shape[2]
    partial = jnp.dot(
        tokens.reshape(-1, local_depth), weight_flat, preferred_element_type=jnp.float32
    ).astype(jnp.bfloat16)
    summed = lax.psum_scatter(partial, "row", scatter_dimension=0, tiled=True).reshape(
        piece_frames, row_count, col_count, 2 * local_gated
    )
    expanded = jax.nn.silu(summed.astype(jnp.float32)).astype(jnp.bfloat16)
    padded_expanded = padded_2(expanded, (("row", 1),), 1)
    hidden = depthwise(padded_expanded, conv_taps, row_count, col_count, local_gated)
    hidden_flat = hidden.reshape(-1, local_gated)
    projected = jnp.dot(hidden_flat, out_weight, preferred_element_type=jnp.float32).astype(
        jnp.bfloat16
    )
    frame_blocks = jnp.split(projected, frame_parts, axis=0)
    ffn_rows = sum(
        piece.astype(jnp.float32) for piece in swap_chunks(frame_blocks, "frame")
    ).reshape(token_count, model_width)
    block_out = (stream_out.astype(jnp.float32) + ffn_rows).astype(jnp.bfloat16)
    grid_shape = (frame_count, row_count, col_count, model_width)
    return (stream_out.reshape(grid_shape), block_out.reshape(grid_shape))


def solution(mesh):
    in_specs = (
        P(("groups", "frame"), "row", None, None),
        P(("groups", "frame"), "row", None, None),
        P(("groups", "frame"), "row", None, None),
        P(("groups", "frame"), "row", None, None),
        P(),
        P(),
        P("row", None, "frame"),
        P(None, None, "frame"),
        P("frame", None),
    )
    out_specs = (
        P(("groups", "frame"), "row", None, None),
        P(("groups", "frame"), "row", None, None),
    )
    return jax.shard_map(local, mesh=mesh, in_specs=in_specs, out_specs=out_specs, check_vma=False)
```

```python
import jax
import jax.numpy as jnp
from jax import lax
from jax.sharding import PartitionSpec as P

HEADS = 20
HEAD_DIM = 112


NORM_EPS = 1e-06
SHARE_EPS = 1e-06


def padded_2(cells, sides, width):
    for axis, dim in sides:
        count = lax.axis_size(axis)
        ends = count - 1
        head = lax.slice_in_dim(cells, 0, width, axis=dim)
        tail = lax.slice_in_dim(cells, cells.shape[dim] - width, cells.shape[dim], axis=dim)
        cells = jnp.concatenate(
            [
                lax.ppermute(tail, axis, [(i, (i + 1) % count) for i in range(ends)]),
                cells,
                lax.ppermute(head, axis, [((i + 1) % count, i) for i in range(ends)]),
            ],
            axis=dim,
        )
    return cells


def exchange_steps(axes):
    steps = []
    for axis in axes:
        count = lax.axis_size(axis)
        bit = 1
        while bit < count:
            steps.append((axis, count, bit))
            bit *= 2
    return steps


def halving_sum(block, axes, inner_axis):
    steps = exchange_steps(axes)
    for axis, count, bit in steps:
        upper = (lax.axis_index(axis) & bit) != 0
        half = block.shape[1] // 2
        low, high = block[:, :half], block[:, half:]
        sent = jnp.where(upper, low, high)
        kept = jnp.where(upper, high, low)
        sent = sent.astype(jnp.bfloat16)
        block = kept + lax.ppermute(sent, axis, [(i, i ^ bit) for i in range(count)]).astype(
            jnp.float32
        )
    inner_count = lax.axis_size(inner_axis)
    pieces = [piece.astype(jnp.bfloat16) for piece in jnp.split(block, inner_count, axis=1)]
    mine = sum(piece.astype(jnp.float32) for piece in swap_chunks(pieces, inner_axis))
    shared = swap_chunks([mine.astype(jnp.bfloat16)] * inner_count, inner_axis)
    block = jnp.concatenate([piece.astype(jnp.float32) for piece in shared], axis=1)
    for axis, count, bit in reversed(steps):
        upper = (lax.axis_index(axis) & bit) != 0
        other = lax.ppermute(
            block.astype(jnp.bfloat16), axis, [(i, i ^ bit) for i in range(count)]
        ).astype(jnp.float32)
        block = jnp.where(
            upper, jnp.concatenate([other, block], 1), jnp.concatenate([block, other], 1)
        )
    return block


def pick(blocks, index):
    stacked = jnp.stack(blocks)
    return lax.dynamic_index_in_dim(stacked, index, axis=0, keepdims=False)


def swap_chunks(chunks, axis):
    count = lax.axis_size(axis)
    own = lax.axis_index(axis)
    by_mask = [pick(chunks, own)]
    for mask in range(1, count):
        sent = pick(chunks, own ^ mask)
        by_mask.append(lax.ppermute(sent, axis, [(i, i ^ mask) for i in range(count)]))
    return [pick(by_mask, own ^ source) for source in range(count)]


def doubling_gather(block, axis):
    count = lax.axis_size(axis)
    own = lax.axis_index(axis)
    by_mask = {0: block}
    bit = count // 2
    while bit >= 1:
        keys = sorted(by_mask)
        received = lax.ppermute(
            jnp.stack([by_mask[key] for key in keys]), axis, [(i, i ^ bit) for i in range(count)]
        )
        for at, key in enumerate(keys):
            by_mask[key ^ bit] = received[at]
        bit //= 2
    ordered = [by_mask[mask] for mask in range(count)]
    return [pick(ordered, own ^ source) for source in range(count)]


def rms_norm(features):
    return features * lax.rsqrt(jnp.mean(features * features, axis=-1, keepdims=True) + NORM_EPS)


def depthwise(padded, conv_taps, row_count, col_count, half_width):
    widened = jnp.pad(padded, ((0, 0), (0, 0), (1, 1), (0, 0)))
    summed = jnp.zeros((padded.shape[0], row_count, col_count, padded.shape[3]), jnp.float32)
    for row_off in range(3):
        for col_off in range(3):
            window = widened[
                :, row_off : row_off + row_count, col_off : col_off + col_count, :
            ].astype(jnp.float32)
            summed = summed + window * conv_taps[row_off * 3 + col_off]
    return (summed[..., :half_width] * jax.nn.silu(summed[..., half_width:])).astype(jnp.bfloat16)


def local(
    query_in, key_in, value_in, stream_in, attn_gain, ffn_gain, in_weight, conv_weight, out_weight
):
    frame_count, row_count, col_count, model_width = query_in.shape
    token_count = frame_count * row_count * col_count
    local_gated = in_weight.shape[2]
    highest = lax.Precision.HIGHEST
    key_pos = jnp.maximum(key_in, 0).reshape(token_count, HEADS, HEAD_DIM)
    value_heads = value_in.reshape(token_count, HEADS, HEAD_DIM)
    local_state = jnp.einsum(
        "thi,thj->ihj", key_pos, value_heads, preferred_element_type=jnp.float32
    ).reshape(HEAD_DIM, model_width)
    local_total = jnp.sum(key_pos.reshape(token_count, model_width), axis=0, dtype=jnp.float32)
    stats = jnp.concatenate([local_state, local_total[None, :]], axis=0)
    parts = 1
    for axis, count, bit in exchange_steps(("frame", "row")):
        parts *= 2
    padded_width = -(-model_width // parts) * parts
    stats = jnp.pad(stats, ((0, 0), (0, padded_width - model_width)))
    stats = halving_sum(stats, ("frame",), inner_axis="row")[:, :model_width]
    kv_state, key_total = stats[:HEAD_DIM], stats[HEAD_DIM]
    query_pos = jnp.maximum(query_in, 0).reshape(token_count, HEADS, HEAD_DIM).astype(jnp.float32)
    numerator = jnp.einsum(
        "thi,ihj->thj", query_pos, kv_state.reshape(HEAD_DIM, HEADS, HEAD_DIM), precision=highest
    )
    denominator = jnp.einsum(
        "thi,hi->th", query_pos, key_total.reshape(HEADS, HEAD_DIM), precision=highest
    )
    attended = (numerator / (denominator[:, :, None] + SHARE_EPS)).reshape(token_count, model_width)
    stream_flat = stream_in.reshape(token_count, model_width).astype(jnp.float32)
    stream_out = (stream_flat + attn_gain.astype(jnp.float32) * rms_norm(attended)).astype(
        jnp.bfloat16
    )
    normed = (rms_norm(stream_out.astype(jnp.float32)) * ffn_gain.astype(jnp.float32)).astype(
        jnp.bfloat16
    )
    normed_grid = normed.reshape(frame_count, row_count, col_count, model_width)
    conv_taps = conv_weight.reshape(9, 2 * local_gated).astype(jnp.float32)
    row_parts = lax.axis_size("row")
    local_depth = in_weight.shape[0]
    depth_chunks = [
        normed_grid[..., part * local_depth : (part + 1) * local_depth] for part in range(row_parts)
    ]
    by_row = jnp.concatenate(swap_chunks(depth_chunks, "row"), axis=1)
    frame_parts = lax.axis_size("frame")
    by_frame = doubling_gather(by_row, "frame")
    whole_frames = (
        frame_parts == row_parts and frame_parts % 2 == 0 and frame_count == 1 and row_count == 1
    )
    weight_flat = in_weight.reshape(local_depth, 2 * local_gated)
    if whole_frames:
        tokens = jnp.stack([piece[0] for piece in by_frame])
        partial = jnp.dot(
            tokens.reshape(-1, local_depth), weight_flat, preferred_element_type=jnp.float32
        ).astype(jnp.bfloat16)
        summed = lax.psum_scatter(partial, "row", scatter_dimension=0, tiled=True)
        frame_rows = tokens.shape[1]
        expanded = (
            jax.nn.silu(summed.astype(jnp.float32))
            .astype(jnp.bfloat16)
            .reshape(1, frame_rows, col_count, 2 * local_gated)
        )
        padded_expanded = jnp.pad(expanded, ((0, 0), (1, 1), (0, 0), (0, 0)))
        hidden = depthwise(padded_expanded, conv_taps, frame_rows, col_count, local_gated)
        projected = jnp.dot(
            hidden.reshape(-1, local_gated), out_weight, preferred_element_type=jnp.float32
        ).astype(jnp.bfloat16)
        frame_at = lax.axis_index("frame")
        core_at = frame_at % 2
        chip_at = frame_at // 2
        chips = frame_parts // 2
        core_pairs = [(i, i ^ 1) for i in range(frame_parts)]
        by_parity = projected.reshape(chips, 2, -1, model_width)
        partner_rows = lax.dynamic_index_in_dim(by_parity, 1 - core_at, axis=1, keepdims=False)
        own_rows = lax.dynamic_index_in_dim(by_parity, core_at, axis=1, keepdims=False)
        from_partner = lax.ppermute(partner_rows, "frame", core_pairs)
        pair_sums = (own_rows.astype(jnp.float32) + from_partner.astype(jnp.float32)).astype(
            jnp.bfloat16
        )
        pair_sums = [pair_sums[chip] for chip in range(chips)]
        arrived = []
        for mask in range(chips):
            arrived.append(
                lax.ppermute(
                    pick(pair_sums, chip_at ^ mask),
                    ("frame", "row"),
                    [
                        (f * row_parts + r, r * row_parts + (f % 2) + 2 * ((f // 2) ^ mask))
                        for f in range(frame_parts)
                        for r in range(row_parts)
                    ],
                ).astype(jnp.float32)
            )
        ffn_rows = sum(arrived).reshape(token_count, model_width)
        block_out = (stream_out.astype(jnp.float32) + ffn_rows).astype(jnp.bfloat16)
        grid_shape = (frame_count, row_count, col_count, model_width)
        return (stream_out.reshape(grid_shape), block_out.reshape(grid_shape))
    tokens = jnp.stack([piece.transpose(1, 0, 2, 3) for piece in by_frame], axis=1)
    piece_frames = tokens.shape[1] * tokens.shape[2]
    partial = jnp.dot(
        tokens.reshape(-1, local_depth), weight_flat, preferred_element_type=jnp.float32
    ).astype(jnp.bfloat16)
    summed = lax.psum_scatter(partial, "row", scatter_dimension=0, tiled=True).reshape(
        piece_frames, row_count, col_count, 2 * local_gated
    )
    expanded = jax.nn.silu(summed.astype(jnp.float32)).astype(jnp.bfloat16)
    padded_expanded = padded_2(expanded, (("row", 1),), 1)
    hidden = depthwise(padded_expanded, conv_taps, row_count, col_count, local_gated)
    hidden_flat = hidden.reshape(-1, local_gated)
    projected = jnp.dot(hidden_flat, out_weight, preferred_element_type=jnp.float32).astype(
        jnp.bfloat16
    )
    frame_blocks = jnp.split(projected, frame_parts, axis=0)
    ffn_rows = sum(
        piece.astype(jnp.float32) for piece in swap_chunks(frame_blocks, "frame")
    ).reshape(token_count, model_width)
    block_out = (stream_out.astype(jnp.float32) + ffn_rows).astype(jnp.bfloat16)
    grid_shape = (frame_count, row_count, col_count, model_width)
    return (stream_out.reshape(grid_shape), block_out.reshape(grid_shape))


def solution(mesh):
    in_specs = (
        P(("groups", "frame"), "row", None, None),
        P(("groups", "frame"), "row", None, None),
        P(("groups", "frame"), "row", None, None),
        P(("groups", "frame"), "row", None, None),
        P(),
        P(),
        P("row", None, "frame"),
        P(None, None, "frame"),
        P("frame", None),
    )
    out_specs = (
        P(("groups", "frame"), "row", None, None),
        P(("groups", "frame"), "row", None, None),
    )
    return jax.shard_map(local, mesh=mesh, in_specs=in_specs, out_specs=out_specs, check_vma=False)
```

```python
import jax
import jax.numpy as jnp
from jax import lax
from jax.sharding import PartitionSpec as P

HEADS = 20
HEAD_DIM = 112


NORM_EPS = 1e-06
SHARE_EPS = 1e-06


def padded_2(cells, sides, width):
    for axis, dim in sides:
        count = lax.axis_size(axis)
        ends = count - 1
        head = lax.slice_in_dim(cells, 0, width, axis=dim)
        tail = lax.slice_in_dim(cells, cells.shape[dim] - width, cells.shape[dim], axis=dim)
        cells = jnp.concatenate(
            [
                lax.ppermute(tail, axis, [(i, (i + 1) % count) for i in range(ends)]),
                cells,
                lax.ppermute(head, axis, [((i + 1) % count, i) for i in range(ends)]),
            ],
            axis=dim,
        )
    return cells


def exchange_steps(axes):
    steps = []
    for axis in axes:
        count = lax.axis_size(axis)
        bit = 1
        while bit < count:
            steps.append((axis, count, bit))
            bit *= 2
    return steps


def halving_sum(block, axes, inner_axis):
    steps = exchange_steps(axes)
    for axis, count, bit in steps:
        upper = (lax.axis_index(axis) & bit) != 0
        half = block.shape[1] // 2
        low, high = block[:, :half], block[:, half:]
        sent = jnp.where(upper, low, high)
        kept = jnp.where(upper, high, low)
        sent = sent.astype(jnp.bfloat16)
        block = kept + lax.ppermute(sent, axis, [(i, i ^ bit) for i in range(count)]).astype(
            jnp.float32
        )
    inner_count = lax.axis_size(inner_axis)
    pieces = [piece.astype(jnp.bfloat16) for piece in jnp.split(block, inner_count, axis=1)]
    mine = sum(piece.astype(jnp.float32) for piece in swap_chunks(pieces, inner_axis))
    shared = swap_chunks([mine.astype(jnp.bfloat16)] * inner_count, inner_axis)
    block = jnp.concatenate([piece.astype(jnp.float32) for piece in shared], axis=1)
    for axis, count, bit in reversed(steps):
        upper = (lax.axis_index(axis) & bit) != 0
        other = lax.ppermute(
            block.astype(jnp.bfloat16), axis, [(i, i ^ bit) for i in range(count)]
        ).astype(jnp.float32)
        block = jnp.where(
            upper, jnp.concatenate([other, block], 1), jnp.concatenate([block, other], 1)
        )
    return block


def pick(blocks, index):
    stacked = jnp.stack(blocks)
    return lax.dynamic_index_in_dim(stacked, index, axis=0, keepdims=False)


def swap_stacked(stacked, axis):
    count = lax.axis_size(axis)
    own = lax.axis_index(axis)
    by_mask = [lax.dynamic_index_in_dim(stacked, own, axis=0, keepdims=False)]
    for mask in range(1, count):
        sent = lax.dynamic_index_in_dim(stacked, own ^ mask, axis=0, keepdims=False)
        by_mask.append(lax.ppermute(sent, axis, [(i, i ^ mask) for i in range(count)]))
    return jnp.take(jnp.stack(by_mask), own ^ jnp.arange(count), axis=0)


def swap_chunks(chunks, axis):
    arrived = swap_stacked(jnp.stack(chunks), axis)
    return [arrived[source] for source in range(len(chunks))]


def doubling_gather(block, axis):
    count = lax.axis_size(axis)
    own = lax.axis_index(axis)
    by_mask = {0: block}
    bit = count // 2
    while bit >= 1:
        keys = sorted(by_mask)
        received = lax.ppermute(
            jnp.stack([by_mask[key] for key in keys]), axis, [(i, i ^ bit) for i in range(count)]
        )
        for at, key in enumerate(keys):
            by_mask[key ^ bit] = received[at]
        bit //= 2
    ordered = jnp.take(
        jnp.stack([by_mask[mask] for mask in range(count)]), own ^ jnp.arange(count), axis=0
    )
    return [ordered[source] for source in range(count)]


def rms_norm(features):
    return features * lax.rsqrt(jnp.mean(features * features, axis=-1, keepdims=True) + NORM_EPS)


def depthwise(padded, conv_taps, row_count, col_count, half_width):
    widened = jnp.pad(padded, ((0, 0), (0, 0), (1, 1), (0, 0)))
    summed = jnp.zeros((padded.shape[0], row_count, col_count, padded.shape[3]), jnp.float32)
    for row_off in range(3):
        for col_off in range(3):
            window = widened[
                :, row_off : row_off + row_count, col_off : col_off + col_count, :
            ].astype(jnp.float32)
            summed = summed + window * conv_taps[row_off * 3 + col_off]
    return (summed[..., :half_width] * jax.nn.silu(summed[..., half_width:])).astype(jnp.bfloat16)


def local(
    query_in, key_in, value_in, stream_in, attn_gain, ffn_gain, in_weight, conv_weight, out_weight
):
    frame_count, row_count, col_count, model_width = query_in.shape
    token_count = frame_count * row_count * col_count
    local_gated = in_weight.shape[2]
    highest = lax.Precision.HIGHEST
    key_pos = jnp.maximum(key_in, 0).reshape(token_count, HEADS, HEAD_DIM)
    value_heads = value_in.reshape(token_count, HEADS, HEAD_DIM)
    local_state = jnp.einsum(
        "thi,thj->ihj", key_pos, value_heads, preferred_element_type=jnp.float32
    ).reshape(HEAD_DIM, model_width)
    local_total = jnp.sum(key_pos.reshape(token_count, model_width), axis=0, dtype=jnp.float32)
    stats = jnp.concatenate([local_state, local_total[None, :]], axis=0)
    parts = 1
    for axis, count, bit in exchange_steps(("frame", "row")):
        parts *= 2
    padded_width = -(-model_width // parts) * parts
    stats = jnp.pad(stats, ((0, 0), (0, padded_width - model_width)))
    stats = halving_sum(stats, ("frame",), inner_axis="row")[:, :model_width]
    kv_state, key_total = stats[:HEAD_DIM], stats[HEAD_DIM]
    query_pos = jnp.maximum(query_in, 0).reshape(token_count, HEADS, HEAD_DIM).astype(jnp.float32)
    numerator = jnp.einsum(
        "thi,ihj->thj", query_pos, kv_state.reshape(HEAD_DIM, HEADS, HEAD_DIM), precision=highest
    )
    denominator = jnp.einsum(
        "thi,hi->th", query_pos, key_total.reshape(HEADS, HEAD_DIM), precision=highest
    )
    attended = (numerator / (denominator[:, :, None] + SHARE_EPS)).reshape(token_count, model_width)
    stream_flat = stream_in.reshape(token_count, model_width).astype(jnp.float32)
    stream_out = (stream_flat + attn_gain.astype(jnp.float32) * rms_norm(attended)).astype(
        jnp.bfloat16
    )
    normed = (rms_norm(stream_out.astype(jnp.float32)) * ffn_gain.astype(jnp.float32)).astype(
        jnp.bfloat16
    )
    normed_grid = normed.reshape(frame_count, row_count, col_count, model_width)
    conv_taps = conv_weight.reshape(9, 2 * local_gated).astype(jnp.float32)
    row_parts = lax.axis_size("row")
    local_depth = in_weight.shape[0]
    depth_split = jnp.moveaxis(
        normed_grid.reshape(frame_count, row_count, col_count, row_parts, local_depth), 3, 0
    )
    by_row = jnp.concatenate(list(swap_stacked(depth_split, "row")), axis=1)
    frame_parts = lax.axis_size("frame")
    by_frame = doubling_gather(by_row, "frame")
    whole_frames = (
        frame_parts == row_parts and frame_parts % 2 == 0 and frame_count == 1 and row_count == 1
    )
    weight_flat = in_weight.reshape(local_depth, 2 * local_gated)
    if whole_frames:
        tokens = jnp.stack([piece[0] for piece in by_frame])
        partial = jnp.dot(
            tokens.reshape(-1, local_depth), weight_flat, preferred_element_type=jnp.float32
        ).astype(jnp.bfloat16)
        summed = lax.psum_scatter(partial, "row", scatter_dimension=0, tiled=True)
        frame_rows = tokens.shape[1]
        expanded = (
            jax.nn.silu(summed.astype(jnp.float32))
            .astype(jnp.bfloat16)
            .reshape(1, frame_rows, col_count, 2 * local_gated)
        )
        padded_expanded = jnp.pad(expanded, ((0, 0), (1, 1), (0, 0), (0, 0)))
        hidden = depthwise(padded_expanded, conv_taps, frame_rows, col_count, local_gated)
        projected = jnp.dot(
            hidden.reshape(-1, local_gated), out_weight, preferred_element_type=jnp.float32
        ).astype(jnp.bfloat16)
        frame_at = lax.axis_index("frame")
        core_at = frame_at % 2
        chip_at = frame_at // 2
        chips = frame_parts // 2
        core_pairs = [(i, i ^ 1) for i in range(frame_parts)]
        by_parity = projected.reshape(chips, 2, -1, model_width)
        partner_rows = lax.dynamic_index_in_dim(by_parity, 1 - core_at, axis=1, keepdims=False)
        own_rows = lax.dynamic_index_in_dim(by_parity, core_at, axis=1, keepdims=False)
        from_partner = lax.ppermute(partner_rows, "frame", core_pairs)
        pair_sums = (own_rows.astype(jnp.float32) + from_partner.astype(jnp.float32)).astype(
            jnp.bfloat16
        )
        arrived = []
        for mask in range(chips):
            arrived.append(
                lax.ppermute(
                    lax.dynamic_index_in_dim(pair_sums, chip_at ^ mask, axis=0, keepdims=False),
                    ("frame", "row"),
                    [
                        (f * row_parts + r, r * row_parts + (f % 2) + 2 * ((f // 2) ^ mask))
                        for f in range(frame_parts)
                        for r in range(row_parts)
                    ],
                ).astype(jnp.float32)
            )
        ffn_rows = sum(arrived).reshape(token_count, model_width)
        block_out = (stream_out.astype(jnp.float32) + ffn_rows).astype(jnp.bfloat16)
        grid_shape = (frame_count, row_count, col_count, model_width)
        return (stream_out.reshape(grid_shape), block_out.reshape(grid_shape))
    tokens = jnp.stack([piece.transpose(1, 0, 2, 3) for piece in by_frame], axis=1)
    piece_frames = tokens.shape[1] * tokens.shape[2]
    partial = jnp.dot(
        tokens.reshape(-1, local_depth), weight_flat, preferred_element_type=jnp.float32
    ).astype(jnp.bfloat16)
    summed = lax.psum_scatter(partial, "row", scatter_dimension=0, tiled=True).reshape(
        piece_frames, row_count, col_count, 2 * local_gated
    )
    expanded = jax.nn.silu(summed.astype(jnp.float32)).astype(jnp.bfloat16)
    padded_expanded = padded_2(expanded, (("row", 1),), 1)
    hidden = depthwise(padded_expanded, conv_taps, row_count, col_count, local_gated)
    hidden_flat = hidden.reshape(-1, local_gated)
    projected = jnp.dot(hidden_flat, out_weight, preferred_element_type=jnp.float32).astype(
        jnp.bfloat16
    )
    frame_blocks = jnp.split(projected, frame_parts, axis=0)
    ffn_rows = sum(
        piece.astype(jnp.float32) for piece in swap_chunks(frame_blocks, "frame")
    ).reshape(token_count, model_width)
    block_out = (stream_out.astype(jnp.float32) + ffn_rows).astype(jnp.bfloat16)
    grid_shape = (frame_count, row_count, col_count, model_width)
    return (stream_out.reshape(grid_shape), block_out.reshape(grid_shape))


def solution(mesh):
    in_specs = (
        P(("groups", "frame"), "row", None, None),
        P(("groups", "frame"), "row", None, None),
        P(("groups", "frame"), "row", None, None),
        P(("groups", "frame"), "row", None, None),
        P(),
        P(),
        P("row", None, "frame"),
        P(None, None, "frame"),
        P("frame", None),
    )
    out_specs = (
        P(("groups", "frame"), "row", None, None),
        P(("groups", "frame"), "row", None, None),
    )
    return jax.shard_map(local, mesh=mesh, in_specs=in_specs, out_specs=out_specs, check_vma=False)
```

```python
import jax
import jax.numpy as jnp
from jax import lax
from jax.sharding import PartitionSpec as P

HEADS = 20
HEAD_DIM = 112


NORM_EPS = 1e-06
SHARE_EPS = 1e-06


def padded_2(cells, sides, width):
    for axis, dim in sides:
        count = lax.axis_size(axis)
        ends = count - 1
        head = lax.slice_in_dim(cells, 0, width, axis=dim)
        tail = lax.slice_in_dim(cells, cells.shape[dim] - width, cells.shape[dim], axis=dim)
        cells = jnp.concatenate(
            [
                lax.ppermute(tail, axis, [(i, (i + 1) % count) for i in range(ends)]),
                cells,
                lax.ppermute(head, axis, [((i + 1) % count, i) for i in range(ends)]),
            ],
            axis=dim,
        )
    return cells


def exchange_steps(axes):
    steps = []
    for axis in axes:
        count = lax.axis_size(axis)
        bit = 1
        while bit < count:
            steps.append((axis, count, bit))
            bit *= 2
    return steps


def halving_sum(block, axes, inner_axis):
    steps = exchange_steps(axes)
    for axis, count, bit in steps:
        upper = (lax.axis_index(axis) & bit) != 0
        half = block.shape[1] // 2
        low, high = block[:, :half], block[:, half:]
        sent = jnp.where(upper, low, high)
        kept = jnp.where(upper, high, low)
        sent = sent.astype(jnp.bfloat16)
        block = kept + lax.ppermute(sent, axis, [(i, i ^ bit) for i in range(count)]).astype(
            jnp.float32
        )
    inner_count = lax.axis_size(inner_axis)
    pieces = [piece.astype(jnp.bfloat16) for piece in jnp.split(block, inner_count, axis=1)]
    mine = sum(piece.astype(jnp.float32) for piece in swap_chunks(pieces, inner_axis))
    shared = swap_chunks([mine.astype(jnp.bfloat16)] * inner_count, inner_axis)
    block = jnp.concatenate([piece.astype(jnp.float32) for piece in shared], axis=1)
    for axis, count, bit in reversed(steps):
        upper = (lax.axis_index(axis) & bit) != 0
        other = lax.ppermute(
            block.astype(jnp.bfloat16), axis, [(i, i ^ bit) for i in range(count)]
        ).astype(jnp.float32)
        block = jnp.where(
            upper, jnp.concatenate([other, block], 1), jnp.concatenate([block, other], 1)
        )
    return block


def pick(blocks, index):
    stacked = jnp.stack(blocks)
    return lax.dynamic_index_in_dim(stacked, index, axis=0, keepdims=False)


def swap_chunks(chunks, axis):
    count = lax.axis_size(axis)
    own = lax.axis_index(axis)
    by_mask = [pick(chunks, own)]
    for mask in range(1, count):
        sent = pick(chunks, own ^ mask)
        by_mask.append(lax.ppermute(sent, axis, [(i, i ^ mask) for i in range(count)]))
    return [pick(by_mask, own ^ source) for source in range(count)]


def doubling_gather(block, axis, rider):
    count = lax.axis_size(axis)
    own = lax.axis_index(axis)
    by_mask = {0: block}
    bit = count // 2
    while bit >= 1:
        keys = sorted(by_mask)
        outgoing = jnp.stack([by_mask[key] for key in keys])
        if bit == 1:
            outgoing, rider = lax.optimization_barrier((outgoing, rider))
        received = lax.ppermute(outgoing, axis, [(i, i ^ bit) for i in range(count)])
        for at, key in enumerate(keys):
            by_mask[key ^ bit] = received[at]
        bit //= 2
    ordered = [by_mask[mask] for mask in range(count)]
    return [pick(ordered, own ^ source) for source in range(count)], rider


def rms_norm(features):
    return features * lax.rsqrt(jnp.mean(features * features, axis=-1, keepdims=True) + NORM_EPS)


def depthwise(padded, conv_taps, row_count, col_count, half_width):
    widened = jnp.pad(padded, ((0, 0), (0, 0), (1, 1), (0, 0)))
    summed = jnp.zeros((padded.shape[0], row_count, col_count, padded.shape[3]), jnp.float32)
    for row_off in range(3):
        for col_off in range(3):
            window = widened[
                :, row_off : row_off + row_count, col_off : col_off + col_count, :
            ].astype(jnp.float32)
            summed = summed + window * conv_taps[row_off * 3 + col_off]
    return (summed[..., :half_width] * jax.nn.silu(summed[..., half_width:])).astype(jnp.bfloat16)


def local(
    query_in, key_in, value_in, stream_in, attn_gain, ffn_gain, in_weight, conv_weight, out_weight
):
    frame_count, row_count, col_count, model_width = query_in.shape
    token_count = frame_count * row_count * col_count
    local_gated = in_weight.shape[2]
    highest = lax.Precision.HIGHEST
    key_pos = jnp.maximum(key_in, 0).reshape(token_count, HEADS, HEAD_DIM)
    value_heads = value_in.reshape(token_count, HEADS, HEAD_DIM)
    local_state = jnp.einsum(
        "thi,thj->ihj", key_pos, value_heads, preferred_element_type=jnp.float32
    ).reshape(HEAD_DIM, model_width)
    local_total = jnp.sum(key_pos.reshape(token_count, model_width), axis=0, dtype=jnp.float32)
    stats = jnp.concatenate([local_state, local_total[None, :]], axis=0)
    parts = 1
    for axis, count, bit in exchange_steps(("frame", "row")):
        parts *= 2
    padded_width = -(-model_width // parts) * parts
    stats = jnp.pad(stats, ((0, 0), (0, padded_width - model_width)))
    stats = halving_sum(stats, ("frame",), inner_axis="row")[:, :model_width]
    kv_state, key_total = stats[:HEAD_DIM], stats[HEAD_DIM]
    query_pos = jnp.maximum(query_in, 0).reshape(token_count, HEADS, HEAD_DIM).astype(jnp.float32)
    numerator = jnp.einsum(
        "thi,ihj->thj", query_pos, kv_state.reshape(HEAD_DIM, HEADS, HEAD_DIM), precision=highest
    )
    denominator = jnp.einsum(
        "thi,hi->th", query_pos, key_total.reshape(HEADS, HEAD_DIM), precision=highest
    )
    attended = (numerator / (denominator[:, :, None] + SHARE_EPS)).reshape(token_count, model_width)
    stream_flat = stream_in.reshape(token_count, model_width).astype(jnp.float32)
    stream_out = (stream_flat + attn_gain.astype(jnp.float32) * rms_norm(attended)).astype(
        jnp.bfloat16
    )
    normed = (rms_norm(stream_out.astype(jnp.float32)) * ffn_gain.astype(jnp.float32)).astype(
        jnp.bfloat16
    )
    normed_grid = normed.reshape(frame_count, row_count, col_count, model_width)
    conv_taps = conv_weight.reshape(9, 2 * local_gated).astype(jnp.float32)
    row_parts = lax.axis_size("row")
    local_depth = in_weight.shape[0]
    depth_chunks = [
        normed_grid[..., part * local_depth : (part + 1) * local_depth] for part in range(row_parts)
    ]
    by_row = jnp.concatenate(swap_chunks(depth_chunks, "row"), axis=1)
    frame_parts = lax.axis_size("frame")
    by_frame, weight_late = doubling_gather(by_row, "frame", in_weight)
    whole_frames = (
        frame_parts == row_parts and frame_parts % 2 == 0 and frame_count == 1 and row_count == 1
    )
    weight_flat = weight_late.reshape(local_depth, 2 * local_gated)
    if whole_frames:
        tokens = jnp.stack([piece[0] for piece in by_frame])
        partial = jnp.dot(
            tokens.reshape(-1, local_depth), weight_flat, preferred_element_type=jnp.float32
        ).astype(jnp.bfloat16)
        summed = lax.psum_scatter(partial, "row", scatter_dimension=0, tiled=True)
        frame_rows = tokens.shape[1]
        expanded = (
            jax.nn.silu(summed.astype(jnp.float32))
            .astype(jnp.bfloat16)
            .reshape(1, frame_rows, col_count, 2 * local_gated)
        )
        padded_expanded = jnp.pad(expanded, ((0, 0), (1, 1), (0, 0), (0, 0)))
        hidden = depthwise(padded_expanded, conv_taps, frame_rows, col_count, local_gated)
        projected = jnp.dot(
            hidden.reshape(-1, local_gated), out_weight, preferred_element_type=jnp.float32
        ).astype(jnp.bfloat16)
        frame_at = lax.axis_index("frame")
        core_at = frame_at % 2
        chip_at = frame_at // 2
        chips = frame_parts // 2
        core_pairs = [(i, i ^ 1) for i in range(frame_parts)]
        by_parity = projected.reshape(chips, 2, -1, model_width)
        partner_rows = lax.dynamic_index_in_dim(by_parity, 1 - core_at, axis=1, keepdims=False)
        own_rows = lax.dynamic_index_in_dim(by_parity, core_at, axis=1, keepdims=False)
        from_partner = lax.ppermute(partner_rows, "frame", core_pairs)
        pair_sums = (own_rows.astype(jnp.float32) + from_partner.astype(jnp.float32)).astype(
            jnp.bfloat16
        )
        pair_sums = [pair_sums[chip] for chip in range(chips)]
        arrived = []
        for mask in range(chips):
            arrived.append(
                lax.ppermute(
                    pick(pair_sums, chip_at ^ mask),
                    ("frame", "row"),
                    [
                        (f * row_parts + r, r * row_parts + (f % 2) + 2 * ((f // 2) ^ mask))
                        for f in range(frame_parts)
                        for r in range(row_parts)
                    ],
                ).astype(jnp.float32)
            )
        ffn_rows = sum(arrived).reshape(token_count, model_width)
        block_out = (stream_out.astype(jnp.float32) + ffn_rows).astype(jnp.bfloat16)
        grid_shape = (frame_count, row_count, col_count, model_width)
        return (stream_out.reshape(grid_shape), block_out.reshape(grid_shape))
    tokens = jnp.stack([piece.transpose(1, 0, 2, 3) for piece in by_frame], axis=1)
    piece_frames = tokens.shape[1] * tokens.shape[2]
    partial = jnp.dot(
        tokens.reshape(-1, local_depth), weight_flat, preferred_element_type=jnp.float32
    ).astype(jnp.bfloat16)
    summed = lax.psum_scatter(partial, "row", scatter_dimension=0, tiled=True).reshape(
        piece_frames, row_count, col_count, 2 * local_gated
    )
    expanded = jax.nn.silu(summed.astype(jnp.float32)).astype(jnp.bfloat16)
    padded_expanded = padded_2(expanded, (("row", 1),), 1)
    hidden = depthwise(padded_expanded, conv_taps, row_count, col_count, local_gated)
    hidden_flat = hidden.reshape(-1, local_gated)
    projected = jnp.dot(hidden_flat, out_weight, preferred_element_type=jnp.float32).astype(
        jnp.bfloat16
    )
    frame_blocks = jnp.split(projected, frame_parts, axis=0)
    ffn_rows = sum(
        piece.astype(jnp.float32) for piece in swap_chunks(frame_blocks, "frame")
    ).reshape(token_count, model_width)
    block_out = (stream_out.astype(jnp.float32) + ffn_rows).astype(jnp.bfloat16)
    grid_shape = (frame_count, row_count, col_count, model_width)
    return (stream_out.reshape(grid_shape), block_out.reshape(grid_shape))


def solution(mesh):
    in_specs = (
        P(("groups", "frame"), "row", None, None),
        P(("groups", "frame"), "row", None, None),
        P(("groups", "frame"), "row", None, None),
        P(("groups", "frame"), "row", None, None),
        P(),
        P(),
        P("row", None, "frame"),
        P(None, None, "frame"),
        P("frame", None),
    )
    out_specs = (
        P(("groups", "frame"), "row", None, None),
        P(("groups", "frame"), "row", None, None),
    )
    return jax.shard_map(local, mesh=mesh, in_specs=in_specs, out_specs=out_specs, check_vma=False)
```

```python
import jax
import jax.numpy as jnp
from jax import lax
from jax.sharding import PartitionSpec as P

HEADS = 20
HEAD_DIM = 112


NORM_EPS = 1e-06
SHARE_EPS = 1e-06


def padded_2(cells, sides, width):
    for axis, dim in sides:
        count = lax.axis_size(axis)
        ends = count - 1
        head = lax.slice_in_dim(cells, 0, width, axis=dim)
        tail = lax.slice_in_dim(cells, cells.shape[dim] - width, cells.shape[dim], axis=dim)
        cells = jnp.concatenate(
            [
                lax.ppermute(tail, axis, [(i, (i + 1) % count) for i in range(ends)]),
                cells,
                lax.ppermute(head, axis, [((i + 1) % count, i) for i in range(ends)]),
            ],
            axis=dim,
        )
    return cells


def exchange_steps(axes):
    steps = []
    for axis in axes:
        count = lax.axis_size(axis)
        bit = 1
        while bit < count:
            steps.append((axis, count, bit))
            bit *= 2
    return steps


def halving_sum(block, axes, inner_axis):
    steps = exchange_steps(axes)
    for axis, count, bit in steps:
        upper = (lax.axis_index(axis) & bit) != 0
        half = block.shape[1] // 2
        low, high = block[:, :half], block[:, half:]
        sent = jnp.where(upper, low, high)
        kept = jnp.where(upper, high, low)
        sent = sent.astype(jnp.bfloat16)
        block = kept + lax.ppermute(sent, axis, [(i, i ^ bit) for i in range(count)]).astype(
            jnp.float32
        )
    inner_count = lax.axis_size(inner_axis)
    pieces = [piece.astype(jnp.bfloat16) for piece in jnp.split(block, inner_count, axis=1)]
    mine = sum(piece.astype(jnp.float32) for piece in swap_chunks(pieces, inner_axis))
    shared = swap_chunks([mine.astype(jnp.bfloat16)] * inner_count, inner_axis)
    block = jnp.concatenate([piece.astype(jnp.float32) for piece in shared], axis=1)
    for axis, count, bit in reversed(steps):
        upper = (lax.axis_index(axis) & bit) != 0
        other = lax.ppermute(
            block.astype(jnp.bfloat16), axis, [(i, i ^ bit) for i in range(count)]
        ).astype(jnp.float32)
        block = jnp.where(
            upper, jnp.concatenate([other, block], 1), jnp.concatenate([block, other], 1)
        )
    return block


def pick(blocks, index):
    stacked = jnp.stack(blocks)
    return lax.dynamic_index_in_dim(stacked, index, axis=0, keepdims=False)


def swap_chunks(chunks, axis):
    count = lax.axis_size(axis)
    own = lax.axis_index(axis)
    by_mask = [pick(chunks, own)]
    for mask in range(1, count):
        sent = pick(chunks, own ^ mask)
        by_mask.append(lax.ppermute(sent, axis, [(i, i ^ mask) for i in range(count)]))
    return [pick(by_mask, own ^ source) for source in range(count)]


def doubling_gather(block, axis):
    count = lax.axis_size(axis)
    own = lax.axis_index(axis)
    by_mask = {0: block}
    bit = count // 2
    while bit >= 1:
        keys = sorted(by_mask)
        received = lax.ppermute(
            jnp.stack([by_mask[key] for key in keys]), axis, [(i, i ^ bit) for i in range(count)]
        )
        for at, key in enumerate(keys):
            by_mask[key ^ bit] = received[at]
        bit //= 2
    ordered = [by_mask[mask] for mask in range(count)]
    return [pick(ordered, own ^ source) for source in range(count)]


def rms_norm(features):
    return features * lax.rsqrt(jnp.mean(features * features, axis=-1, keepdims=True) + NORM_EPS)


def depthwise(padded, conv_taps, row_count, col_count, half_width):
    widened = jnp.pad(padded, ((0, 0), (0, 0), (1, 1), (0, 0)))
    summed = jnp.zeros((padded.shape[0], row_count, col_count, padded.shape[3]), jnp.float32)
    for row_off in range(3):
        for col_off in range(3):
            window = widened[
                :, row_off : row_off + row_count, col_off : col_off + col_count, :
            ].astype(jnp.float32)
            summed = summed + window * conv_taps[row_off * 3 + col_off]
    return (summed[..., :half_width] * jax.nn.silu(summed[..., half_width:])).astype(jnp.bfloat16)


def local(
    query_in, key_in, value_in, stream_in, attn_gain, ffn_gain, in_weight, conv_weight, out_weight
):
    frame_count, row_count, col_count, model_width = query_in.shape
    token_count = frame_count * row_count * col_count
    local_gated = in_weight.shape[2]
    highest = lax.Precision.HIGHEST
    key_pos = jnp.maximum(key_in, 0).reshape(token_count, HEADS, HEAD_DIM)
    value_heads = value_in.reshape(token_count, HEADS, HEAD_DIM)
    local_state = jnp.einsum(
        "thi,thj->ihj", key_pos, value_heads, preferred_element_type=jnp.float32
    ).reshape(HEAD_DIM, model_width)
    local_total = jnp.sum(key_pos.reshape(token_count, model_width), axis=0, dtype=jnp.float32)
    stats = jnp.concatenate([local_state, local_total[None, :]], axis=0)
    parts = 1
    for axis, count, bit in exchange_steps(("frame", "row")):
        parts *= 2
    padded_width = -(-model_width // parts) * parts
    stat_rows = -(-stats.shape[0] // 16) * 16
    stats = jnp.pad(stats, ((0, stat_rows - stats.shape[0]), (0, padded_width - model_width)))
    stats = halving_sum(stats, ("frame",), inner_axis="row")[:, :model_width]
    kv_state, key_total = stats[:HEAD_DIM], stats[HEAD_DIM]
    query_pos = jnp.maximum(query_in, 0).reshape(token_count, HEADS, HEAD_DIM).astype(jnp.float32)
    numerator = jnp.einsum(
        "thi,ihj->thj", query_pos, kv_state.reshape(HEAD_DIM, HEADS, HEAD_DIM), precision=highest
    )
    denominator = jnp.einsum(
        "thi,hi->th", query_pos, key_total.reshape(HEADS, HEAD_DIM), precision=highest
    )
    attended = (numerator / (denominator[:, :, None] + SHARE_EPS)).reshape(token_count, model_width)
    stream_flat = stream_in.reshape(token_count, model_width).astype(jnp.float32)
    stream_out = (stream_flat + attn_gain.astype(jnp.float32) * rms_norm(attended)).astype(
        jnp.bfloat16
    )
    normed = (rms_norm(stream_out.astype(jnp.float32)) * ffn_gain.astype(jnp.float32)).astype(
        jnp.bfloat16
    )
    normed_grid = normed.reshape(frame_count, row_count, col_count, model_width)
    conv_taps = conv_weight.reshape(9, 2 * local_gated).astype(jnp.float32)
    row_parts = lax.axis_size("row")
    local_depth = in_weight.shape[0]
    depth_chunks = [
        normed_grid[..., part * local_depth : (part + 1) * local_depth] for part in range(row_parts)
    ]
    by_row = jnp.concatenate(swap_chunks(depth_chunks, "row"), axis=1)
    frame_parts = lax.axis_size("frame")
    by_frame = doubling_gather(by_row, "frame")
    whole_frames = (
        frame_parts == row_parts and frame_parts % 2 == 0 and frame_count == 1 and row_count == 1
    )
    weight_flat = in_weight.reshape(local_depth, 2 * local_gated)
    if whole_frames:
        tokens = jnp.stack([piece[0] for piece in by_frame])
        partial = jnp.dot(
            tokens.reshape(-1, local_depth), weight_flat, preferred_element_type=jnp.float32
        ).astype(jnp.bfloat16)
        summed = lax.psum_scatter(partial, "row", scatter_dimension=0, tiled=True)
        frame_rows = tokens.shape[1]
        expanded = (
            jax.nn.silu(summed.astype(jnp.float32))
            .astype(jnp.bfloat16)
            .reshape(1, frame_rows, col_count, 2 * local_gated)
        )
        padded_expanded = jnp.pad(expanded, ((0, 0), (1, 1), (0, 0), (0, 0)))
        hidden = depthwise(padded_expanded, conv_taps, frame_rows, col_count, local_gated)
        projected = jnp.dot(
            hidden.reshape(-1, local_gated), out_weight, preferred_element_type=jnp.float32
        ).astype(jnp.bfloat16)
        frame_at = lax.axis_index("frame")
        core_at = frame_at % 2
        chip_at = frame_at // 2
        chips = frame_parts // 2
        core_pairs = [(i, i ^ 1) for i in range(frame_parts)]
        by_parity = projected.reshape(chips, 2, -1, model_width)
        partner_rows = lax.dynamic_index_in_dim(by_parity, 1 - core_at, axis=1, keepdims=False)
        own_rows = lax.dynamic_index_in_dim(by_parity, core_at, axis=1, keepdims=False)
        from_partner = lax.ppermute(partner_rows, "frame", core_pairs)
        pair_sums = (own_rows.astype(jnp.float32) + from_partner.astype(jnp.float32)).astype(
            jnp.bfloat16
        )
        pair_sums = [pair_sums[chip] for chip in range(chips)]
        arrived = []
        for mask in range(chips):
            arrived.append(
                lax.ppermute(
                    pick(pair_sums, chip_at ^ mask),
                    ("frame", "row"),
                    [
                        (f * row_parts + r, r * row_parts + (f % 2) + 2 * ((f // 2) ^ mask))
                        for f in range(frame_parts)
                        for r in range(row_parts)
                    ],
                ).astype(jnp.float32)
            )
        ffn_rows = sum(arrived).reshape(token_count, model_width)
        block_out = (stream_out.astype(jnp.float32) + ffn_rows).astype(jnp.bfloat16)
        grid_shape = (frame_count, row_count, col_count, model_width)
        return (stream_out.reshape(grid_shape), block_out.reshape(grid_shape))
    tokens = jnp.stack([piece.transpose(1, 0, 2, 3) for piece in by_frame], axis=1)
    piece_frames = tokens.shape[1] * tokens.shape[2]
    partial = jnp.dot(
        tokens.reshape(-1, local_depth), weight_flat, preferred_element_type=jnp.float32
    ).astype(jnp.bfloat16)
    summed = lax.psum_scatter(partial, "row", scatter_dimension=0, tiled=True).reshape(
        piece_frames, row_count, col_count, 2 * local_gated
    )
    expanded = jax.nn.silu(summed.astype(jnp.float32)).astype(jnp.bfloat16)
    padded_expanded = padded_2(expanded, (("row", 1),), 1)
    hidden = depthwise(padded_expanded, conv_taps, row_count, col_count, local_gated)
    hidden_flat = hidden.reshape(-1, local_gated)
    projected = jnp.dot(hidden_flat, out_weight, preferred_element_type=jnp.float32).astype(
        jnp.bfloat16
    )
    frame_blocks = jnp.split(projected, frame_parts, axis=0)
    ffn_rows = sum(
        piece.astype(jnp.float32) for piece in swap_chunks(frame_blocks, "frame")
    ).reshape(token_count, model_width)
    block_out = (stream_out.astype(jnp.float32) + ffn_rows).astype(jnp.bfloat16)
    grid_shape = (frame_count, row_count, col_count, model_width)
    return (stream_out.reshape(grid_shape), block_out.reshape(grid_shape))


def solution(mesh):
    in_specs = (
        P(("groups", "frame"), "row", None, None),
        P(("groups", "frame"), "row", None, None),
        P(("groups", "frame"), "row", None, None),
        P(("groups", "frame"), "row", None, None),
        P(),
        P(),
        P("row", None, "frame"),
        P(None, None, "frame"),
        P("frame", None),
    )
    out_specs = (
        P(("groups", "frame"), "row", None, None),
        P(("groups", "frame"), "row", None, None),
    )
    return jax.shard_map(local, mesh=mesh, in_specs=in_specs, out_specs=out_specs, check_vma=False)
```

```python
import jax
import jax.numpy as jnp
from jax import lax
from jax.sharding import PartitionSpec as P

HEADS = 20
HEAD_DIM = 112


NORM_EPS = 1e-06
SHARE_EPS = 1e-06


def padded_2(cells, sides, width):
    for axis, dim in sides:
        count = lax.axis_size(axis)
        ends = count - 1
        head = lax.slice_in_dim(cells, 0, width, axis=dim)
        tail = lax.slice_in_dim(cells, cells.shape[dim] - width, cells.shape[dim], axis=dim)
        cells = jnp.concatenate(
            [
                lax.ppermute(tail, axis, [(i, (i + 1) % count) for i in range(ends)]),
                cells,
                lax.ppermute(head, axis, [((i + 1) % count, i) for i in range(ends)]),
            ],
            axis=dim,
        )
    return cells


def exchange_steps(axes):
    steps = []
    for axis in axes:
        count = lax.axis_size(axis)
        bit = 1
        while bit < count:
            steps.append((axis, count, bit))
            bit *= 2
    return steps


def halving_sum(block, axes, inner_axis):
    steps = exchange_steps(axes)
    for axis, count, bit in steps:
        upper = (lax.axis_index(axis) & bit) != 0
        half = block.shape[1] // 2
        low, high = block[:, :half], block[:, half:]
        sent = jnp.where(upper, low, high)
        kept = jnp.where(upper, high, low)
        sent = sent.astype(jnp.bfloat16)
        block = kept + lax.ppermute(sent, axis, [(i, i ^ bit) for i in range(count)]).astype(
            jnp.float32
        )
    inner_count = lax.axis_size(inner_axis)
    pieces = [piece.astype(jnp.bfloat16) for piece in jnp.split(block, inner_count, axis=1)]
    mine = sum(piece.astype(jnp.float32) for piece in swap_chunks(pieces, inner_axis))
    shared = swap_chunks([mine.astype(jnp.bfloat16)] * inner_count, inner_axis)
    block = jnp.concatenate([piece.astype(jnp.float32) for piece in shared], axis=1)
    for axis, count, bit in reversed(steps):
        upper = (lax.axis_index(axis) & bit) != 0
        other = lax.ppermute(
            block.astype(jnp.bfloat16), axis, [(i, i ^ bit) for i in range(count)]
        ).astype(jnp.float32)
        block = jnp.where(
            upper, jnp.concatenate([other, block], 1), jnp.concatenate([block, other], 1)
        )
    return block


def pick(blocks, index):
    stacked = jnp.stack(blocks)
    return lax.dynamic_index_in_dim(stacked, index, axis=0, keepdims=False)


def swap_chunks(chunks, axis):
    count = lax.axis_size(axis)
    own = lax.axis_index(axis)
    by_mask = [pick(chunks, own)]
    for mask in range(1, count):
        sent = pick(chunks, own ^ mask)
        by_mask.append(lax.ppermute(sent, axis, [(i, i ^ mask) for i in range(count)]))
    return [pick(by_mask, own ^ source) for source in range(count)]


def doubling_gather(block, axis):
    count = lax.axis_size(axis)
    own = lax.axis_index(axis)
    by_mask = {0: block}
    bit = count // 2
    while bit >= 1:
        keys = sorted(by_mask)
        received = lax.ppermute(
            jnp.stack([by_mask[key] for key in keys]), axis, [(i, i ^ bit) for i in range(count)]
        )
        for at, key in enumerate(keys):
            by_mask[key ^ bit] = received[at]
        bit //= 2
    ordered = [by_mask[mask] for mask in range(count)]
    return [pick(ordered, own ^ source) for source in range(count)]


def rms_norm(features):
    return features * lax.rsqrt(jnp.mean(features * features, axis=-1, keepdims=True) + NORM_EPS)


def depthwise(padded, conv_taps, row_count, col_count, half_width):
    widened = jnp.pad(padded, ((0, 0), (0, 0), (1, 1), (0, 0)))
    summed = jnp.zeros((padded.shape[0], row_count, col_count, padded.shape[3]), jnp.float32)
    for row_off in range(3):
        for col_off in range(3):
            window = widened[
                :, row_off : row_off + row_count, col_off : col_off + col_count, :
            ].astype(jnp.float32)
            summed = summed + window * conv_taps[row_off * 3 + col_off]
    return (summed[..., :half_width] * jax.nn.silu(summed[..., half_width:])).astype(jnp.bfloat16)


def local(
    query_in, key_in, value_in, stream_in, attn_gain, ffn_gain, in_weight, conv_weight, out_weight
):
    frame_count, row_count, col_count, model_width = query_in.shape
    token_count = frame_count * row_count * col_count
    local_gated = in_weight.shape[2]
    highest = lax.Precision.HIGHEST
    key_pos = jnp.maximum(key_in, 0).reshape(token_count, HEADS, HEAD_DIM)
    value_heads = value_in.reshape(token_count, HEADS, HEAD_DIM)
    local_state = jnp.einsum(
        "thi,thj->ihj", key_pos, value_heads, preferred_element_type=jnp.float32
    ).reshape(HEAD_DIM, model_width)
    local_total = jnp.sum(key_pos.reshape(token_count, model_width), axis=0, dtype=jnp.float32)
    stats = jnp.concatenate([local_state, local_total[None, :]], axis=0)
    parts = 1
    for axis, count, bit in exchange_steps(("frame", "row")):
        parts *= 2
    padded_width = -(-model_width // parts) * parts
    stat_rows = -(-stats.shape[0] // 16) * 16
    stats = jnp.pad(stats, ((0, stat_rows - stats.shape[0]), (0, padded_width - model_width)))
    stats = halving_sum(stats, ("frame",), inner_axis="row")[:, :model_width]
    kv_state, key_total = stats[:HEAD_DIM], stats[HEAD_DIM]
    query_pos = jnp.maximum(query_in, 0).reshape(token_count, HEADS, HEAD_DIM).astype(jnp.float32)
    numerator = jnp.einsum(
        "thi,ihj->thj", query_pos, kv_state.reshape(HEAD_DIM, HEADS, HEAD_DIM), precision=highest
    )
    denominator = jnp.einsum(
        "thi,hi->th", query_pos, key_total.reshape(HEADS, HEAD_DIM), precision=highest
    )
    attended = (numerator / (denominator[:, :, None] + SHARE_EPS)).reshape(token_count, model_width)
    stream_flat = stream_in.reshape(token_count, model_width).astype(jnp.float32)
    stream_out = (stream_flat + attn_gain.astype(jnp.float32) * rms_norm(attended)).astype(
        jnp.bfloat16
    )
    normed = (rms_norm(stream_out.astype(jnp.float32)) * ffn_gain.astype(jnp.float32)).astype(
        jnp.bfloat16
    )
    normed_grid = normed.reshape(frame_count, row_count, col_count, model_width)
    conv_taps = conv_weight.reshape(9, 2 * local_gated).astype(jnp.float32)
    row_parts = lax.axis_size("row")
    local_depth = in_weight.shape[0]
    lane_depth = -(-local_depth // 128) * 128
    depth_chunks = [
        jnp.pad(
            normed_grid[..., part * local_depth : (part + 1) * local_depth],
            ((0, 0), (0, 0), (0, 0), (0, lane_depth - local_depth)),
        )
        for part in range(row_parts)
    ]
    by_row = jnp.concatenate(swap_chunks(depth_chunks, "row"), axis=1)
    frame_parts = lax.axis_size("frame")
    by_frame = doubling_gather(by_row, "frame")
    whole_frames = (
        frame_parts == row_parts and frame_parts % 2 == 0 and frame_count == 1 and row_count == 1
    )
    weight_flat = jnp.pad(
        in_weight.reshape(local_depth, 2 * local_gated), ((0, lane_depth - local_depth), (0, 0))
    )
    if whole_frames:
        tokens = jnp.stack([piece[0] for piece in by_frame])
        partial = jnp.dot(
            tokens.reshape(-1, lane_depth), weight_flat, preferred_element_type=jnp.float32
        ).astype(jnp.bfloat16)
        summed = lax.psum_scatter(partial, "row", scatter_dimension=0, tiled=True)
        frame_rows = tokens.shape[1]
        expanded = (
            jax.nn.silu(summed.astype(jnp.float32))
            .astype(jnp.bfloat16)
            .reshape(1, frame_rows, col_count, 2 * local_gated)
        )
        padded_expanded = jnp.pad(expanded, ((0, 0), (1, 1), (0, 0), (0, 0)))
        hidden = depthwise(padded_expanded, conv_taps, frame_rows, col_count, local_gated)
        projected = jnp.dot(
            hidden.reshape(-1, local_gated), out_weight, preferred_element_type=jnp.float32
        ).astype(jnp.bfloat16)
        frame_at = lax.axis_index("frame")
        core_at = frame_at % 2
        chip_at = frame_at // 2
        chips = frame_parts // 2
        core_pairs = [(i, i ^ 1) for i in range(frame_parts)]
        by_parity = projected.reshape(chips, 2, -1, model_width)
        partner_rows = lax.dynamic_index_in_dim(by_parity, 1 - core_at, axis=1, keepdims=False)
        own_rows = lax.dynamic_index_in_dim(by_parity, core_at, axis=1, keepdims=False)
        from_partner = lax.ppermute(partner_rows, "frame", core_pairs)
        pair_sums = (own_rows.astype(jnp.float32) + from_partner.astype(jnp.float32)).astype(
            jnp.bfloat16
        )
        pair_sums = [pair_sums[chip] for chip in range(chips)]
        arrived = []
        for mask in range(chips):
            arrived.append(
                lax.ppermute(
                    pick(pair_sums, chip_at ^ mask),
                    ("frame", "row"),
                    [
                        (f * row_parts + r, r * row_parts + (f % 2) + 2 * ((f // 2) ^ mask))
                        for f in range(frame_parts)
                        for r in range(row_parts)
                    ],
                ).astype(jnp.float32)
            )
        ffn_rows = sum(arrived).reshape(token_count, model_width)
        block_out = (stream_out.astype(jnp.float32) + ffn_rows).astype(jnp.bfloat16)
        grid_shape = (frame_count, row_count, col_count, model_width)
        return (stream_out.reshape(grid_shape), block_out.reshape(grid_shape))
    tokens = jnp.stack([piece.transpose(1, 0, 2, 3) for piece in by_frame], axis=1)
    piece_frames = tokens.shape[1] * tokens.shape[2]
    partial = jnp.dot(
        tokens.reshape(-1, lane_depth), weight_flat, preferred_element_type=jnp.float32
    ).astype(jnp.bfloat16)
    summed = lax.psum_scatter(partial, "row", scatter_dimension=0, tiled=True).reshape(
        piece_frames, row_count, col_count, 2 * local_gated
    )
    expanded = jax.nn.silu(summed.astype(jnp.float32)).astype(jnp.bfloat16)
    padded_expanded = padded_2(expanded, (("row", 1),), 1)
    hidden = depthwise(padded_expanded, conv_taps, row_count, col_count, local_gated)
    hidden_flat = hidden.reshape(-1, local_gated)
    projected = jnp.dot(hidden_flat, out_weight, preferred_element_type=jnp.float32).astype(
        jnp.bfloat16
    )
    frame_blocks = jnp.split(projected, frame_parts, axis=0)
    ffn_rows = sum(
        piece.astype(jnp.float32) for piece in swap_chunks(frame_blocks, "frame")
    ).reshape(token_count, model_width)
    block_out = (stream_out.astype(jnp.float32) + ffn_rows).astype(jnp.bfloat16)
    grid_shape = (frame_count, row_count, col_count, model_width)
    return (stream_out.reshape(grid_shape), block_out.reshape(grid_shape))


def solution(mesh):
    in_specs = (
        P(("groups", "frame"), "row", None, None),
        P(("groups", "frame"), "row", None, None),
        P(("groups", "frame"), "row", None, None),
        P(("groups", "frame"), "row", None, None),
        P(),
        P(),
        P("row", None, "frame"),
        P(None, None, "frame"),
        P("frame", None),
    )
    out_specs = (
        P(("groups", "frame"), "row", None, None),
        P(("groups", "frame"), "row", None, None),
    )
    return jax.shard_map(local, mesh=mesh, in_specs=in_specs, out_specs=out_specs, check_vma=False)
```

```python
import jax
import jax.numpy as jnp
from jax import lax
from jax.sharding import PartitionSpec as P

HEADS = 20
HEAD_DIM = 112


NORM_EPS = 1e-06
SHARE_EPS = 1e-06


def padded_2(cells, sides, width):
    for axis, dim in sides:
        count = lax.axis_size(axis)
        ends = count - 1
        head = lax.slice_in_dim(cells, 0, width, axis=dim)
        tail = lax.slice_in_dim(cells, cells.shape[dim] - width, cells.shape[dim], axis=dim)
        cells = jnp.concatenate(
            [
                lax.ppermute(tail, axis, [(i, (i + 1) % count) for i in range(ends)]),
                cells,
                lax.ppermute(head, axis, [((i + 1) % count, i) for i in range(ends)]),
            ],
            axis=dim,
        )
    return cells


def exchange_steps(axes):
    steps = []
    for axis in axes:
        count = lax.axis_size(axis)
        bit = 1
        while bit < count:
            steps.append((axis, count, bit))
            bit *= 2
    return steps


def halving_sum(block, axes, inner_axis):
    steps = exchange_steps(axes)
    for axis, count, bit in steps:
        upper = (lax.axis_index(axis) & bit) != 0
        half = block.shape[1] // 2
        low, high = block[:, :half], block[:, half:]
        sent = jnp.where(upper, low, high)
        kept = jnp.where(upper, high, low)
        sent = sent.astype(jnp.bfloat16)
        block = kept + lax.ppermute(sent, axis, [(i, i ^ bit) for i in range(count)]).astype(
            jnp.float32
        )
    inner_count = lax.axis_size(inner_axis)
    pieces = [piece.astype(jnp.bfloat16) for piece in jnp.split(block, inner_count, axis=1)]
    mine = sum(piece.astype(jnp.float32) for piece in swap_chunks(pieces, inner_axis))
    shared = swap_chunks([mine.astype(jnp.bfloat16)] * inner_count, inner_axis)
    block = jnp.concatenate([piece.astype(jnp.float32) for piece in shared], axis=1)
    for axis, count, bit in reversed(steps):
        upper = (lax.axis_index(axis) & bit) != 0
        other = lax.ppermute(
            block.astype(jnp.bfloat16), axis, [(i, i ^ bit) for i in range(count)]
        ).astype(jnp.float32)
        block = jnp.where(
            upper, jnp.concatenate([other, block], 1), jnp.concatenate([block, other], 1)
        )
    return block


def pick(blocks, index):
    stacked = jnp.stack(blocks)
    return lax.dynamic_index_in_dim(stacked, index, axis=0, keepdims=False)


def swap_chunks(chunks, axis):
    count = lax.axis_size(axis)
    own = lax.axis_index(axis)
    by_mask = [pick(chunks, own)]
    for mask in range(1, count):
        sent = pick(chunks, own ^ mask)
        by_mask.append(lax.ppermute(sent, axis, [(i, i ^ mask) for i in range(count)]))
    return [pick(by_mask, own ^ source) for source in range(count)]


def doubling_gather(block, axis):
    count = lax.axis_size(axis)
    own = lax.axis_index(axis)
    by_mask = {0: block}
    bit = count // 2
    while bit >= 1:
        keys = sorted(by_mask)
        received = lax.ppermute(
            jnp.stack([by_mask[key] for key in keys]), axis, [(i, i ^ bit) for i in range(count)]
        )
        for at, key in enumerate(keys):
            by_mask[key ^ bit] = received[at]
        bit //= 2
    ordered = [by_mask[mask] for mask in range(count)]
    return [pick(ordered, own ^ source) for source in range(count)]


def rms_norm(features):
    return features * lax.rsqrt(jnp.mean(features * features, axis=-1, keepdims=True) + NORM_EPS)


def depthwise(padded, conv_taps, row_count, col_count, half_width):
    widened = jnp.pad(padded, ((0, 0), (0, 0), (1, 1), (0, 0)))
    summed = jnp.zeros((padded.shape[0], row_count, col_count, padded.shape[3]), jnp.float32)
    for row_off in range(3):
        for col_off in range(3):
            window = widened[
                :, row_off : row_off + row_count, col_off : col_off + col_count, :
            ].astype(jnp.float32)
            summed = summed + window * conv_taps[row_off * 3 + col_off]
    return (summed[..., :half_width] * jax.nn.silu(summed[..., half_width:])).astype(jnp.bfloat16)


def local(
    query_in, key_in, value_in, stream_in, attn_gain, ffn_gain, in_weight, conv_weight, out_weight
):
    frame_count, row_count, col_count, model_width = query_in.shape
    token_count = frame_count * row_count * col_count
    local_gated = in_weight.shape[2]
    highest = lax.Precision.HIGHEST
    key_pos = jnp.maximum(key_in, 0).reshape(token_count, HEADS, HEAD_DIM)
    value_heads = value_in.reshape(token_count, HEADS, HEAD_DIM)
    local_state = jnp.einsum(
        "thi,thj->ihj", key_pos, value_heads, preferred_element_type=jnp.float32
    ).reshape(HEAD_DIM, model_width)
    local_total = jnp.sum(key_pos.reshape(token_count, model_width), axis=0, dtype=jnp.float32)
    stats = jnp.concatenate([local_state, local_total[None, :]], axis=0)
    parts = 1
    for axis, count, bit in exchange_steps(("frame", "row")):
        parts *= 2
    padded_width = -(-model_width // parts) * parts
    stat_rows = -(-stats.shape[0] // 16) * 16
    stats = jnp.pad(stats, ((0, stat_rows - stats.shape[0]), (0, padded_width - model_width)))
    stats = halving_sum(stats, ("frame",), inner_axis="row")[:, :model_width]
    kv_state, key_total = stats[:HEAD_DIM], stats[HEAD_DIM]
    query_pos = jnp.maximum(query_in, 0).reshape(token_count, HEADS, HEAD_DIM).astype(jnp.float32)
    query_narrow = query_pos.astype(jnp.bfloat16)
    numerator = jnp.einsum(
        "thi,ihj->thj",
        query_narrow,
        kv_state.astype(jnp.bfloat16).reshape(HEAD_DIM, HEADS, HEAD_DIM),
        preferred_element_type=jnp.float32,
    )
    denominator = jnp.einsum(
        "thi,hi->th",
        query_narrow,
        key_total.astype(jnp.bfloat16).reshape(HEADS, HEAD_DIM),
        preferred_element_type=jnp.float32,
    )
    attended = (numerator / (denominator[:, :, None] + SHARE_EPS)).reshape(token_count, model_width)
    stream_flat = stream_in.reshape(token_count, model_width).astype(jnp.float32)
    stream_out = (stream_flat + attn_gain.astype(jnp.float32) * rms_norm(attended)).astype(
        jnp.bfloat16
    )
    normed = (rms_norm(stream_out.astype(jnp.float32)) * ffn_gain.astype(jnp.float32)).astype(
        jnp.bfloat16
    )
    normed_grid = normed.reshape(frame_count, row_count, col_count, model_width)
    conv_taps = conv_weight.reshape(9, 2 * local_gated).astype(jnp.float32)
    row_parts = lax.axis_size("row")
    local_depth = in_weight.shape[0]
    depth_chunks = [
        normed_grid[..., part * local_depth : (part + 1) * local_depth] for part in range(row_parts)
    ]
    by_row = jnp.concatenate(swap_chunks(depth_chunks, "row"), axis=1)
    frame_parts = lax.axis_size("frame")
    by_frame = doubling_gather(by_row, "frame")
    whole_frames = (
        frame_parts == row_parts and frame_parts % 2 == 0 and frame_count == 1 and row_count == 1
    )
    weight_flat = in_weight.reshape(local_depth, 2 * local_gated)
    if whole_frames:
        tokens = jnp.stack([piece[0] for piece in by_frame])
        partial = jnp.dot(
            tokens.reshape(-1, local_depth), weight_flat, preferred_element_type=jnp.float32
        ).astype(jnp.bfloat16)
        summed = lax.psum_scatter(partial, "row", scatter_dimension=0, tiled=True)
        frame_rows = tokens.shape[1]
        expanded = (
            jax.nn.silu(summed.astype(jnp.float32))
            .astype(jnp.bfloat16)
            .reshape(1, frame_rows, col_count, 2 * local_gated)
        )
        padded_expanded = jnp.pad(expanded, ((0, 0), (1, 1), (0, 0), (0, 0)))
        hidden = depthwise(padded_expanded, conv_taps, frame_rows, col_count, local_gated)
        projected = jnp.dot(
            hidden.reshape(-1, local_gated), out_weight, preferred_element_type=jnp.float32
        ).astype(jnp.bfloat16)
        frame_at = lax.axis_index("frame")
        core_at = frame_at % 2
        chip_at = frame_at // 2
        chips = frame_parts // 2
        core_pairs = [(i, i ^ 1) for i in range(frame_parts)]
        by_parity = projected.reshape(chips, 2, -1, model_width)
        partner_rows = lax.dynamic_index_in_dim(by_parity, 1 - core_at, axis=1, keepdims=False)
        own_rows = lax.dynamic_index_in_dim(by_parity, core_at, axis=1, keepdims=False)
        from_partner = lax.ppermute(partner_rows, "frame", core_pairs)
        pair_sums = (own_rows.astype(jnp.float32) + from_partner.astype(jnp.float32)).astype(
            jnp.bfloat16
        )
        pair_sums = [pair_sums[chip] for chip in range(chips)]
        arrived = []
        for mask in range(chips):
            arrived.append(
                lax.ppermute(
                    pick(pair_sums, chip_at ^ mask),
                    ("frame", "row"),
                    [
                        (f * row_parts + r, r * row_parts + (f % 2) + 2 * ((f // 2) ^ mask))
                        for f in range(frame_parts)
                        for r in range(row_parts)
                    ],
                ).astype(jnp.float32)
            )
        ffn_rows = sum(arrived).reshape(token_count, model_width)
        block_out = (stream_out.astype(jnp.float32) + ffn_rows).astype(jnp.bfloat16)
        grid_shape = (frame_count, row_count, col_count, model_width)
        return (stream_out.reshape(grid_shape), block_out.reshape(grid_shape))
    tokens = jnp.stack([piece.transpose(1, 0, 2, 3) for piece in by_frame], axis=1)
    piece_frames = tokens.shape[1] * tokens.shape[2]
    partial = jnp.dot(
        tokens.reshape(-1, local_depth), weight_flat, preferred_element_type=jnp.float32
    ).astype(jnp.bfloat16)
    summed = lax.psum_scatter(partial, "row", scatter_dimension=0, tiled=True).reshape(
        piece_frames, row_count, col_count, 2 * local_gated
    )
    expanded = jax.nn.silu(summed.astype(jnp.float32)).astype(jnp.bfloat16)
    padded_expanded = padded_2(expanded, (("row", 1),), 1)
    hidden = depthwise(padded_expanded, conv_taps, row_count, col_count, local_gated)
    hidden_flat = hidden.reshape(-1, local_gated)
    projected = jnp.dot(hidden_flat, out_weight, preferred_element_type=jnp.float32).astype(
        jnp.bfloat16
    )
    frame_blocks = jnp.split(projected, frame_parts, axis=0)
    ffn_rows = sum(
        piece.astype(jnp.float32) for piece in swap_chunks(frame_blocks, "frame")
    ).reshape(token_count, model_width)
    block_out = (stream_out.astype(jnp.float32) + ffn_rows).astype(jnp.bfloat16)
    grid_shape = (frame_count, row_count, col_count, model_width)
    return (stream_out.reshape(grid_shape), block_out.reshape(grid_shape))


def solution(mesh):
    in_specs = (
        P(("groups", "frame"), "row", None, None),
        P(("groups", "frame"), "row", None, None),
        P(("groups", "frame"), "row", None, None),
        P(("groups", "frame"), "row", None, None),
        P(),
        P(),
        P("row", None, "frame"),
        P(None, None, "frame"),
        P("frame", None),
    )
    out_specs = (
        P(("groups", "frame"), "row", None, None),
        P(("groups", "frame"), "row", None, None),
    )
    return jax.shard_map(local, mesh=mesh, in_specs=in_specs, out_specs=out_specs, check_vma=False)
```

```python
import jax
import jax.numpy as jnp
from jax import lax
from jax.sharding import PartitionSpec as P

HEADS = 20
HEAD_DIM = 112


NORM_EPS = 1e-06
SHARE_EPS = 1e-06


def padded_2(cells, sides, width):
    for axis, dim in sides:
        count = lax.axis_size(axis)
        ends = count - 1
        head = lax.slice_in_dim(cells, 0, width, axis=dim)
        tail = lax.slice_in_dim(cells, cells.shape[dim] - width, cells.shape[dim], axis=dim)
        cells = jnp.concatenate(
            [
                lax.ppermute(tail, axis, [(i, (i + 1) % count) for i in range(ends)]),
                cells,
                lax.ppermute(head, axis, [((i + 1) % count, i) for i in range(ends)]),
            ],
            axis=dim,
        )
    return cells


def exchange_steps(axes):
    steps = []
    for axis in axes:
        count = lax.axis_size(axis)
        bit = 1
        while bit < count:
            steps.append((axis, count, bit))
            bit *= 2
    return steps


def halving_sum(block, axes, inner_axis):
    steps = exchange_steps(axes)
    for axis, count, bit in steps:
        upper = (lax.axis_index(axis) & bit) != 0
        half = block.shape[1] // 2
        low, high = block[:, :half], block[:, half:]
        sent = jnp.where(upper, low, high)
        kept = jnp.where(upper, high, low)
        sent = sent.astype(jnp.bfloat16)
        block = kept + lax.ppermute(sent, axis, [(i, i ^ bit) for i in range(count)]).astype(
            jnp.float32
        )
    inner_count = lax.axis_size(inner_axis)
    pieces = [piece.astype(jnp.bfloat16) for piece in jnp.split(block, inner_count, axis=1)]
    mine = sum(piece.astype(jnp.float32) for piece in swap_chunks(pieces, inner_axis))
    shared = swap_chunks([mine.astype(jnp.bfloat16)] * inner_count, inner_axis)
    block = jnp.concatenate([piece.astype(jnp.float32) for piece in shared], axis=1)
    for axis, count, bit in reversed(steps):
        upper = (lax.axis_index(axis) & bit) != 0
        other = lax.ppermute(
            block.astype(jnp.bfloat16), axis, [(i, i ^ bit) for i in range(count)]
        ).astype(jnp.float32)
        block = jnp.where(
            upper, jnp.concatenate([other, block], 1), jnp.concatenate([block, other], 1)
        )
    return block


def pick(blocks, index):
    stacked = jnp.stack(blocks)
    return lax.dynamic_index_in_dim(stacked, index, axis=0, keepdims=False)


def swap_chunks(chunks, axis):
    count = lax.axis_size(axis)
    own = lax.axis_index(axis)
    by_mask = [pick(chunks, own)]
    for mask in range(1, count):
        sent = pick(chunks, own ^ mask)
        by_mask.append(lax.ppermute(sent, axis, [(i, i ^ mask) for i in range(count)]))
    return [pick(by_mask, own ^ source) for source in range(count)]


def doubling_gather(block, axis):
    count = lax.axis_size(axis)
    own = lax.axis_index(axis)
    by_mask = {0: block}
    bit = count // 2
    while bit >= 1:
        keys = sorted(by_mask)
        received = lax.ppermute(
            jnp.stack([by_mask[key] for key in keys]), axis, [(i, i ^ bit) for i in range(count)]
        )
        for at, key in enumerate(keys):
            by_mask[key ^ bit] = received[at]
        bit //= 2
    ordered = [by_mask[mask] for mask in range(count)]
    return [pick(ordered, own ^ source) for source in range(count)]


def rms_norm(features):
    return features * lax.rsqrt(jnp.mean(features * features, axis=-1, keepdims=True) + NORM_EPS)


def depthwise(padded, conv_taps, row_count, col_count, half_width):
    widened = jnp.pad(padded, ((0, 0), (0, 0), (1, 1), (0, 0)))
    summed = jnp.zeros((padded.shape[0], row_count, col_count, padded.shape[3]), jnp.float32)
    for row_off in range(3):
        for col_off in range(3):
            window = widened[
                :, row_off : row_off + row_count, col_off : col_off + col_count, :
            ].astype(jnp.float32)
            summed = summed + window * conv_taps[row_off * 3 + col_off]
    return (summed[..., :half_width] * jax.nn.silu(summed[..., half_width:])).astype(jnp.bfloat16)


def local(
    query_in, key_in, value_in, stream_in, attn_gain, ffn_gain, in_weight, conv_weight, out_weight
):
    frame_count, row_count, col_count, model_width = query_in.shape
    token_count = frame_count * row_count * col_count
    local_gated = in_weight.shape[2]
    highest = lax.Precision.HIGHEST
    key_pos = jnp.maximum(key_in, 0).reshape(token_count, HEADS, HEAD_DIM)
    value_heads = value_in.reshape(token_count, HEADS, HEAD_DIM)
    local_state = jnp.einsum(
        "thi,thj->ihj", key_pos, value_heads, preferred_element_type=jnp.float32
    ).reshape(HEAD_DIM, model_width)
    local_total = jnp.dot(
        jnp.ones((1, token_count), key_pos.dtype),
        key_pos.reshape(token_count, model_width),
        preferred_element_type=jnp.float32,
    )
    stats = jnp.concatenate([local_state, local_total], axis=0)
    parts = 1
    for axis, count, bit in exchange_steps(("frame", "row")):
        parts *= 2
    padded_width = -(-model_width // parts) * parts
    stat_rows = -(-stats.shape[0] // 16) * 16
    stats = jnp.pad(stats, ((0, stat_rows - stats.shape[0]), (0, padded_width - model_width)))
    stats = halving_sum(stats, ("frame",), inner_axis="row")[:, :model_width]
    kv_state, key_total = stats[:HEAD_DIM], stats[HEAD_DIM]
    query_pos = jnp.maximum(query_in, 0).reshape(token_count, HEADS, HEAD_DIM).astype(jnp.float32)
    query_narrow = query_pos.astype(jnp.bfloat16)
    numerator = jnp.einsum(
        "thi,ihj->thj",
        query_narrow,
        kv_state.astype(jnp.bfloat16).reshape(HEAD_DIM, HEADS, HEAD_DIM),
        preferred_element_type=jnp.float32,
    )
    denominator = jnp.einsum(
        "thi,hi->th",
        query_narrow,
        key_total.astype(jnp.bfloat16).reshape(HEADS, HEAD_DIM),
        preferred_element_type=jnp.float32,
    )
    attended = (numerator / (denominator[:, :, None] + SHARE_EPS)).reshape(token_count, model_width)
    stream_flat = stream_in.reshape(token_count, model_width).astype(jnp.float32)
    stream_out = (stream_flat + attn_gain.astype(jnp.float32) * rms_norm(attended)).astype(
        jnp.bfloat16
    )
    normed = (rms_norm(stream_out.astype(jnp.float32)) * ffn_gain.astype(jnp.float32)).astype(
        jnp.bfloat16
    )
    normed_grid = normed.reshape(frame_count, row_count, col_count, model_width)
    conv_taps = conv_weight.reshape(9, 2 * local_gated).astype(jnp.float32)
    row_parts = lax.axis_size("row")
    local_depth = in_weight.shape[0]
    depth_chunks = [
        normed_grid[..., part * local_depth : (part + 1) * local_depth] for part in range(row_parts)
    ]
    by_row = jnp.concatenate(swap_chunks(depth_chunks, "row"), axis=1)
    frame_parts = lax.axis_size("frame")
    by_frame = doubling_gather(by_row, "frame")
    whole_frames = (
        frame_parts == row_parts and frame_parts % 2 == 0 and frame_count == 1 and row_count == 1
    )
    weight_flat = in_weight.reshape(local_depth, 2 * local_gated)
    if whole_frames:
        tokens = jnp.stack([piece[0] for piece in by_frame])
        partial = jnp.dot(
            tokens.reshape(-1, local_depth), weight_flat, preferred_element_type=jnp.float32
        ).astype(jnp.bfloat16)
        summed = lax.psum_scatter(partial, "row", scatter_dimension=0, tiled=True)
        frame_rows = tokens.shape[1]
        expanded = (
            jax.nn.silu(summed.astype(jnp.float32))
            .astype(jnp.bfloat16)
            .reshape(1, frame_rows, col_count, 2 * local_gated)
        )
        padded_expanded = jnp.pad(expanded, ((0, 0), (1, 1), (0, 0), (0, 0)))
        hidden = depthwise(padded_expanded, conv_taps, frame_rows, col_count, local_gated)
        projected = jnp.dot(
            hidden.reshape(-1, local_gated), out_weight, preferred_element_type=jnp.float32
        ).astype(jnp.bfloat16)
        frame_at = lax.axis_index("frame")
        core_at = frame_at % 2
        chip_at = frame_at // 2
        chips = frame_parts // 2
        core_pairs = [(i, i ^ 1) for i in range(frame_parts)]
        by_parity = projected.reshape(chips, 2, -1, model_width)
        partner_rows = lax.dynamic_index_in_dim(by_parity, 1 - core_at, axis=1, keepdims=False)
        own_rows = lax.dynamic_index_in_dim(by_parity, core_at, axis=1, keepdims=False)
        from_partner = lax.ppermute(partner_rows, "frame", core_pairs)
        pair_sums = (own_rows.astype(jnp.float32) + from_partner.astype(jnp.float32)).astype(
            jnp.bfloat16
        )
        pair_sums = [pair_sums[chip] for chip in range(chips)]
        arrived = []
        for mask in range(chips):
            arrived.append(
                lax.ppermute(
                    pick(pair_sums, chip_at ^ mask),
                    ("frame", "row"),
                    [
                        (f * row_parts + r, r * row_parts + (f % 2) + 2 * ((f // 2) ^ mask))
                        for f in range(frame_parts)
                        for r in range(row_parts)
                    ],
                ).astype(jnp.float32)
            )
        ffn_rows = sum(arrived).reshape(token_count, model_width)
        block_out = (stream_out.astype(jnp.float32) + ffn_rows).astype(jnp.bfloat16)
        grid_shape = (frame_count, row_count, col_count, model_width)
        return (stream_out.reshape(grid_shape), block_out.reshape(grid_shape))
    tokens = jnp.stack([piece.transpose(1, 0, 2, 3) for piece in by_frame], axis=1)
    piece_frames = tokens.shape[1] * tokens.shape[2]
    partial = jnp.dot(
        tokens.reshape(-1, local_depth), weight_flat, preferred_element_type=jnp.float32
    ).astype(jnp.bfloat16)
    summed = lax.psum_scatter(partial, "row", scatter_dimension=0, tiled=True).reshape(
        piece_frames, row_count, col_count, 2 * local_gated
    )
    expanded = jax.nn.silu(summed.astype(jnp.float32)).astype(jnp.bfloat16)
    padded_expanded = padded_2(expanded, (("row", 1),), 1)
    hidden = depthwise(padded_expanded, conv_taps, row_count, col_count, local_gated)
    hidden_flat = hidden.reshape(-1, local_gated)
    projected = jnp.dot(hidden_flat, out_weight, preferred_element_type=jnp.float32).astype(
        jnp.bfloat16
    )
    frame_blocks = jnp.split(projected, frame_parts, axis=0)
    ffn_rows = sum(
        piece.astype(jnp.float32) for piece in swap_chunks(frame_blocks, "frame")
    ).reshape(token_count, model_width)
    block_out = (stream_out.astype(jnp.float32) + ffn_rows).astype(jnp.bfloat16)
    grid_shape = (frame_count, row_count, col_count, model_width)
    return (stream_out.reshape(grid_shape), block_out.reshape(grid_shape))


def solution(mesh):
    in_specs = (
        P(("groups", "frame"), "row", None, None),
        P(("groups", "frame"), "row", None, None),
        P(("groups", "frame"), "row", None, None),
        P(("groups", "frame"), "row", None, None),
        P(),
        P(),
        P("row", None, "frame"),
        P(None, None, "frame"),
        P("frame", None),
    )
    out_specs = (
        P(("groups", "frame"), "row", None, None),
        P(("groups", "frame"), "row", None, None),
    )
    return jax.shard_map(local, mesh=mesh, in_specs=in_specs, out_specs=out_specs, check_vma=False)
```

```python
import jax
import jax.numpy as jnp
from jax import lax
from jax.sharding import PartitionSpec as P

HEADS = 20
HEAD_DIM = 112


NORM_EPS = 1e-06
SHARE_EPS = 1e-06


def padded_2(cells, sides, width):
    for axis, dim in sides:
        count = lax.axis_size(axis)
        ends = count - 1
        head = lax.slice_in_dim(cells, 0, width, axis=dim)
        tail = lax.slice_in_dim(cells, cells.shape[dim] - width, cells.shape[dim], axis=dim)
        cells = jnp.concatenate(
            [
                lax.ppermute(tail, axis, [(i, (i + 1) % count) for i in range(ends)]),
                cells,
                lax.ppermute(head, axis, [((i + 1) % count, i) for i in range(ends)]),
            ],
            axis=dim,
        )
    return cells


def exchange_steps(axes):
    steps = []
    for axis in axes:
        count = lax.axis_size(axis)
        bit = 1
        while bit < count:
            steps.append((axis, count, bit))
            bit *= 2
    return steps


def halving_sum(block, axes, inner_axis):
    steps = exchange_steps(axes)
    for axis, count, bit in steps:
        upper = (lax.axis_index(axis) & bit) != 0
        half = block.shape[1] // 2
        low, high = block[:, :half], block[:, half:]
        sent = jnp.where(upper, low, high)
        kept = jnp.where(upper, high, low)
        sent = sent.astype(jnp.bfloat16)
        block = kept + lax.ppermute(sent, axis, [(i, i ^ bit) for i in range(count)]).astype(
            jnp.float32
        )
    inner_count = lax.axis_size(inner_axis)
    pieces = [piece.astype(jnp.bfloat16) for piece in jnp.split(block, inner_count, axis=1)]
    mine = sum(piece.astype(jnp.float32) for piece in swap_chunks(pieces, inner_axis))
    shared = swap_chunks([mine.astype(jnp.bfloat16)] * inner_count, inner_axis)
    block = jnp.concatenate([piece.astype(jnp.float32) for piece in shared], axis=1)
    for axis, count, bit in reversed(steps):
        upper = (lax.axis_index(axis) & bit) != 0
        other = lax.ppermute(
            block.astype(jnp.bfloat16), axis, [(i, i ^ bit) for i in range(count)]
        ).astype(jnp.float32)
        block = jnp.where(
            upper, jnp.concatenate([other, block], 1), jnp.concatenate([block, other], 1)
        )
    return block


def pick(blocks, index):
    stacked = jnp.stack(blocks)
    return lax.dynamic_index_in_dim(stacked, index, axis=0, keepdims=False)


def swap_chunks(chunks, axis):
    count = lax.axis_size(axis)
    own = lax.axis_index(axis)
    by_mask = [pick(chunks, own)]
    for mask in range(1, count):
        sent = pick(chunks, own ^ mask)
        by_mask.append(lax.ppermute(sent, axis, [(i, i ^ mask) for i in range(count)]))
    return [pick(by_mask, own ^ source) for source in range(count)]


def doubling_gather(block, axis):
    count = lax.axis_size(axis)
    own = lax.axis_index(axis)
    by_mask = {0: block}
    bit = count // 2
    while bit >= 1:
        keys = sorted(by_mask)
        received = lax.ppermute(
            jnp.stack([by_mask[key] for key in keys]), axis, [(i, i ^ bit) for i in range(count)]
        )
        for at, key in enumerate(keys):
            by_mask[key ^ bit] = received[at]
        bit //= 2
    ordered = [by_mask[mask] for mask in range(count)]
    return [pick(ordered, own ^ source) for source in range(count)]


def rms_norm(features):
    return features * lax.rsqrt(jnp.mean(features * features, axis=-1, keepdims=True) + NORM_EPS)


def depthwise(padded, conv_taps, row_count, col_count, half_width):
    widened = jnp.pad(padded, ((0, 0), (0, 0), (1, 1), (0, 0)))
    summed = jnp.zeros((padded.shape[0], row_count, col_count, padded.shape[3]), jnp.float32)
    for row_off in range(3):
        for col_off in range(3):
            window = widened[
                :, row_off : row_off + row_count, col_off : col_off + col_count, :
            ].astype(jnp.float32)
            summed = summed + window * conv_taps[row_off * 3 + col_off]
    return (summed[..., :half_width] * jax.nn.silu(summed[..., half_width:])).astype(jnp.bfloat16)


def local(
    query_in, key_in, value_in, stream_in, attn_gain, ffn_gain, in_weight, conv_weight, out_weight
):
    frame_count, row_count, col_count, model_width = query_in.shape
    token_count = frame_count * row_count * col_count
    local_gated = in_weight.shape[2]
    highest = lax.Precision.HIGHEST
    key_pos = jnp.maximum(key_in, 0).reshape(token_count, HEADS, HEAD_DIM)
    value_heads = value_in.reshape(token_count, HEADS, HEAD_DIM)
    local_state = jnp.einsum(
        "thi,thj->ihj", key_pos, value_heads, preferred_element_type=jnp.float32
    ).reshape(HEAD_DIM, model_width)
    local_total = jnp.sum(key_pos.reshape(token_count, model_width), axis=0, dtype=jnp.float32)
    stats = jnp.concatenate([local_state, local_total[None, :]], axis=0)
    parts = 1
    for axis, count, bit in exchange_steps(("frame", "row")):
        parts *= 2
    padded_width = -(-model_width // parts) * parts
    stat_rows = -(-stats.shape[0] // 16) * 16
    stats = jnp.pad(stats, ((0, stat_rows - stats.shape[0]), (0, padded_width - model_width)))
    stats = halving_sum(stats, ("frame",), inner_axis="row")[:, :model_width]
    kv_state, key_total = stats[:HEAD_DIM], stats[HEAD_DIM]
    query_pos = jnp.maximum(query_in, 0).reshape(token_count, HEADS, HEAD_DIM).astype(jnp.float32)
    query_narrow = query_pos.astype(jnp.bfloat16)
    numerator = jnp.einsum(
        "thi,ihj->thj",
        query_narrow,
        kv_state.astype(jnp.bfloat16).reshape(HEAD_DIM, HEADS, HEAD_DIM),
        preferred_element_type=jnp.float32,
    )
    denominator = jnp.einsum(
        "thi,hi->th",
        query_narrow,
        key_total.astype(jnp.bfloat16).reshape(HEADS, HEAD_DIM),
        preferred_element_type=jnp.float32,
    )
    attended = (numerator / (denominator[:, :, None] + SHARE_EPS)).reshape(token_count, model_width)
    stream_flat = stream_in.reshape(token_count, model_width).astype(jnp.float32)
    stream_out = (stream_flat + attn_gain.astype(jnp.float32) * rms_norm(attended)).astype(
        jnp.bfloat16
    )
    normed = (rms_norm(stream_out.astype(jnp.float32)) * ffn_gain.astype(jnp.float32)).astype(
        jnp.bfloat16
    )
    normed_grid = normed.reshape(frame_count, row_count, col_count, model_width)
    conv_taps = conv_weight.reshape(9, 2 * local_gated).astype(jnp.float32)
    row_parts = lax.axis_size("row")
    local_depth = in_weight.shape[0]
    depth_chunks = [
        normed_grid[..., part * local_depth : (part + 1) * local_depth] for part in range(row_parts)
    ]
    by_row = jnp.concatenate(swap_chunks(depth_chunks, "row"), axis=1)
    frame_parts = lax.axis_size("frame")
    by_frame = doubling_gather(by_row, "frame")
    whole_frames = (
        frame_parts == row_parts and frame_parts % 2 == 0 and frame_count == 1 and row_count == 1
    )
    weight_flat = in_weight.reshape(local_depth, 2 * local_gated)
    if whole_frames:
        tokens = jnp.stack([piece[0] for piece in by_frame])
        partial = jnp.dot(
            tokens.reshape(-1, local_depth), weight_flat, preferred_element_type=jnp.float32
        ).astype(jnp.bfloat16)
        summed = lax.psum_scatter(partial, "row", scatter_dimension=0, tiled=True)
        frame_rows = tokens.shape[1]
        expanded = (
            jax.nn.silu(summed.astype(jnp.float32))
            .astype(jnp.bfloat16)
            .reshape(1, frame_rows, col_count, 2 * local_gated)
        )
        padded_expanded = jnp.pad(expanded.astype(jnp.float32), ((0, 0), (1, 1), (0, 0), (0, 0)))
        hidden = depthwise(padded_expanded, conv_taps, frame_rows, col_count, local_gated)
        projected = jnp.dot(
            hidden.reshape(-1, local_gated), out_weight, preferred_element_type=jnp.float32
        ).astype(jnp.bfloat16)
        frame_at = lax.axis_index("frame")
        core_at = frame_at % 2
        chip_at = frame_at // 2
        chips = frame_parts // 2
        core_pairs = [(i, i ^ 1) for i in range(frame_parts)]
        by_parity = projected.reshape(chips, 2, -1, model_width)
        partner_rows = lax.dynamic_index_in_dim(by_parity, 1 - core_at, axis=1, keepdims=False)
        own_rows = lax.dynamic_index_in_dim(by_parity, core_at, axis=1, keepdims=False)
        from_partner = lax.ppermute(partner_rows, "frame", core_pairs)
        pair_sums = (own_rows.astype(jnp.float32) + from_partner.astype(jnp.float32)).astype(
            jnp.bfloat16
        )
        pair_sums = [pair_sums[chip] for chip in range(chips)]
        arrived = []
        for mask in range(chips):
            arrived.append(
                lax.ppermute(
                    pick(pair_sums, chip_at ^ mask),
                    ("frame", "row"),
                    [
                        (f * row_parts + r, r * row_parts + (f % 2) + 2 * ((f // 2) ^ mask))
                        for f in range(frame_parts)
                        for r in range(row_parts)
                    ],
                ).astype(jnp.float32)
            )
        ffn_rows = sum(arrived).reshape(token_count, model_width)
        block_out = (stream_out.astype(jnp.float32) + ffn_rows).astype(jnp.bfloat16)
        grid_shape = (frame_count, row_count, col_count, model_width)
        return (stream_out.reshape(grid_shape), block_out.reshape(grid_shape))
    tokens = jnp.stack([piece.transpose(1, 0, 2, 3) for piece in by_frame], axis=1)
    piece_frames = tokens.shape[1] * tokens.shape[2]
    partial = jnp.dot(
        tokens.reshape(-1, local_depth), weight_flat, preferred_element_type=jnp.float32
    ).astype(jnp.bfloat16)
    summed = lax.psum_scatter(partial, "row", scatter_dimension=0, tiled=True).reshape(
        piece_frames, row_count, col_count, 2 * local_gated
    )
    expanded = jax.nn.silu(summed.astype(jnp.float32)).astype(jnp.bfloat16)
    padded_expanded = padded_2(expanded, (("row", 1),), 1)
    hidden = depthwise(padded_expanded, conv_taps, row_count, col_count, local_gated)
    hidden_flat = hidden.reshape(-1, local_gated)
    projected = jnp.dot(hidden_flat, out_weight, preferred_element_type=jnp.float32).astype(
        jnp.bfloat16
    )
    frame_blocks = jnp.split(projected, frame_parts, axis=0)
    ffn_rows = sum(
        piece.astype(jnp.float32) for piece in swap_chunks(frame_blocks, "frame")
    ).reshape(token_count, model_width)
    block_out = (stream_out.astype(jnp.float32) + ffn_rows).astype(jnp.bfloat16)
    grid_shape = (frame_count, row_count, col_count, model_width)
    return (stream_out.reshape(grid_shape), block_out.reshape(grid_shape))


def solution(mesh):
    in_specs = (
        P(("groups", "frame"), "row", None, None),
        P(("groups", "frame"), "row", None, None),
        P(("groups", "frame"), "row", None, None),
        P(("groups", "frame"), "row", None, None),
        P(),
        P(),
        P("row", None, "frame"),
        P(None, None, "frame"),
        P("frame", None),
    )
    out_specs = (
        P(("groups", "frame"), "row", None, None),
        P(("groups", "frame"), "row", None, None),
    )
    return jax.shard_map(local, mesh=mesh, in_specs=in_specs, out_specs=out_specs, check_vma=False)
```
